32 devices in a mesh: seq: 8 (over z, x), head: 4 (over y, core).
Axes of the slice: x: 2, y: 2, z: 4, core: 2. Of those that a mesh axis runs over, the one named last changes fastest.
Arguments:
- features: float32 [1024, 5120], P('seq', 'head'), may hold values from -20 to 20
- gate_pre: float32 [1024, 5120], P('seq', 'head'), may hold values from -6 to 6
- write_keys: float32 [1024, 128], P('seq'), may hold values from -6 to 6
- read_queries: float32 [1024, 128], P('seq'), may hold values from -0.5 to 0.5
- step_sizes: float32 [80, 1024], P('head', 'seq'), may hold values from 0.02 to 0.2
- log_decay: float32 [80, 1024], P('head', 'seq'), may hold values from -2 to 0
- skip_scale: float32 [80], P('head'), may hold values from 0.5 to 1.5
- norm_gain: float32 [5120], P('head'), may hold values from 0.1 to 1.9
- out_grad: float32 [1024, 5120], P('seq', 'head'), may hold values from -6 to 6
Outputs:
- grad_features: float32 [1024, 5120], P('seq', 'head')
- grad_gate: float32 [1024, 5120], P('seq', 'head')
- grad_write: float32 [1024, 128], P('seq')
- grad_read: float32 [1024, 128], P('seq')
- grad_steps: float32 [80, 1024], P('head', 'seq')
- grad_decay: float32 [80, 1024], P('head', 'seq')
The draws below stay inside these ranges and needn't reach their ends.
All inputs are finite; a program needn't handle non-finite values.
Results may differ from the reference program's by a relative error of at most 0.00022.
Values sent between devices are 32-bit elements; how exact they have to be, the bound alone decides.
No kernel may reach another device: no remote copies, remote signals or barrier semaphores. Data moves between devices by JAX's collectives and lax.ppermute only.
A program may use at most 128 MiB of HBM per device.

```python
import math
import jax
import jax.numpy as jnp
from jax import lax

HEADS = 80
P_SIZE = 64
N = 128
TOK_DEV = 128
BLOCK = 128
TOKENS = 1024
CHANNELS = 5120


def draw_features(key, part):
    key_values = jax.random.fold_in(key, 11)
    key_factor = jax.random.fold_in(key, 12)
    column = jnp.arange(CHANNELS).astype(jnp.float32) / max(CHANNELS - 1, 1)
    factor = jax.random.uniform(key_factor, (1, CHANNELS), jnp.float32, 0.7, 1.3)
    elements = jax.random.truncated_normal(key_values, -4.0, 4.0, (TOKENS, CHANNELS), jnp.float32)
    rising = jnp.exp(jnp.log(3.0) * column)
    return elements * rising[None, :] * factor


def draw_log_decay(key, part):
    subkeys = jax.random.split(jax.random.fold_in(key, 21), 7)
    slow_share = 4
    is_slow = jax.random.randint(subkeys[0], (HEADS, 1), 0, 8) < slow_share
    slow_rate = jnp.exp(jax.random.uniform(subkeys[1], (HEADS, 1), jnp.float32, jnp.log(0.2), jnp.log(0.8))) / TOKENS
    fast_rate = 1.0 / jax.random.uniform(subkeys[2], (HEADS, 1), jnp.float32, 30.0, 50.0)
    decay_speed = jnp.where(is_slow, slow_rate, fast_rate)
    token_share = jax.random.uniform(subkeys[3], (HEADS, TOKENS), jnp.float32, 0.5, 1.5)
    device_factor = jax.random.uniform(subkeys[4], (HEADS, TOKENS // TOK_DEV), jnp.float32, 0.6, 1.4)
    device_share = jnp.repeat(device_factor, TOK_DEV, axis=1)
    positions = jax.random.randint(subkeys[5], (3,), 0, TOKENS)
    kept_fraction = jax.random.uniform(subkeys[6], (3,), jnp.float32, 0.6, 0.8)
    match_count = (jnp.arange(TOKENS)[None, :] == positions[:, None]).astype(jnp.float32)
    spike_events = jnp.sum(match_count * jnp.log(kept_fraction)[:, None], axis=0)
    return -decay_speed * token_share * device_share + spike_events[None, :]


def level_of(rng, extent, cuts, least, top_value):
    level = 1.0
    for axis_at, shards_of in cuts:
        steps = jax.random.uniform(jax.random.fold_in(jax.random.fold_in(rng, 6), axis_at), (shards_of,), jnp.float32, least / len(cuts), top_value / len(cuts))
        level = level * jnp.repeat(jnp.exp(steps), extent[axis_at] // shards_of).reshape((-1,) + (1,) * (len(extent) - 1 - axis_at))
    return level


def noise(stream_key, shape, width, bound, cuts=(), kind=jnp.bfloat16):
    result = jax.random.normal(stream_key, shape, jnp.float32) * width
    if len(cuts) > 0:
        result = level_of(stream_key, shape, cuts, -0.22, 0.18) * result
    return jnp.clip(result, min=-bound, max=bound).astype(kind)


def setup_inputs(seed: int = 0) -> dict:
    arg_keys = jax.random.split(jax.random.key(seed), 10)
    return {
        "features": draw_features(jax.random.fold_in(arg_keys[9], 71), 0),
        "gate_pre": noise(arg_keys[1], (TOKENS, CHANNELS), 1.0, 6.0, ((0, 8), (1, 4)), jnp.float32),
        "write_keys": noise(arg_keys[2], (TOKENS, N), 1.0, 6.0, ((0, 8),), jnp.float32),
        "read_queries": noise(arg_keys[3], (TOKENS, N), N ** -0.5, 0.5, ((0, 8),), jnp.float32),
        "step_sizes": jnp.clip(jnp.exp(math.log(0.2) - 2.3025851 * jax.random.uniform(arg_keys[4], (HEADS, TOKENS), jnp.float32) ** level_of(arg_keys[4], (HEADS, TOKENS), ((0, 4), (1, 8)), -0.2, 0.2)), 0.02, 0.2),
        "log_decay": draw_log_decay(jax.random.fold_in(arg_keys[9], 71), 0),
        "skip_scale": jnp.clip(0.5 + 1.0 * jax.random.uniform(arg_keys[6], (HEADS,), jnp.float32) ** level_of(arg_keys[6], (HEADS,), ((0, 4),), -0.2, 0.2), 0.5, 1.5),
        "norm_gain": jnp.clip(1.0 + 0.18 * jax.random.normal(arg_keys[7], (CHANNELS,), jnp.float32), 0.1, 1.9),
        "out_grad": noise(arg_keys[8], (TOKENS, CHANNELS), 1.0, 6.0, ((0, 8), (1, 4)), jnp.float32),
    }


eps = 1e-05
highest = lax.Precision.HIGHEST

def block_step(carry_state, inputs, skip_scale):
    feat_block, step_block, decay_block, write_block, read_block = inputs
    length = decay_block.shape[1]
    cumul = jnp.cumsum(decay_block, axis=1)
    row_index = lax.broadcasted_iota(jnp.int32, (length, length), 0)
    col_index = lax.broadcasted_iota(jnp.int32, (length, length), 1)
    causal = row_index >= col_index
    gaps = jnp.where(causal[None], cumul[:, :, None] - cumul[:, None, :], 0.0)
    weights = jnp.where(causal[None], jnp.exp(gaps), 0.0)
    scores = jnp.dot(read_block, jnp.transpose(write_block), precision=highest)
    scaled = feat_block * jnp.transpose(step_block)[:, :, None]
    masked = weights * scores[None]
    within = jnp.einsum('hij,jhp->ihp', masked, scaled, precision=highest)
    carried = jnp.einsum('in,hpn->ihp', read_block, carry_state, precision=highest)
    carried = carried * jnp.transpose(jnp.exp(cumul))[:, :, None]
    output = within + carried + skip_scale[None, :, None] * feat_block
    to_end = jnp.exp(cumul[:, -1:] - cumul)
    weighted_in = scaled * jnp.transpose(to_end)[:, :, None]
    update = jnp.einsum('jhp,jn->hpn', weighted_in, write_block, precision=highest)
    new_state = jnp.exp(cumul[:, -1])[:, None, None] * carry_state + update
    return (new_state, output)

def run_mixer(features, step_sizes, log_decay, write_keys, read_queries, carry_state, skip_scale, block, saving):
    length = features.shape[0]
    head_count = step_sizes.shape[0]
    head_width = features.shape[1] // head_count
    block_total = length // block
    feat_blocks = features.reshape(block_total, block, head_count, head_width)
    step_blocks = jnp.transpose(step_sizes.reshape(head_count, block_total, block), (1, 0, 2))
    decay_blocks = jnp.transpose(log_decay.reshape(head_count, block_total, block), (1, 0, 2))
    write_blocks = write_keys.reshape(block_total, block, write_keys.shape[1])
    read_blocks = read_queries.reshape(block_total, block, read_queries.shape[1])

    def advance(carried_in, inputs):
        return block_step(carried_in, inputs, skip_scale)
    if saving:
        advance = jax.checkpoint(advance)
    last_state, outputs = lax.scan(advance, carry_state, (feat_blocks, step_blocks, decay_blocks, write_blocks, read_blocks))
    return (last_state, outputs.reshape(length, head_count * head_width))

def reference(features, gate_pre, write_keys, read_queries, step_sizes, log_decay, skip_scale, norm_gain, out_grad):

    def forward(feat_in, gate_in, write_in, read_in, step_in, decay_in):
        start_state = jnp.zeros((HEADS, P_SIZE, N), jnp.float32)
        unused_state, mixed = run_mixer(feat_in, step_in, decay_in, write_in, read_in, start_state, skip_scale, BLOCK, True)
        gated_out = mixed * jax.nn.silu(gate_in)
        meansq = lax.optimization_barrier(jnp.mean(gated_out * gated_out, axis=1, keepdims=True))
        return gated_out * lax.rsqrt(meansq + eps) * norm_gain[None, :]
    unused_out, pullback = jax.vjp(forward, features, gate_pre, write_keys, read_queries, step_sizes, log_decay)
    grad_features, grad_gate, grad_write, grad_read, grad_steps, grad_decay = pullback(out_grad)
    return (grad_features, grad_gate, grad_write, grad_read, grad_steps, grad_decay)
```

```python
import jax
import jax.numpy as jnp
from jax import lax
from jax.sharding import PartitionSpec as P

BLOCK = 128


eps = 1e-05
highest = lax.Precision.HIGHEST


def combine(earlier, later):
    return (earlier[0] * later[0], later[0][:, None, None] * earlier[1] + later[1])


def pair_scan(decay, state, axis, reverse):
    count = lax.axis_size(axis)
    if count == 1:
        return jnp.zeros_like(state)
    assert count % 2 == 0 and decay.shape[0] % 2 == 0
    place = lax.axis_index(axis)
    virt = count - 1 - place if reverse else place

    def phys(u):
        return count - 1 - u if reverse else u

    half = decay.shape[0] // 2
    groups = count // 2
    side = virt % 2
    group = virt // 2
    first = side == 0
    own_start = (1 - side) * half
    send_start = side * half

    def part(x, start):
        return lax.dynamic_slice_in_dim(x, start, half, 0)

    a_own, s_own = part(decay, own_start), part(state, own_start)
    a_snd, s_snd = part(decay, send_start), part(state, send_start)
    swap = [(phys(u), phys(u ^ 1)) for u in range(count)]
    a_rcv, s_rcv = lax.ppermute((a_snd, s_snd), axis, swap)
    lead = (jnp.where(first, a_own, a_rcv), jnp.where(first, s_own, s_rcv))
    trail = (jnp.where(first, a_rcv, a_own), jnp.where(first, s_rcv, s_own))
    a_tot, s_tot = combine(lead, trail)

    def shift_pairs(k):
        return [
            (phys(2 * g + x), phys(2 * (g + k) + x)) for g in range(groups - k) for x in (0, 1)
        ]

    if groups <= 4:
        a_g = jnp.ones_like(a_tot)
        s_g = jnp.zeros_like(s_tot)
        for r in range(groups - 1):
            out = combine((a_g, s_g), (a_tot, s_tot))
            pairs = [(phys(2 * r + x), phys(2 * (r + 1) + x)) for x in (0, 1)]
            if r == groups - 2:
                s_in = lax.ppermute(out[1], axis, pairs)
                a_in = a_g
            else:
                a_in, s_in = lax.ppermute(out, axis, pairs)
            dst = group == r + 1
            a_g = jnp.where(dst, a_in, a_g)
            s_g = jnp.where(dst, s_in, s_g)
    else:
        a_g, s_g = lax.ppermute((a_tot, s_tot), axis, shift_pairs(1))
        a_g = jnp.where(group == 0, 1.0, a_g)
        s_g = jnp.where(group == 0, 0.0, s_g)
        k = 1
        while k < groups:
            got = lax.ppermute((a_g, s_g), axis, shift_pairs(k))
            a_c, s_c = combine(got, (a_g, s_g))
            a_g = jnp.where(group >= k, a_c, a_g)
            s_g = jnp.where(group >= k, s_c, s_g)
            k *= 2

    with_lead_own = a_own[:, None, None] * s_g + s_own
    with_lead_rcv = a_rcv[:, None, None] * s_g + s_rcv
    send = jnp.where(first, with_lead_own, s_g)
    keep = jnp.where(first, s_g, with_lead_rcv)
    other = lax.ppermute(send, axis, swap)
    return jnp.where(
        first, jnp.concatenate([other, keep], 0), jnp.concatenate([keep, other], 0)
    )


def butterfly_psum(parts, axis):
    count = lax.axis_size(axis)
    if count & (count - 1):
        return lax.psum(parts, axis)
    k = 1
    while k < count:
        got = lax.ppermute(parts, axis, [(i, i ^ k) for i in range(count)])
        parts = jax.tree.map(jnp.add, parts, got)
        k *= 2
    return parts


def block_step(carry_state, inputs, skip_scale):
    feat_block, step_block, decay_block, write_block, read_block = inputs
    length = decay_block.shape[1]
    cumul = jnp.cumsum(decay_block, axis=1)
    row_index = lax.broadcasted_iota(jnp.int32, (length, length), 0)
    col_index = lax.broadcasted_iota(jnp.int32, (length, length), 1)
    causal = row_index >= col_index
    gaps = jnp.where(causal[None], cumul[:, :, None] - cumul[:, None, :], 0.0)
    weights = jnp.where(causal[None], jnp.exp(gaps), 0.0)
    scores = jnp.dot(read_block, jnp.transpose(write_block), precision=highest)
    scaled = feat_block * jnp.transpose(step_block)[:, :, None]
    masked = weights * scores[None]
    within = jnp.einsum("hij,jhp->ihp", masked, scaled, precision=highest)
    carried = jnp.einsum("in,hpn->ihp", read_block, carry_state, precision=highest)
    carried = carried * jnp.transpose(jnp.exp(cumul))[:, :, None]
    output = within + carried + skip_scale[None, :, None] * feat_block
    to_end = jnp.exp(cumul[:, -1:] - cumul)
    weighted_in = scaled * jnp.transpose(to_end)[:, :, None]
    update = jnp.einsum("jhp,jn->hpn", weighted_in, write_block, precision=highest)
    new_state = jnp.exp(cumul[:, -1])[:, None, None] * carry_state + update
    return (new_state, output)


def run_mixer(
    features, step_sizes, log_decay, write_keys, read_queries, carry_state, skip_scale, block
):
    length = features.shape[0]
    head_count = step_sizes.shape[0]
    head_width = features.shape[1] // head_count
    block_total = length // block
    feat_blocks = features.reshape(block_total, block, head_count, head_width)
    step_blocks = jnp.transpose(step_sizes.reshape(head_count, block_total, block), (1, 0, 2))
    decay_blocks = jnp.transpose(log_decay.reshape(head_count, block_total, block), (1, 0, 2))
    write_blocks = write_keys.reshape(block_total, block, write_keys.shape[1])
    read_blocks = read_queries.reshape(block_total, block, read_queries.shape[1])

    def advance(carried_in, inputs):
        return block_step(carried_in, inputs, skip_scale)

    last_state, outputs = lax.scan(
        advance, carry_state, (feat_blocks, step_blocks, decay_blocks, write_blocks, read_blocks)
    )
    return (last_state, outputs.reshape(length, head_count * head_width))


def local(
    features,
    gate_pre,
    write_keys,
    read_queries,
    step_sizes,
    log_decay,
    skip_scale,
    norm_gain,
    out_grad,
):
    head_count, length = step_sizes.shape
    head_width = features.shape[1] // head_count
    channels = features.shape[1] * lax.axis_size("head")
    cumul = jnp.cumsum(log_decay, axis=1)
    decay_total = jnp.exp(cumul[:, -1])
    scaled = (
        features.reshape(length, head_count, head_width) * jnp.transpose(step_sizes)[:, :, None]
    )
    to_end = jnp.exp(cumul[:, -1:] - cumul)
    weighted_in = scaled * jnp.transpose(to_end)[:, :, None]
    local_state = jnp.einsum("jhp,jn->hpn", weighted_in, write_keys, precision=highest)
    state_in = pair_scan(decay_total, local_state, "seq", False)

    def local_mixer(feat_in, step_in, decay_factors, writes, read_in):
        return run_mixer(
            feat_in, step_in, decay_factors, writes, read_in, state_in, skip_scale, BLOCK
        )

    primal, pullback = jax.vjp(
        local_mixer, features, step_sizes, log_decay, write_keys, read_queries
    )
    mixed_out = primal[1]
    sigmoid_gate = jax.nn.sigmoid(gate_pre)
    active = gate_pre * sigmoid_gate
    gated_out = mixed_out * active
    weighted = out_grad * norm_gain[None, :]
    square_sum, cross_sum = butterfly_psum(
        (jnp.sum(gated_out * gated_out, axis=1), jnp.sum(weighted * gated_out, axis=1)), "head"
    )
    inverse = lax.rsqrt(square_sum / channels + eps)
    grad_gated = (
        inverse[:, None] * weighted
        - (inverse * inverse * inverse * cross_sum / channels)[:, None] * gated_out
    )
    grad_mixed = grad_gated * active
    grad_gate = grad_gated * mixed_out * sigmoid_gate * (1.0 + gate_pre * (1.0 - sigmoid_gate))
    from_start = jnp.transpose(jnp.exp(cumul))
    weighted_grad = grad_mixed.reshape(length, head_count, head_width) * from_start[:, :, None]
    local_grad = jnp.einsum("jhp,jn->hpn", weighted_grad, read_queries, precision=highest)
    state_grad = pair_scan(decay_total, local_grad, "seq", True)
    grad_features, grad_steps, grad_decay, grad_write, grad_read = pullback(
        (state_grad, grad_mixed)
    )
    grad_write, grad_read = butterfly_psum((grad_write, grad_read), "head")
    return (grad_features, grad_gate, grad_write, grad_read, grad_steps, grad_decay)


def solution(mesh):
    placed = (
        P("seq", "head"),
        P("seq", "head"),
        P("seq", None),
        P("seq", None),
        P("head", "seq"),
        P("head", "seq"),
        P("head"),
        P("head"),
        P("seq", "head"),
    )
    return jax.shard_map(
        local,
        mesh=mesh,
        in_specs=placed,
        out_specs=(
            P("seq", "head"),
            P("seq", "head"),
            P("seq", None),
            P("seq", None),
            P("head", "seq"),
            P("head", "seq"),
        ),
        check_vma=False,
    )
```

```python
import jax
import jax.numpy as jnp
from jax import lax
from jax.sharding import PartitionSpec as P

BLOCK = 128


eps = 1e-05
highest = lax.Precision.HIGHEST


def combine(earlier, later):
    return (earlier[0] * later[0], later[0][:, None, None] * earlier[1] + later[1])


def pair_scan(decay, state, axis, reverse):
    count = lax.axis_size(axis)
    if count == 1:
        return jnp.zeros_like(state)
    assert count % 2 == 0 and decay.shape[0] % 2 == 0
    place = lax.axis_index(axis)
    virt = count - 1 - place if reverse else place

    def phys(u):
        return count - 1 - u if reverse else u

    half = decay.shape[0] // 2
    groups = count // 2
    side = virt % 2
    group = virt // 2
    first = side == 0
    own_start = (1 - side) * half
    send_start = side * half

    def part(x, start):
        return lax.dynamic_slice_in_dim(x, start, half, 0)

    a_own, s_own = part(decay, own_start), part(state, own_start)
    a_snd, s_snd = part(decay, send_start), part(state, send_start)
    swap = [(phys(u), phys(u ^ 1)) for u in range(count)]
    a_rcv, s_rcv = lax.ppermute((a_snd, s_snd), axis, swap)
    lead = (jnp.where(first, a_own, a_rcv), jnp.where(first, s_own, s_rcv))
    trail = (jnp.where(first, a_rcv, a_own), jnp.where(first, s_rcv, s_own))
    a_tot, s_tot = combine(lead, trail)

    def shift_pairs(k):
        return [
            (phys(2 * g + x), phys(2 * (g + k) + x)) for g in range(groups - k) for x in (0, 1)
        ]

    if groups <= 4:
        a_g = jnp.ones_like(a_tot)
        s_g = jnp.zeros_like(s_tot)
        for r in range(groups - 1):
            out = combine((a_g, s_g), (a_tot, s_tot))
            pairs = [(phys(2 * r + x), phys(2 * (r + 1) + x)) for x in (0, 1)]
            if r == groups - 2:
                s_in = lax.ppermute(out[1], axis, pairs)
                a_in = a_g
            else:
                a_in, s_in = lax.ppermute(out, axis, pairs)
            dst = group == r + 1
            a_g = jnp.where(dst, a_in, a_g)
            s_g = jnp.where(dst, s_in, s_g)
    else:
        a_g, s_g = lax.ppermute((a_tot, s_tot), axis, shift_pairs(1))
        a_g = jnp.where(group == 0, 1.0, a_g)
        s_g = jnp.where(group == 0, 0.0, s_g)
        k = 1
        while k < groups:
            got = lax.ppermute((a_g, s_g), axis, shift_pairs(k))
            a_c, s_c = combine(got, (a_g, s_g))
            a_g = jnp.where(group >= k, a_c, a_g)
            s_g = jnp.where(group >= k, s_c, s_g)
            k *= 2

    with_lead_own = a_own[:, None, None] * s_g + s_own
    with_lead_rcv = a_rcv[:, None, None] * s_g + s_rcv
    send = jnp.where(first, with_lead_own, s_g)
    keep = jnp.where(first, s_g, with_lead_rcv)
    other = lax.ppermute(send, axis, swap)
    return jnp.where(
        first, jnp.concatenate([other, keep], 0), jnp.concatenate([keep, other], 0)
    )


def butterfly_psum(parts, axis):
    count = lax.axis_size(axis)
    if count & (count - 1):
        return lax.psum(parts, axis)
    k = 1
    while k < count:
        got = lax.ppermute(parts, axis, [(i, i ^ k) for i in range(count)])
        parts = jax.tree.map(jnp.add, parts, got)
        k *= 2
    return parts


def block_step(carry_state, inputs, skip_scale):
    feat_block, step_block, decay_block, write_block, read_block = inputs
    length = decay_block.shape[1]
    cumul = jnp.cumsum(decay_block, axis=1)
    row_index = lax.broadcasted_iota(jnp.int32, (length, length), 0)
    col_index = lax.broadcasted_iota(jnp.int32, (length, length), 1)
    causal = row_index >= col_index
    gaps = jnp.where(causal[None], cumul[:, :, None] - cumul[:, None, :], 0.0)
    weights = jnp.where(causal[None], jnp.exp(gaps), 0.0)
    scores = jnp.dot(read_block, jnp.transpose(write_block), precision=highest)
    scaled = feat_block * jnp.transpose(step_block)[:, :, None]
    masked = weights * scores[None]
    within = jnp.einsum("hij,jhp->ihp", masked, scaled, precision=highest)
    carried = jnp.einsum("in,hpn->ihp", read_block, carry_state, precision=highest)
    carried = carried * jnp.transpose(jnp.exp(cumul))[:, :, None]
    output = within + carried + skip_scale[None, :, None] * feat_block
    to_end = jnp.exp(cumul[:, -1:] - cumul)
    weighted_in = scaled * jnp.transpose(to_end)[:, :, None]
    update = jnp.einsum("jhp,jn->hpn", weighted_in, write_block, precision=highest)
    new_state = jnp.exp(cumul[:, -1])[:, None, None] * carry_state + update
    return (new_state, output)


def run_mixer(
    features, step_sizes, log_decay, write_keys, read_queries, carry_state, skip_scale, block
):
    length = features.shape[0]
    head_count = step_sizes.shape[0]
    head_width = features.shape[1] // head_count
    block_total = length // block
    feat_blocks = features.reshape(block_total, block, head_count, head_width)
    step_blocks = jnp.transpose(step_sizes.reshape(head_count, block_total, block), (1, 0, 2))
    decay_blocks = jnp.transpose(log_decay.reshape(head_count, block_total, block), (1, 0, 2))
    write_blocks = write_keys.reshape(block_total, block, write_keys.shape[1])
    read_blocks = read_queries.reshape(block_total, block, read_queries.shape[1])

    def advance(carried_in, inputs):
        return block_step(carried_in, inputs, skip_scale)

    last_state, outputs = lax.scan(
        advance, carry_state, (feat_blocks, step_blocks, decay_blocks, write_blocks, read_blocks)
    )
    return (last_state, outputs.reshape(length, head_count * head_width))


def within_part(feat_in, step_in, decay_in, writes, read_in, skip_scale):
    head_count, length = step_in.shape
    head_width = feat_in.shape[1] // head_count
    cumul = jnp.cumsum(decay_in, axis=1)
    row_index = lax.broadcasted_iota(jnp.int32, (length, length), 0)
    col_index = lax.broadcasted_iota(jnp.int32, (length, length), 1)
    causal = row_index >= col_index
    gaps = jnp.where(causal[None], cumul[:, :, None] - cumul[:, None, :], 0.0)
    weights = jnp.where(causal[None], jnp.exp(gaps), 0.0)
    scores = jnp.dot(read_in, jnp.transpose(writes), precision=highest)
    feat3 = feat_in.reshape(length, head_count, head_width)
    scaled = feat3 * jnp.transpose(step_in)[:, :, None]
    masked = weights * scores[None]
    within = jnp.einsum("hij,jhp->ihp", masked, scaled, precision=highest)
    return (within + skip_scale[None, :, None] * feat3).reshape(length, -1)


def carried_part(decay_in, read_in, state_in):
    length = decay_in.shape[1]
    cumul = jnp.cumsum(decay_in, axis=1)
    carried = jnp.einsum("in,hpn->ihp", read_in, state_in, precision=highest)
    carried = carried * jnp.transpose(jnp.exp(cumul))[:, :, None]
    return carried.reshape(length, -1)


def state_update(feat_in, step_in, decay_in, writes):
    head_count, length = step_in.shape
    head_width = feat_in.shape[1] // head_count
    cumul = jnp.cumsum(decay_in, axis=1)
    scaled = feat_in.reshape(length, head_count, head_width) * jnp.transpose(step_in)[:, :, None]
    to_end = jnp.exp(cumul[:, -1:] - cumul)
    weighted_in = scaled * jnp.transpose(to_end)[:, :, None]
    return jnp.einsum("jhp,jn->hpn", weighted_in, writes, precision=highest)


def end_part(feat_in, step_in, decay_in, writes, state_in):
    total = jnp.exp(jnp.cumsum(decay_in, axis=1)[:, -1])
    return total[:, None, None] * state_in + state_update(feat_in, step_in, decay_in, writes)


def local(
    features,
    gate_pre,
    write_keys,
    read_queries,
    step_sizes,
    log_decay,
    skip_scale,
    norm_gain,
    out_grad,
):
    head_count, length = step_sizes.shape
    head_width = features.shape[1] // head_count
    channels = features.shape[1] * lax.axis_size("head")
    cumul = jnp.cumsum(log_decay, axis=1)
    decay_total = jnp.exp(cumul[:, -1])
    scaled = (
        features.reshape(length, head_count, head_width) * jnp.transpose(step_sizes)[:, :, None]
    )
    to_end = jnp.exp(cumul[:, -1:] - cumul)
    weighted_in = scaled * jnp.transpose(to_end)[:, :, None]
    local_state = jnp.einsum("jhp,jn->hpn", weighted_in, write_keys, precision=highest)
    state_in = pair_scan(decay_total, local_state, "seq", False)
    single = length == BLOCK
    if single:
        mixed_w, pull_w = jax.vjp(
            lambda f, s, d, w, r: within_part(f, s, d, w, r, skip_scale),
            features, step_sizes, log_decay, write_keys, read_queries,
        )
        mixed_c, pull_c = jax.vjp(
            lambda d, r: carried_part(d, r, state_in), log_decay, read_queries
        )
        mixed_out = mixed_w + mixed_c
    else:

        def local_mixer(feat_in, step_in, decay_factors, writes, read_in):
            return run_mixer(
                feat_in, step_in, decay_factors, writes, read_in, state_in, skip_scale, BLOCK
            )

        primal, pullback = jax.vjp(
            local_mixer, features, step_sizes, log_decay, write_keys, read_queries
        )
        mixed_out = primal[1]
    sigmoid_gate = jax.nn.sigmoid(gate_pre)
    active = gate_pre * sigmoid_gate
    gated_out = mixed_out * active
    weighted = out_grad * norm_gain[None, :]
    square_sum, cross_sum = butterfly_psum(
        (jnp.sum(gated_out * gated_out, axis=1), jnp.sum(weighted * gated_out, axis=1)), "head"
    )
    inverse = lax.rsqrt(square_sum / channels + eps)
    grad_gated = (
        inverse[:, None] * weighted
        - (inverse * inverse * inverse * cross_sum / channels)[:, None] * gated_out
    )
    grad_mixed = grad_gated * active
    grad_gate = grad_gated * mixed_out * sigmoid_gate * (1.0 + gate_pre * (1.0 - sigmoid_gate))
    from_start = jnp.transpose(jnp.exp(cumul))
    weighted_grad = grad_mixed.reshape(length, head_count, head_width) * from_start[:, :, None]
    local_grad = jnp.einsum("jhp,jn->hpn", weighted_grad, read_queries, precision=highest)
    state_grad = pair_scan(decay_total, local_grad, "seq", True)
    if single:
        gf_w, gs_w, gd_w, gw_w, gr_w = pull_w(grad_mixed)
        gd_c, gr_c = pull_c(grad_mixed)
        grad_read = butterfly_psum(gr_w + gr_c, "head")
        _, pull_e = jax.vjp(
            lambda f, s, d, w: end_part(f, s, d, w, state_in),
            features, step_sizes, log_decay, write_keys,
        )
        gf_e, gs_e, gd_e, gw_e = pull_e(state_grad)
        grad_features = gf_w + gf_e
        grad_steps = gs_w + gs_e
        grad_decay = gd_w + gd_c + gd_e
        grad_write = butterfly_psum(gw_w + gw_e, "head")
    else:
        grad_features, grad_steps, grad_decay, grad_write, grad_read = pullback(
            (state_grad, grad_mixed)
        )
        grad_write, grad_read = butterfly_psum((grad_write, grad_read), "head")
    return (grad_features, grad_gate, grad_write, grad_read, grad_steps, grad_decay)


def solution(mesh):
    placed = (
        P("seq", "head"),
        P("seq", "head"),
        P("seq", None),
        P("seq", None),
        P("head", "seq"),
        P("head", "seq"),
        P("head"),
        P("head"),
        P("seq", "head"),
    )
    return jax.shard_map(
        local,
        mesh=mesh,
        in_specs=placed,
        out_specs=(
            P("seq", "head"),
            P("seq", "head"),
            P("seq", None),
            P("seq", None),
            P("head", "seq"),
            P("head", "seq"),
        ),
        check_vma=False,
    )
```

```python
import jax
import jax.numpy as jnp
from jax import lax
from jax.sharding import PartitionSpec as P

BLOCK = 128


eps = 1e-05
highest = lax.Precision.HIGHEST


def combine(earlier, later):
    return (earlier[0] * later[0], later[0][:, None, None] * earlier[1] + later[1])


def pair_scan(decay, state, axis, reverse):
    count = lax.axis_size(axis)
    if count == 1:
        return jnp.zeros_like(state)
    assert count % 2 == 0 and decay.shape[0] % 2 == 0
    place = lax.axis_index(axis)
    virt = count - 1 - place if reverse else place

    def phys(u):
        return count - 1 - u if reverse else u

    half = decay.shape[0] // 2
    groups = count // 2
    side = virt % 2
    group = virt // 2
    first = side == 0
    own_start = (1 - side) * half
    send_start = side * half

    def part(x, start):
        return lax.dynamic_slice_in_dim(x, start, half, 0)

    a_own, s_own = part(decay, own_start), part(state, own_start)
    a_snd, s_snd = part(decay, send_start), part(state, send_start)
    swap = [(phys(u), phys(u ^ 1)) for u in range(count)]

    def shift_pairs(k):
        return [
            (phys(2 * g + x), phys(2 * (g + k) + x)) for g in range(groups - k) for x in (0, 1)
        ]

    if groups <= 4:
        return wavefront(
            a_own, s_own, a_snd, s_snd, first, group, groups, axis, swap, shift_pairs(1)
        )

    a_rcv, s_rcv = lax.ppermute((a_snd, s_snd), axis, swap)
    lead = (jnp.where(first, a_own, a_rcv), jnp.where(first, s_own, s_rcv))
    trail = (jnp.where(first, a_rcv, a_own), jnp.where(first, s_rcv, s_own))
    a_tot, s_tot = combine(lead, trail)
    a_g, s_g = lax.ppermute((a_tot, s_tot), axis, shift_pairs(1))
    a_g = jnp.where(group == 0, 1.0, a_g)
    s_g = jnp.where(group == 0, 0.0, s_g)
    k = 1
    while k < groups:
        got = lax.ppermute((a_g, s_g), axis, shift_pairs(k))
        a_c, s_c = combine(got, (a_g, s_g))
        a_g = jnp.where(group >= k, a_c, a_g)
        s_g = jnp.where(group >= k, s_c, s_g)
        k *= 2

    with_lead_own = a_own[:, None, None] * s_g + s_own
    with_lead_rcv = a_rcv[:, None, None] * s_g + s_rcv
    send = jnp.where(first, with_lead_own, s_g)
    keep = jnp.where(first, s_g, with_lead_rcv)
    other = lax.ppermute(send, axis, swap)
    return jnp.where(
        first, jnp.concatenate([other, keep], 0), jnp.concatenate([keep, other], 0)
    )


def wavefront(a_own, s_own, a_snd, s_snd, first, group, groups, axis, swap, chain):
    half = a_own.shape[0]
    chunks = 2 if half % 2 == 0 else 1
    width = half // chunks

    def split(x):
        return x.reshape((chunks, width) + x.shape[1:])

    a_own, s_own, a_snd, s_snd = split(a_own), split(s_own), split(a_snd), split(s_snd)
    a_rcv = jnp.zeros_like(a_own)
    s_rcv = jnp.zeros_like(s_own)
    a_tot = jnp.ones_like(a_own)
    s_tot = jnp.zeros_like(s_own)
    a_g = jnp.ones_like(a_own)
    s_g = jnp.zeros_like(s_own)
    other = jnp.zeros_like(s_own)
    keep = jnp.zeros_like(s_own)

    def pick(x, i):
        return lax.dynamic_index_in_dim(x, jnp.clip(i, 0, chunks - 1), 0, False)

    def put(x, v, i, ok):
        i = jnp.clip(i, 0, chunks - 1)
        old = lax.dynamic_index_in_dim(x, i, 0, False)
        return lax.dynamic_update_index_in_dim(x, jnp.where(ok, v, old), i, 0)

    for t in range(chunks + groups):
        late = t - 1 - group
        late_ok = (late >= 0) & (late < chunks)
        do_first = t < chunks
        do_last = t >= 1
        do_chain = 1 <= t <= chunks + groups - 2
        if do_last or do_chain:
            ag, sg = pick(a_g, late), pick(s_g, late)
            at, st = pick(a_tot, late), pick(s_tot, late)
        if do_last:
            ao, so = pick(a_own, late), pick(s_own, late)
            ar, sr = pick(a_rcv, late), pick(s_rcv, late)
            last_send = jnp.where(first, ao[:, None, None] * sg + so, sg)
            last_keep = jnp.where(first, sg, ar[:, None, None] * sg + sr)
            keep = put(keep, last_keep, late, late_ok)
        payload = {}
        if do_first:
            payload["a"] = a_snd[t]
            payload["s"] = s_snd[t]
        if do_last:
            payload["e"] = last_send
        got = lax.ppermute(payload, axis, swap)
        if do_chain:
            out = combine((ag, sg), (at, st))
            a_in, s_in = lax.ppermute(out, axis, chain)
            early = t - group
            early_ok = (group >= 1) & (early >= 0) & (early < chunks)
            a_g = put(a_g, a_in, early, early_ok)
            s_g = put(s_g, s_in, early, early_ok)
        if do_first:
            a_rcv = a_rcv.at[t].set(got["a"])
            s_rcv = s_rcv.at[t].set(got["s"])
            lead = (jnp.where(first, a_own[t], got["a"]), jnp.where(first, s_own[t], got["s"]))
            trail = (jnp.where(first, got["a"], a_own[t]), jnp.where(first, got["s"], s_own[t]))
            a_c, s_c = combine(lead, trail)
            a_tot = a_tot.at[t].set(a_c)
            s_tot = s_tot.at[t].set(s_c)
        if do_last:
            other = put(other, got["e"], late, late_ok)

    other = other.reshape((-1,) + other.shape[2:])
    keep = keep.reshape((-1,) + keep.shape[2:])
    return jnp.where(
        first, jnp.concatenate([other, keep], 0), jnp.concatenate([keep, other], 0)
    )


def butterfly_psum(parts, axis):
    count = lax.axis_size(axis)
    if count & (count - 1):
        return lax.psum(parts, axis)
    k = 1
    while k < count:
        got = lax.ppermute(parts, axis, [(i, i ^ k) for i in range(count)])
        parts = jax.tree.map(jnp.add, parts, got)
        k *= 2
    return parts


def block_step(carry_state, inputs, skip_scale):
    feat_block, step_block, decay_block, write_block, read_block = inputs
    length = decay_block.shape[1]
    cumul = jnp.cumsum(decay_block, axis=1)
    row_index = lax.broadcasted_iota(jnp.int32, (length, length), 0)
    col_index = lax.broadcasted_iota(jnp.int32, (length, length), 1)
    causal = row_index >= col_index
    gaps = jnp.where(causal[None], cumul[:, :, None] - cumul[:, None, :], 0.0)
    weights = jnp.where(causal[None], jnp.exp(gaps), 0.0)
    scores = jnp.dot(read_block, jnp.transpose(write_block), precision=highest)
    scaled = feat_block * jnp.transpose(step_block)[:, :, None]
    masked = weights * scores[None]
    within = jnp.einsum("hij,jhp->ihp", masked, scaled, precision=highest)
    carried = jnp.einsum("in,hpn->ihp", read_block, carry_state, precision=highest)
    carried = carried * jnp.transpose(jnp.exp(cumul))[:, :, None]
    output = within + carried + skip_scale[None, :, None] * feat_block
    to_end = jnp.exp(cumul[:, -1:] - cumul)
    weighted_in = scaled * jnp.transpose(to_end)[:, :, None]
    update = jnp.einsum("jhp,jn->hpn", weighted_in, write_block, precision=highest)
    new_state = jnp.exp(cumul[:, -1])[:, None, None] * carry_state + update
    return (new_state, output)


def run_mixer(
    features, step_sizes, log_decay, write_keys, read_queries, carry_state, skip_scale, block
):
    length = features.shape[0]
    head_count = step_sizes.shape[0]
    head_width = features.shape[1] // head_count
    block_total = length // block
    feat_blocks = features.reshape(block_total, block, head_count, head_width)
    step_blocks = jnp.transpose(step_sizes.reshape(head_count, block_total, block), (1, 0, 2))
    decay_blocks = jnp.transpose(log_decay.reshape(head_count, block_total, block), (1, 0, 2))
    write_blocks = write_keys.reshape(block_total, block, write_keys.shape[1])
    read_blocks = read_queries.reshape(block_total, block, read_queries.shape[1])

    def advance(carried_in, inputs):
        return block_step(carried_in, inputs, skip_scale)

    last_state, outputs = lax.scan(
        advance, carry_state, (feat_blocks, step_blocks, decay_blocks, write_blocks, read_blocks)
    )
    return (last_state, outputs.reshape(length, head_count * head_width))


def within_part(feat_in, step_in, decay_in, writes, read_in, skip_scale):
    head_count, length = step_in.shape
    head_width = feat_in.shape[1] // head_count
    cumul = jnp.cumsum(decay_in, axis=1)
    row_index = lax.broadcasted_iota(jnp.int32, (length, length), 0)
    col_index = lax.broadcasted_iota(jnp.int32, (length, length), 1)
    causal = row_index >= col_index
    gaps = jnp.where(causal[None], cumul[:, :, None] - cumul[:, None, :], 0.0)
    weights = jnp.where(causal[None], jnp.exp(gaps), 0.0)
    scores = jnp.dot(read_in, jnp.transpose(writes), precision=highest)
    feat3 = feat_in.reshape(length, head_count, head_width)
    scaled = feat3 * jnp.transpose(step_in)[:, :, None]
    masked = weights * scores[None]
    within = jnp.einsum("hij,jhp->ihp", masked, scaled, precision=highest)
    return (within + skip_scale[None, :, None] * feat3).reshape(length, -1)


def carried_part(decay_in, read_in, state_in):
    length = decay_in.shape[1]
    cumul = jnp.cumsum(decay_in, axis=1)
    carried = jnp.einsum("in,hpn->ihp", read_in, state_in, precision=highest)
    carried = carried * jnp.transpose(jnp.exp(cumul))[:, :, None]
    return carried.reshape(length, -1)


def state_update(feat_in, step_in, decay_in, writes):
    head_count, length = step_in.shape
    head_width = feat_in.shape[1] // head_count
    cumul = jnp.cumsum(decay_in, axis=1)
    scaled = feat_in.reshape(length, head_count, head_width) * jnp.transpose(step_in)[:, :, None]
    to_end = jnp.exp(cumul[:, -1:] - cumul)
    weighted_in = scaled * jnp.transpose(to_end)[:, :, None]
    return jnp.einsum("jhp,jn->hpn", weighted_in, writes, precision=highest)


def end_part(feat_in, step_in, decay_in, writes, state_in):
    total = jnp.exp(jnp.cumsum(decay_in, axis=1)[:, -1])
    return total[:, None, None] * state_in + state_update(feat_in, step_in, decay_in, writes)


def local(
    features,
    gate_pre,
    write_keys,
    read_queries,
    step_sizes,
    log_decay,
    skip_scale,
    norm_gain,
    out_grad,
):
    head_count, length = step_sizes.shape
    head_width = features.shape[1] // head_count
    channels = features.shape[1] * lax.axis_size("head")
    cumul = jnp.cumsum(log_decay, axis=1)
    decay_total = jnp.exp(cumul[:, -1])
    scaled = (
        features.reshape(length, head_count, head_width) * jnp.transpose(step_sizes)[:, :, None]
    )
    to_end = jnp.exp(cumul[:, -1:] - cumul)
    weighted_in = scaled * jnp.transpose(to_end)[:, :, None]
    local_state = jnp.einsum("jhp,jn->hpn", weighted_in, write_keys, precision=highest)
    state_in = pair_scan(decay_total, local_state, "seq", False)
    single = length == BLOCK
    if single:
        mixed_w, pull_w = jax.vjp(
            lambda f, s, d, w, r: within_part(f, s, d, w, r, skip_scale),
            features, step_sizes, log_decay, write_keys, read_queries,
        )
        mixed_c, pull_c = jax.vjp(
            lambda d, r: carried_part(d, r, state_in), log_decay, read_queries
        )
        mixed_out = mixed_w + mixed_c
    else:

        def local_mixer(feat_in, step_in, decay_factors, writes, read_in):
            return run_mixer(
                feat_in, step_in, decay_factors, writes, read_in, state_in, skip_scale, BLOCK
            )

        primal, pullback = jax.vjp(
            local_mixer, features, step_sizes, log_decay, write_keys, read_queries
        )
        mixed_out = primal[1]
    sigmoid_gate = jax.nn.sigmoid(gate_pre)
    active = gate_pre * sigmoid_gate
    gated_out = mixed_out * active
    weighted = out_grad * norm_gain[None, :]
    square_sum, cross_sum = butterfly_psum(
        (jnp.sum(gated_out * gated_out, axis=1), jnp.sum(weighted * gated_out, axis=1)), "head"
    )
    inverse = lax.rsqrt(square_sum / channels + eps)
    grad_gated = (
        inverse[:, None] * weighted
        - (inverse * inverse * inverse * cross_sum / channels)[:, None] * gated_out
    )
    grad_mixed = grad_gated * active
    grad_gate = grad_gated * mixed_out * sigmoid_gate * (1.0 + gate_pre * (1.0 - sigmoid_gate))
    from_start = jnp.transpose(jnp.exp(cumul))
    weighted_grad = grad_mixed.reshape(length, head_count, head_width) * from_start[:, :, None]
    local_grad = jnp.einsum("jhp,jn->hpn", weighted_grad, read_queries, precision=highest)
    state_grad = pair_scan(decay_total, local_grad, "seq", True)
    if single:
        gf_w, gs_w, gd_w, gw_w, gr_w = pull_w(grad_mixed)
        gd_c, gr_c = pull_c(grad_mixed)
        grad_read = butterfly_psum(gr_w + gr_c, "head")
        _, pull_e = jax.vjp(
            lambda f, s, d, w: end_part(f, s, d, w, state_in),
            features, step_sizes, log_decay, write_keys,
        )
        gf_e, gs_e, gd_e, gw_e = pull_e(state_grad)
        grad_features = gf_w + gf_e
        grad_steps = gs_w + gs_e
        grad_decay = gd_w + gd_c + gd_e
        grad_write = butterfly_psum(gw_w + gw_e, "head")
    else:
        grad_features, grad_steps, grad_decay, grad_write, grad_read = pullback(
            (state_grad, grad_mixed)
        )
        grad_write, grad_read = butterfly_psum((grad_write, grad_read), "head")
    return (grad_features, grad_gate, grad_write, grad_read, grad_steps, grad_decay)


def solution(mesh):
    placed = (
        P("seq", "head"),
        P("seq", "head"),
        P("seq", None),
        P("seq", None),
        P("head", "seq"),
        P("head", "seq"),
        P("head"),
        P("head"),
        P("seq", "head"),
    )
    return jax.shard_map(
        local,
        mesh=mesh,
        in_specs=placed,
        out_specs=(
            P("seq", "head"),
            P("seq", "head"),
            P("seq", None),
            P("seq", None),
            P("head", "seq"),
            P("head", "seq"),
        ),
        check_vma=False,
    )
```

```python
import jax
import jax.numpy as jnp
from jax import lax
from jax.sharding import PartitionSpec as P

BLOCK = 128


eps = 1e-05
highest = lax.Precision.HIGHEST


def combine(earlier, later):
    return (earlier[0] * later[0], later[0][:, None, None] * earlier[1] + later[1])


def pair_scan(decay, state, axis, reverse):
    count = lax.axis_size(axis)
    if count == 1:
        return jnp.zeros_like(state)
    assert count % 2 == 0 and decay.shape[0] % 2 == 0
    place = lax.axis_index(axis)
    virt = count - 1 - place if reverse else place

    def phys(u):
        return count - 1 - u if reverse else u

    half = decay.shape[0] // 2
    groups = count // 2
    side = virt % 2
    group = virt // 2
    first = side == 0
    own_start = (1 - side) * half
    send_start = side * half

    def part(x, start):
        return lax.dynamic_slice_in_dim(x, start, half, 0)

    a_own, s_own = part(decay, own_start), part(state, own_start)
    a_snd, s_snd = part(decay, send_start), part(state, send_start)
    swap = [(phys(u), phys(u ^ 1)) for u in range(count)]
    a_rcv, s_rcv = lax.ppermute((a_snd, s_snd), axis, swap)
    lead = (jnp.where(first, a_own, a_rcv), jnp.where(first, s_own, s_rcv))
    trail = (jnp.where(first, a_rcv, a_own), jnp.where(first, s_rcv, s_own))
    a_tot, s_tot = combine(lead, trail)

    def shift_pairs(k):
        return [
            (phys(2 * g + x), phys(2 * (g + k) + x)) for g in range(groups - k) for x in (0, 1)
        ]

    if groups <= 4:
        a_g = jnp.ones_like(a_tot)
        s_g = jnp.zeros_like(s_tot)
        for r in range(groups - 1):
            out = combine((a_g, s_g), (a_tot, s_tot))
            pairs = [(phys(2 * r + x), phys(2 * (r + 1) + x)) for x in (0, 1)]
            if r == groups - 2:
                s_in = lax.ppermute(out[1], axis, pairs)
                a_in = a_g
            else:
                a_in, s_in = lax.ppermute(out, axis, pairs)
            dst = group == r + 1
            a_g = jnp.where(dst, a_in, a_g)
            s_g = jnp.where(dst, s_in, s_g)
    else:
        a_g, s_g = lax.ppermute((a_tot, s_tot), axis, shift_pairs(1))
        a_g = jnp.where(group == 0, 1.0, a_g)
        s_g = jnp.where(group == 0, 0.0, s_g)
        k = 1
        while k < groups:
            got = lax.ppermute((a_g, s_g), axis, shift_pairs(k))
            a_c, s_c = combine(got, (a_g, s_g))
            a_g = jnp.where(group >= k, a_c, a_g)
            s_g = jnp.where(group >= k, s_c, s_g)
            k *= 2

    with_lead_own = a_own[:, None, None] * s_g + s_own
    with_lead_rcv = a_rcv[:, None, None] * s_g + s_rcv
    send = jnp.where(first, with_lead_own, s_g)
    keep = jnp.where(first, s_g, with_lead_rcv)
    other = lax.ppermute(send, axis, swap)
    return jnp.where(
        first, jnp.concatenate([other, keep], 0), jnp.concatenate([keep, other], 0)
    )


def butterfly_psum(parts, axis):
    count = lax.axis_size(axis)
    if count & (count - 1):
        return lax.psum(parts, axis)
    k = 1
    while k < count:
        got = lax.ppermute(parts, axis, [(i, i ^ k) for i in range(count)])
        parts = jax.tree.map(jnp.add, parts, got)
        k *= 2
    return parts


def block_step(carry_state, inputs, skip_scale):
    feat_block, step_block, decay_block, write_block, read_block = inputs
    length = decay_block.shape[1]
    cumul = jnp.cumsum(decay_block, axis=1)
    row_index = lax.broadcasted_iota(jnp.int32, (length, length), 0)
    col_index = lax.broadcasted_iota(jnp.int32, (length, length), 1)
    causal = row_index >= col_index
    gaps = jnp.where(causal[None], cumul[:, :, None] - cumul[:, None, :], 0.0)
    weights = jnp.where(causal[None], jnp.exp(gaps), 0.0)
    scores = jnp.dot(read_block, jnp.transpose(write_block), precision=highest)
    scaled = feat_block * jnp.transpose(step_block)[:, :, None]
    masked = weights * scores[None]
    within = jnp.einsum("hij,jhp->ihp", masked, scaled, precision=highest)
    carried = jnp.einsum("in,hpn->ihp", read_block, carry_state, precision=highest)
    carried = carried * jnp.transpose(jnp.exp(cumul))[:, :, None]
    output = within + carried + skip_scale[None, :, None] * feat_block
    to_end = jnp.exp(cumul[:, -1:] - cumul)
    weighted_in = scaled * jnp.transpose(to_end)[:, :, None]
    update = jnp.einsum("jhp,jn->hpn", weighted_in, write_block, precision=highest)
    new_state = jnp.exp(cumul[:, -1])[:, None, None] * carry_state + update
    return (new_state, output)


def run_mixer(
    features, step_sizes, log_decay, write_keys, read_queries, carry_state, skip_scale, block
):
    length = features.shape[0]
    head_count = step_sizes.shape[0]
    head_width = features.shape[1] // head_count
    block_total = length // block
    feat_blocks = features.reshape(block_total, block, head_count, head_width)
    step_blocks = jnp.transpose(step_sizes.reshape(head_count, block_total, block), (1, 0, 2))
    decay_blocks = jnp.transpose(log_decay.reshape(head_count, block_total, block), (1, 0, 2))
    write_blocks = write_keys.reshape(block_total, block, write_keys.shape[1])
    read_blocks = read_queries.reshape(block_total, block, read_queries.shape[1])

    def advance(carried_in, inputs):
        return block_step(carried_in, inputs, skip_scale)

    last_state, outputs = lax.scan(
        advance, carry_state, (feat_blocks, step_blocks, decay_blocks, write_blocks, read_blocks)
    )
    return (last_state, outputs.reshape(length, head_count * head_width))


def prefix_sum(decay_in):
    length = decay_in.shape[1]
    upper = (
        lax.broadcasted_iota(jnp.int32, (length, length), 0)
        <= lax.broadcasted_iota(jnp.int32, (length, length), 1)
    ).astype(decay_in.dtype)
    return jnp.dot(decay_in, upper, precision=highest)


def within_part(feat_in, step_in, decay_in, writes, read_in, skip_scale):
    head_count, length = step_in.shape
    head_width = feat_in.shape[1] // head_count
    cumul = prefix_sum(decay_in)
    row_index = lax.broadcasted_iota(jnp.int32, (length, length), 0)
    col_index = lax.broadcasted_iota(jnp.int32, (length, length), 1)
    causal = row_index >= col_index
    gaps = jnp.where(causal[None], cumul[:, :, None] - cumul[:, None, :], 0.0)
    weights = jnp.where(causal[None], jnp.exp(gaps), 0.0)
    scores = jnp.dot(read_in, jnp.transpose(writes), precision=highest)
    feat3 = feat_in.reshape(length, head_count, head_width)
    scaled = feat3 * jnp.transpose(step_in)[:, :, None]
    masked = weights * scores[None]
    within = jnp.einsum("hij,jhp->ihp", masked, scaled, precision=highest)
    return (within + skip_scale[None, :, None] * feat3).reshape(length, -1)


def carried_part(decay_in, read_in, state_in):
    length = decay_in.shape[1]
    cumul = prefix_sum(decay_in)
    carried = jnp.einsum("in,hpn->ihp", read_in, state_in, precision=highest)
    carried = carried * jnp.transpose(jnp.exp(cumul))[:, :, None]
    return carried.reshape(length, -1)


def state_update(feat_in, step_in, decay_in, writes):
    head_count, length = step_in.shape
    head_width = feat_in.shape[1] // head_count
    cumul = prefix_sum(decay_in)
    scaled = feat_in.reshape(length, head_count, head_width) * jnp.transpose(step_in)[:, :, None]
    to_end = jnp.exp(cumul[:, -1:] - cumul)
    weighted_in = scaled * jnp.transpose(to_end)[:, :, None]
    return jnp.einsum("jhp,jn->hpn", weighted_in, writes, precision=highest)


def end_part(feat_in, step_in, decay_in, writes, state_in):
    total = jnp.exp(prefix_sum(decay_in)[:, -1])
    return total[:, None, None] * state_in + state_update(feat_in, step_in, decay_in, writes)


def local(
    features,
    gate_pre,
    write_keys,
    read_queries,
    step_sizes,
    log_decay,
    skip_scale,
    norm_gain,
    out_grad,
):
    head_count, length = step_sizes.shape
    head_width = features.shape[1] // head_count
    channels = features.shape[1] * lax.axis_size("head")
    cumul = prefix_sum(log_decay)
    decay_total = jnp.exp(cumul[:, -1])
    scaled = (
        features.reshape(length, head_count, head_width) * jnp.transpose(step_sizes)[:, :, None]
    )
    to_end = jnp.exp(cumul[:, -1:] - cumul)
    weighted_in = scaled * jnp.transpose(to_end)[:, :, None]
    local_state = jnp.einsum("jhp,jn->hpn", weighted_in, write_keys, precision=highest)
    state_in = pair_scan(decay_total, local_state, "seq", False)
    single = length == BLOCK
    if single:
        mixed_w, pull_w = jax.vjp(
            lambda f, s, d, w, r: within_part(f, s, d, w, r, skip_scale),
            features, step_sizes, log_decay, write_keys, read_queries,
        )
        mixed_c, pull_c = jax.vjp(
            lambda d, r: carried_part(d, r, state_in), log_decay, read_queries
        )
        mixed_out = mixed_w + mixed_c
    else:

        def local_mixer(feat_in, step_in, decay_factors, writes, read_in):
            return run_mixer(
                feat_in, step_in, decay_factors, writes, read_in, state_in, skip_scale, BLOCK
            )

        primal, pullback = jax.vjp(
            local_mixer, features, step_sizes, log_decay, write_keys, read_queries
        )
        mixed_out = primal[1]
    sigmoid_gate = jax.nn.sigmoid(gate_pre)
    active = gate_pre * sigmoid_gate
    gated_out = mixed_out * active
    weighted = out_grad * norm_gain[None, :]
    square_sum, cross_sum = butterfly_psum(
        (jnp.sum(gated_out * gated_out, axis=1), jnp.sum(weighted * gated_out, axis=1)), "head"
    )
    inverse = lax.rsqrt(square_sum / channels + eps)
    grad_gated = (
        inverse[:, None] * weighted
        - (inverse * inverse * inverse * cross_sum / channels)[:, None] * gated_out
    )
    grad_mixed = grad_gated * active
    grad_gate = grad_gated * mixed_out * sigmoid_gate * (1.0 + gate_pre * (1.0 - sigmoid_gate))
    from_start = jnp.transpose(jnp.exp(cumul))
    weighted_grad = grad_mixed.reshape(length, head_count, head_width) * from_start[:, :, None]
    local_grad = jnp.einsum("jhp,jn->hpn", weighted_grad, read_queries, precision=highest)
    state_grad = pair_scan(decay_total, local_grad, "seq", True)
    if single:
        gf_w, gs_w, gd_w, gw_w, gr_w = pull_w(grad_mixed)
        gd_c, gr_c = pull_c(grad_mixed)
        grad_read = butterfly_psum(gr_w + gr_c, "head")
        _, pull_e = jax.vjp(
            lambda f, s, d, w: end_part(f, s, d, w, state_in),
            features, step_sizes, log_decay, write_keys,
        )
        gf_e, gs_e, gd_e, gw_e = pull_e(state_grad)
        grad_features = gf_w + gf_e
        grad_steps = gs_w + gs_e
        grad_decay = gd_w + gd_c + gd_e
        grad_write = butterfly_psum(gw_w + gw_e, "head")
    else:
        grad_features, grad_steps, grad_decay, grad_write, grad_read = pullback(
            (state_grad, grad_mixed)
        )
        grad_write, grad_read = butterfly_psum((grad_write, grad_read), "head")
    return (grad_features, grad_gate, grad_write, grad_read, grad_steps, grad_decay)


def solution(mesh):
    placed = (
        P("seq", "head"),
        P("seq", "head"),
        P("seq", None),
        P("seq", None),
        P("head", "seq"),
        P("head", "seq"),
        P("head"),
        P("head"),
        P("seq", "head"),
    )
    return jax.shard_map(
        local,
        mesh=mesh,
        in_specs=placed,
        out_specs=(
            P("seq", "head"),
            P("seq", "head"),
            P("seq", None),
            P("seq", None),
            P("head", "seq"),
            P("head", "seq"),
        ),
        check_vma=False,
    )
```

```python
import jax
import jax.numpy as jnp
from jax import lax
from jax.sharding import PartitionSpec as P

BLOCK = 128


eps = 1e-05
highest = lax.Precision.HIGHEST


def combine(earlier, later):
    return (earlier[0] * later[0], later[0][:, None, None] * earlier[1] + later[1])


def pair_scan(decay, state, axis, reverse, tie=None, during=None):
    count = lax.axis_size(axis)
    if count == 1:
        return jnp.zeros_like(state)
    assert count % 2 == 0 and decay.shape[0] % 2 == 0
    place = lax.axis_index(axis)
    virt = count - 1 - place if reverse else place

    def phys(u):
        return count - 1 - u if reverse else u

    half = decay.shape[0] // 2
    groups = count // 2
    side = virt % 2
    group = virt // 2
    first = side == 0
    own_start = (1 - side) * half
    send_start = side * half

    def part(x, start):
        return lax.dynamic_slice_in_dim(x, start, half, 0)

    a_own, s_own = part(decay, own_start), part(state, own_start)
    a_snd, s_snd = part(decay, send_start), part(state, send_start)
    swap = [(phys(u), phys(u ^ 1)) for u in range(count)]
    a_rcv, s_rcv = lax.ppermute((a_snd, s_snd), axis, swap)
    tie_at = groups - 3 if groups <= 4 else -1
    extra = None
    if tie is not None and tie_at < 0:
        s_rcv, tie = lax.optimization_barrier((s_rcv, tie))
        extra = during(tie)
    lead = (jnp.where(first, a_own, a_rcv), jnp.where(first, s_own, s_rcv))
    trail = (jnp.where(first, a_rcv, a_own), jnp.where(first, s_rcv, s_own))
    a_tot, s_tot = combine(lead, trail)

    def shift_pairs(k):
        return [
            (phys(2 * g + x), phys(2 * (g + k) + x)) for g in range(groups - k) for x in (0, 1)
        ]

    if groups <= 4:
        a_g = jnp.ones_like(a_tot)
        s_g = jnp.zeros_like(s_tot)
        for r in range(groups - 1):
            out = combine((a_g, s_g), (a_tot, s_tot))
            pairs = [(phys(2 * r + x), phys(2 * (r + 1) + x)) for x in (0, 1)]
            if r == groups - 2:
                s_in = lax.ppermute(out[1], axis, pairs)
                a_in = a_g
            else:
                a_in, s_in = lax.ppermute(out, axis, pairs)
            if tie is not None and r == tie_at:
                s_in, tie = lax.optimization_barrier((s_in, tie))
                extra = during(tie)
            dst = group == r + 1
            a_g = jnp.where(dst, a_in, a_g)
            s_g = jnp.where(dst, s_in, s_g)
    else:
        a_g, s_g = lax.ppermute((a_tot, s_tot), axis, shift_pairs(1))
        a_g = jnp.where(group == 0, 1.0, a_g)
        s_g = jnp.where(group == 0, 0.0, s_g)
        k = 1
        while k < groups:
            got = lax.ppermute((a_g, s_g), axis, shift_pairs(k))
            a_c, s_c = combine(got, (a_g, s_g))
            a_g = jnp.where(group >= k, a_c, a_g)
            s_g = jnp.where(group >= k, s_c, s_g)
            k *= 2

    with_lead_own = a_own[:, None, None] * s_g + s_own
    with_lead_rcv = a_rcv[:, None, None] * s_g + s_rcv
    send = jnp.where(first, with_lead_own, s_g)
    keep = jnp.where(first, s_g, with_lead_rcv)
    if tie is not None:
        if extra is None:
            extra = during(tie)
        send, extra = lax.optimization_barrier((send, extra))
    other = lax.ppermute(send, axis, swap)
    result = jnp.where(
        first, jnp.concatenate([other, keep], 0), jnp.concatenate([keep, other], 0)
    )
    return result if tie is None else (result, extra)


def butterfly_psum(parts, axis):
    count = lax.axis_size(axis)
    if count & (count - 1):
        return lax.psum(parts, axis)
    k = 1
    while k < count:
        got = lax.ppermute(parts, axis, [(i, i ^ k) for i in range(count)])
        parts = jax.tree.map(jnp.add, parts, got)
        k *= 2
    return parts


def block_step(carry_state, inputs, skip_scale):
    feat_block, step_block, decay_block, write_block, read_block = inputs
    length = decay_block.shape[1]
    cumul = jnp.cumsum(decay_block, axis=1)
    row_index = lax.broadcasted_iota(jnp.int32, (length, length), 0)
    col_index = lax.broadcasted_iota(jnp.int32, (length, length), 1)
    causal = row_index >= col_index
    gaps = jnp.where(causal[None], cumul[:, :, None] - cumul[:, None, :], 0.0)
    weights = jnp.where(causal[None], jnp.exp(gaps), 0.0)
    scores = jnp.dot(read_block, jnp.transpose(write_block), precision=highest)
    scaled = feat_block * jnp.transpose(step_block)[:, :, None]
    masked = weights * scores[None]
    within = jnp.einsum("hij,jhp->ihp", masked, scaled, precision=highest)
    carried = jnp.einsum("in,hpn->ihp", read_block, carry_state, precision=highest)
    carried = carried * jnp.transpose(jnp.exp(cumul))[:, :, None]
    output = within + carried + skip_scale[None, :, None] * feat_block
    to_end = jnp.exp(cumul[:, -1:] - cumul)
    weighted_in = scaled * jnp.transpose(to_end)[:, :, None]
    update = jnp.einsum("jhp,jn->hpn", weighted_in, write_block, precision=highest)
    new_state = jnp.exp(cumul[:, -1])[:, None, None] * carry_state + update
    return (new_state, output)


def run_mixer(
    features, step_sizes, log_decay, write_keys, read_queries, carry_state, skip_scale, block
):
    length = features.shape[0]
    head_count = step_sizes.shape[0]
    head_width = features.shape[1] // head_count
    block_total = length // block
    feat_blocks = features.reshape(block_total, block, head_count, head_width)
    step_blocks = jnp.transpose(step_sizes.reshape(head_count, block_total, block), (1, 0, 2))
    decay_blocks = jnp.transpose(log_decay.reshape(head_count, block_total, block), (1, 0, 2))
    write_blocks = write_keys.reshape(block_total, block, write_keys.shape[1])
    read_blocks = read_queries.reshape(block_total, block, read_queries.shape[1])

    def advance(carried_in, inputs):
        return block_step(carried_in, inputs, skip_scale)

    last_state, outputs = lax.scan(
        advance, carry_state, (feat_blocks, step_blocks, decay_blocks, write_blocks, read_blocks)
    )
    return (last_state, outputs.reshape(length, head_count * head_width))


def prefix_sum(decay_in):
    length = decay_in.shape[1]
    upper = (
        lax.broadcasted_iota(jnp.int32, (length, length), 0)
        <= lax.broadcasted_iota(jnp.int32, (length, length), 1)
    ).astype(decay_in.dtype)
    return jnp.dot(decay_in, upper, precision=highest)


def within_part(feat_in, step_in, decay_in, writes, read_in, skip_scale):
    head_count, length = step_in.shape
    head_width = feat_in.shape[1] // head_count
    cumul = prefix_sum(decay_in)
    row_index = lax.broadcasted_iota(jnp.int32, (length, length), 0)
    col_index = lax.broadcasted_iota(jnp.int32, (length, length), 1)
    causal = row_index >= col_index
    gaps = jnp.where(causal[None], cumul[:, :, None] - cumul[:, None, :], 0.0)
    weights = jnp.where(causal[None], jnp.exp(gaps), 0.0)
    scores = jnp.dot(read_in, jnp.transpose(writes), precision=highest)
    feat3 = feat_in.reshape(length, head_count, head_width)
    scaled = feat3 * jnp.transpose(step_in)[:, :, None]
    masked = weights * scores[None]
    within = jnp.einsum("hij,jhp->ihp", masked, scaled, precision=highest)
    return (within + skip_scale[None, :, None] * feat3).reshape(length, -1)


def carried_part(decay_in, read_in, state_in):
    length = decay_in.shape[1]
    cumul = prefix_sum(decay_in)
    carried = jnp.einsum("in,hpn->ihp", read_in, state_in, precision=highest)
    carried = carried * jnp.transpose(jnp.exp(cumul))[:, :, None]
    return carried.reshape(length, -1)


def state_update(feat_in, step_in, decay_in, writes):
    head_count, length = step_in.shape
    head_width = feat_in.shape[1] // head_count
    cumul = prefix_sum(decay_in)
    scaled = feat_in.reshape(length, head_count, head_width) * jnp.transpose(step_in)[:, :, None]
    to_end = jnp.exp(cumul[:, -1:] - cumul)
    weighted_in = scaled * jnp.transpose(to_end)[:, :, None]
    return jnp.einsum("jhp,jn->hpn", weighted_in, writes, precision=highest)


def end_part(feat_in, step_in, decay_in, writes, state_in):
    total = jnp.exp(prefix_sum(decay_in)[:, -1])
    return total[:, None, None] * state_in + state_update(feat_in, step_in, decay_in, writes)


def local(
    features,
    gate_pre,
    write_keys,
    read_queries,
    step_sizes,
    log_decay,
    skip_scale,
    norm_gain,
    out_grad,
):
    head_count, length = step_sizes.shape
    head_width = features.shape[1] // head_count
    channels = features.shape[1] * lax.axis_size("head")
    cumul = prefix_sum(log_decay)
    decay_total = jnp.exp(cumul[:, -1])
    scaled = (
        features.reshape(length, head_count, head_width) * jnp.transpose(step_sizes)[:, :, None]
    )
    to_end = jnp.exp(cumul[:, -1:] - cumul)
    weighted_in = scaled * jnp.transpose(to_end)[:, :, None]
    local_state = jnp.einsum("jhp,jn->hpn", weighted_in, write_keys, precision=highest)
    single = length == BLOCK
    if single:
        def within_vjp(args):
            return jax.vjp(lambda f, s, d, w, r: within_part(f, s, d, w, r, skip_scale), *args)

        state_in, (mixed_w, pull_w) = pair_scan(
            decay_total, local_state, "seq", False,
            tie=(features, step_sizes, log_decay, write_keys, read_queries),
            during=within_vjp,
        )
        mixed_c, pull_c = jax.vjp(
            lambda d, r: carried_part(d, r, state_in), log_decay, read_queries
        )
        mixed_out = mixed_w + mixed_c
    else:
        state_in = pair_scan(decay_total, local_state, "seq", False)

        def local_mixer(feat_in, step_in, decay_factors, writes, read_in):
            return run_mixer(
                feat_in, step_in, decay_factors, writes, read_in, state_in, skip_scale, BLOCK
            )

        primal, pullback = jax.vjp(
            local_mixer, features, step_sizes, log_decay, write_keys, read_queries
        )
        mixed_out = primal[1]
    sigmoid_gate = jax.nn.sigmoid(gate_pre)
    active = gate_pre * sigmoid_gate
    gated_out = mixed_out * active
    weighted = out_grad * norm_gain[None, :]
    square_sum, cross_sum = butterfly_psum(
        (jnp.sum(gated_out * gated_out, axis=1), jnp.sum(weighted * gated_out, axis=1)), "head"
    )
    inverse = lax.rsqrt(square_sum / channels + eps)
    grad_gated = (
        inverse[:, None] * weighted
        - (inverse * inverse * inverse * cross_sum / channels)[:, None] * gated_out
    )
    grad_mixed = grad_gated * active
    grad_gate = grad_gated * mixed_out * sigmoid_gate * (1.0 + gate_pre * (1.0 - sigmoid_gate))
    from_start = jnp.transpose(jnp.exp(cumul))
    weighted_grad = grad_mixed.reshape(length, head_count, head_width) * from_start[:, :, None]
    local_grad = jnp.einsum("jhp,jn->hpn", weighted_grad, read_queries, precision=highest)
    if single:
        state_grad, ((gf_w, gs_w, gd_w, gw_w, gr_w), (gd_c, gr_c)) = pair_scan(
            decay_total, local_grad, "seq", True, tie=grad_mixed,
            during=lambda g: (pull_w(g), pull_c(g)),
        )
        grad_read = butterfly_psum(gr_w + gr_c, "head")
        _, pull_e = jax.vjp(
            lambda f, s, d, w: end_part(f, s, d, w, state_in),
            features, step_sizes, log_decay, write_keys,
        )
        gf_e, gs_e, gd_e, gw_e = pull_e(state_grad)
        grad_features = gf_w + gf_e
        grad_steps = gs_w + gs_e
        grad_decay = gd_w + gd_c + gd_e
        grad_write = butterfly_psum(gw_w + gw_e, "head")
    else:
        state_grad = pair_scan(decay_total, local_grad, "seq", True)
        grad_features, grad_steps, grad_decay, grad_write, grad_read = pullback(
            (state_grad, grad_mixed)
        )
        grad_write, grad_read = butterfly_psum((grad_write, grad_read), "head")
    return (grad_features, grad_gate, grad_write, grad_read, grad_steps, grad_decay)


def solution(mesh):
    placed = (
        P("seq", "head"),
        P("seq", "head"),
        P("seq", None),
        P("seq", None),
        P("head", "seq"),
        P("head", "seq"),
        P("head"),
        P("head"),
        P("seq", "head"),
    )
    return jax.shard_map(
        local,
        mesh=mesh,
        in_specs=placed,
        out_specs=(
            P("seq", "head"),
            P("seq", "head"),
            P("seq", None),
            P("seq", None),
            P("head", "seq"),
            P("head", "seq"),
        ),
        check_vma=False,
    )
```

```python
import jax
import jax.numpy as jnp
from jax import lax
from jax.sharding import PartitionSpec as P

BLOCK = 128


eps = 1e-05
highest = lax.Precision.HIGHEST


def combine(earlier, later):
    return (earlier[0] * later[0], later[0][:, None, None] * earlier[1] + later[1])


def pair_scan(decay, state, axis, reverse):
    count = lax.axis_size(axis)
    if count == 1:
        return jnp.zeros_like(state)
    assert count % 2 == 0 and decay.shape[0] % 2 == 0
    place = lax.axis_index(axis)
    virt = count - 1 - place if reverse else place

    def phys(u):
        return count - 1 - u if reverse else u

    half = decay.shape[0] // 2
    groups = count // 2
    side = virt % 2
    group = virt // 2
    first = side == 0
    own_start = (1 - side) * half
    send_start = side * half

    def part(x, start):
        return lax.dynamic_slice_in_dim(x, start, half, 0)

    a_own, s_own = part(decay, own_start), part(state, own_start)
    a_snd, s_snd = part(decay, send_start), part(state, send_start)
    swap = [(phys(u), phys(u ^ 1)) for u in range(count)]
    a_rcv, s_rcv = lax.ppermute((a_snd, s_snd), axis, swap)
    lead = (jnp.where(first, a_own, a_rcv), jnp.where(first, s_own, s_rcv))
    trail = (jnp.where(first, a_rcv, a_own), jnp.where(first, s_rcv, s_own))
    a_tot, s_tot = combine(lead, trail)

    def shift_pairs(k):
        return [
            (phys(2 * g + x), phys(2 * (g + k) + x)) for g in range(groups - k) for x in (0, 1)
        ]

    if groups <= 4:
        a_g = jnp.ones_like(a_tot)
        s_g = jnp.zeros_like(s_tot)
        for r in range(groups - 1):
            out = combine((a_g, s_g), (a_tot, s_tot))
            pairs = [(phys(2 * r + x), phys(2 * (r + 1) + x)) for x in (0, 1)]
            if r == groups - 2:
                s_in = lax.ppermute(out[1], axis, pairs)
                a_in = a_g
            else:
                a_in, s_in = lax.ppermute(out, axis, pairs)
            dst = group == r + 1
            a_g = jnp.where(dst, a_in, a_g)
            s_g = jnp.where(dst, s_in, s_g)
    else:
        a_g, s_g = lax.ppermute((a_tot, s_tot), axis, shift_pairs(1))
        a_g = jnp.where(group == 0, 1.0, a_g)
        s_g = jnp.where(group == 0, 0.0, s_g)
        k = 1
        while k < groups:
            got = lax.ppermute((a_g, s_g), axis, shift_pairs(k))
            a_c, s_c = combine(got, (a_g, s_g))
            a_g = jnp.where(group >= k, a_c, a_g)
            s_g = jnp.where(group >= k, s_c, s_g)
            k *= 2

    with_lead_own = a_own[:, None, None] * s_g + s_own
    with_lead_rcv = a_rcv[:, None, None] * s_g + s_rcv
    send = jnp.where(first, with_lead_own, s_g)
    keep = jnp.where(first, s_g, with_lead_rcv)
    other = lax.ppermute(send, axis, swap)
    return jnp.where(
        first, jnp.concatenate([other, keep], 0), jnp.concatenate([keep, other], 0)
    )


def butterfly_psum(parts, axis):
    count = lax.axis_size(axis)
    if count & (count - 1):
        return lax.psum(parts, axis)
    k = 1
    while k < count:
        got = lax.ppermute(parts, axis, [(i, i ^ k) for i in range(count)])
        parts = jax.tree.map(jnp.add, parts, got)
        k *= 2
    return parts


def block_step(carry_state, inputs, skip_scale):
    feat_block, step_block, decay_block, write_block, read_block = inputs
    length = decay_block.shape[1]
    cumul = jnp.cumsum(decay_block, axis=1)
    row_index = lax.broadcasted_iota(jnp.int32, (length, length), 0)
    col_index = lax.broadcasted_iota(jnp.int32, (length, length), 1)
    causal = row_index >= col_index
    gaps = jnp.where(causal[None], cumul[:, :, None] - cumul[:, None, :], 0.0)
    weights = jnp.where(causal[None], jnp.exp(gaps), 0.0)
    scores = jnp.dot(read_block, jnp.transpose(write_block), precision=highest)
    scaled = feat_block * jnp.transpose(step_block)[:, :, None]
    masked = weights * scores[None]
    within = jnp.einsum("hij,jhp->ihp", masked, scaled, precision=highest)
    carried = jnp.einsum("in,hpn->ihp", read_block, carry_state, precision=highest)
    carried = carried * jnp.transpose(jnp.exp(cumul))[:, :, None]
    output = within + carried + skip_scale[None, :, None] * feat_block
    to_end = jnp.exp(cumul[:, -1:] - cumul)
    weighted_in = scaled * jnp.transpose(to_end)[:, :, None]
    update = jnp.einsum("jhp,jn->hpn", weighted_in, write_block, precision=highest)
    new_state = jnp.exp(cumul[:, -1])[:, None, None] * carry_state + update
    return (new_state, output)


def run_mixer(
    features, step_sizes, log_decay, write_keys, read_queries, carry_state, skip_scale, block
):
    length = features.shape[0]
    head_count = step_sizes.shape[0]
    head_width = features.shape[1] // head_count
    block_total = length // block
    feat_blocks = features.reshape(block_total, block, head_count, head_width)
    step_blocks = jnp.transpose(step_sizes.reshape(head_count, block_total, block), (1, 0, 2))
    decay_blocks = jnp.transpose(log_decay.reshape(head_count, block_total, block), (1, 0, 2))
    write_blocks = write_keys.reshape(block_total, block, write_keys.shape[1])
    read_blocks = read_queries.reshape(block_total, block, read_queries.shape[1])

    def advance(carried_in, inputs):
        return block_step(carried_in, inputs, skip_scale)

    last_state, outputs = lax.scan(
        advance, carry_state, (feat_blocks, step_blocks, decay_blocks, write_blocks, read_blocks)
    )
    return (last_state, outputs.reshape(length, head_count * head_width))


def prefix_sum(decay_in):
    length = decay_in.shape[1]
    upper = (
        lax.broadcasted_iota(jnp.int32, (length, length), 0)
        <= lax.broadcasted_iota(jnp.int32, (length, length), 1)
    ).astype(decay_in.dtype)
    return jnp.dot(decay_in, upper, precision=highest)


def within_part(feat_in, step_in, decay_in, writes, read_in, skip_scale):
    head_count, length = step_in.shape
    head_width = feat_in.shape[1] // head_count
    cumul = prefix_sum(decay_in)
    row_index = lax.broadcasted_iota(jnp.int32, (length, length), 0)
    col_index = lax.broadcasted_iota(jnp.int32, (length, length), 1)
    causal = row_index >= col_index
    gaps = jnp.where(causal[None], cumul[:, :, None] - cumul[:, None, :], 0.0)
    weights = jnp.where(causal[None], jnp.exp(gaps), 0.0)
    scores = jnp.dot(read_in, jnp.transpose(writes), precision=highest)
    feat3 = feat_in.reshape(length, head_count, head_width)
    scaled = feat3 * jnp.transpose(step_in)[:, :, None]
    masked = weights * scores[None]
    within = jnp.einsum("hij,jhp->ihp", masked, scaled, precision=highest)
    return (within + skip_scale[None, :, None] * feat3).reshape(length, -1)


def per_channel(factors, head_width):
    return jnp.repeat(jnp.transpose(factors), head_width, axis=1)


def carried_part(decay_in, read_in, state_in):
    head_width = state_in.shape[1]
    flat = state_in.reshape(-1, state_in.shape[2])
    carried = jnp.dot(read_in, jnp.transpose(flat), precision=highest)
    return carried * per_channel(jnp.exp(prefix_sum(decay_in)), head_width)


def state_update(feat_in, step_in, decay_in, writes):
    head_count, length = step_in.shape
    head_width = feat_in.shape[1] // head_count
    cumul = prefix_sum(decay_in)
    to_end = jnp.exp(cumul[:, -1:] - cumul)
    weighted_in = feat_in * per_channel(step_in * to_end, head_width)
    update = lax.dot_general(
        weighted_in, writes, (((0,), (0,)), ((), ())), precision=highest
    )
    return update.reshape(head_count, head_width, writes.shape[1])


def end_part(feat_in, step_in, decay_in, writes, state_in):
    total = jnp.exp(prefix_sum(decay_in)[:, -1])
    return total[:, None, None] * state_in + state_update(feat_in, step_in, decay_in, writes)


def local(
    features,
    gate_pre,
    write_keys,
    read_queries,
    step_sizes,
    log_decay,
    skip_scale,
    norm_gain,
    out_grad,
):
    head_count, length = step_sizes.shape
    head_width = features.shape[1] // head_count
    channels = features.shape[1] * lax.axis_size("head")
    cumul = prefix_sum(log_decay)
    decay_total = jnp.exp(cumul[:, -1])
    local_state = state_update(features, step_sizes, log_decay, write_keys)
    state_in = pair_scan(decay_total, local_state, "seq", False)
    single = length == BLOCK
    if single:
        mixed_w, pull_w = jax.vjp(
            lambda f, s, d, w, r: within_part(f, s, d, w, r, skip_scale),
            features, step_sizes, log_decay, write_keys, read_queries,
        )
        mixed_c, pull_c = jax.vjp(
            lambda d, r: carried_part(d, r, state_in), log_decay, read_queries
        )
        mixed_out = mixed_w + mixed_c
    else:

        def local_mixer(feat_in, step_in, decay_factors, writes, read_in):
            return run_mixer(
                feat_in, step_in, decay_factors, writes, read_in, state_in, skip_scale, BLOCK
            )

        primal, pullback = jax.vjp(
            local_mixer, features, step_sizes, log_decay, write_keys, read_queries
        )
        mixed_out = primal[1]
    sigmoid_gate = jax.nn.sigmoid(gate_pre)
    active = gate_pre * sigmoid_gate
    gated_out = mixed_out * active
    weighted = out_grad * norm_gain[None, :]
    square_sum, cross_sum = butterfly_psum(
        jnp.stack([jnp.sum(gated_out * gated_out, axis=1), jnp.sum(weighted * gated_out, axis=1)]),
        "head",
    )
    inverse = lax.rsqrt(square_sum / channels + eps)
    grad_gated = (
        inverse[:, None] * weighted
        - (inverse * inverse * inverse * cross_sum / channels)[:, None] * gated_out
    )
    grad_mixed = grad_gated * active
    grad_gate = grad_gated * mixed_out * sigmoid_gate * (1.0 + gate_pre * (1.0 - sigmoid_gate))
    weighted_grad = grad_mixed * per_channel(jnp.exp(cumul), head_width)
    local_grad = lax.dot_general(
        weighted_grad, read_queries, (((0,), (0,)), ((), ())), precision=highest
    ).reshape(head_count, head_width, read_queries.shape[1])
    state_grad = pair_scan(decay_total, local_grad, "seq", True)
    if single:
        gf_w, gs_w, gd_w, gw_w, gr_w = pull_w(grad_mixed)
        gd_c, gr_c = pull_c(grad_mixed)
        grad_read = butterfly_psum(gr_w + gr_c, "head")
        _, pull_e = jax.vjp(
            lambda f, s, d, w: end_part(f, s, d, w, state_in),
            features, step_sizes, log_decay, write_keys,
        )
        gf_e, gs_e, gd_e, gw_e = pull_e(state_grad)
        grad_features = gf_w + gf_e
        grad_steps = gs_w + gs_e
        grad_decay = gd_w + gd_c + gd_e
        grad_write = butterfly_psum(gw_w + gw_e, "head")
    else:
        grad_features, grad_steps, grad_decay, grad_write, grad_read = pullback(
            (state_grad, grad_mixed)
        )
        grad_write, grad_read = butterfly_psum((grad_write, grad_read), "head")
    return (grad_features, grad_gate, grad_write, grad_read, grad_steps, grad_decay)


def solution(mesh):
    placed = (
        P("seq", "head"),
        P("seq", "head"),
        P("seq", None),
        P("seq", None),
        P("head", "seq"),
        P("head", "seq"),
        P("head"),
        P("head"),
        P("seq", "head"),
    )
    return jax.shard_map(
        local,
        mesh=mesh,
        in_specs=placed,
        out_specs=(
            P("seq", "head"),
            P("seq", "head"),
            P("seq", None),
            P("seq", None),
            P("head", "seq"),
            P("head", "seq"),
        ),
        check_vma=False,
    )
```

```python
import jax
import jax.numpy as jnp
from jax import lax
from jax.sharding import PartitionSpec as P

BLOCK = 128


eps = 1e-05
highest = lax.Precision.HIGHEST


def combine(earlier, later):
    return (earlier[0] * later[0], later[0][:, None, None] * earlier[1] + later[1])


def pair_scan(decay, state, axis, reverse, tie=None, during=None):
    count = lax.axis_size(axis)
    if count == 1:
        return jnp.zeros_like(state)
    assert count % 2 == 0 and decay.shape[0] % 2 == 0
    place = lax.axis_index(axis)
    virt = count - 1 - place if reverse else place

    def phys(u):
        return count - 1 - u if reverse else u

    half = decay.shape[0] // 2
    groups = count // 2
    side = virt % 2
    group = virt // 2
    first = side == 0
    own_start = (1 - side) * half
    send_start = side * half

    def part(x, start):
        return lax.dynamic_slice_in_dim(x, start, half, 0)

    a_own, s_own = part(decay, own_start), part(state, own_start)
    a_snd, s_snd = part(decay, send_start), part(state, send_start)
    swap = [(phys(u), phys(u ^ 1)) for u in range(count)]
    a_rcv, s_rcv = lax.ppermute((a_snd, s_snd), axis, swap)
    tie_at = groups - 3 if groups <= 4 else -1
    extra = None
    if tie is not None and tie_at < 0:
        s_rcv, tie = lax.optimization_barrier((s_rcv, tie))
        extra = during(tie)
    lead = (jnp.where(first, a_own, a_rcv), jnp.where(first, s_own, s_rcv))
    trail = (jnp.where(first, a_rcv, a_own), jnp.where(first, s_rcv, s_own))
    a_tot, s_tot = combine(lead, trail)

    def shift_pairs(k):
        return [
            (phys(2 * g + x), phys(2 * (g + k) + x)) for g in range(groups - k) for x in (0, 1)
        ]

    if groups <= 4:
        a_g = jnp.ones_like(a_tot)
        s_g = jnp.zeros_like(s_tot)
        for r in range(groups - 1):
            out = combine((a_g, s_g), (a_tot, s_tot))
            pairs = [(phys(2 * r + x), phys(2 * (r + 1) + x)) for x in (0, 1)]
            if r == groups - 2:
                s_in = lax.ppermute(out[1], axis, pairs)
                a_in = a_g
            else:
                a_in, s_in = lax.ppermute(out, axis, pairs)
            if tie is not None and r == tie_at:
                s_in, tie = lax.optimization_barrier((s_in, tie))
                extra = during(tie)
            dst = group == r + 1
            a_g = jnp.where(dst, a_in, a_g)
            s_g = jnp.where(dst, s_in, s_g)
    else:
        a_g, s_g = lax.ppermute((a_tot, s_tot), axis, shift_pairs(1))
        a_g = jnp.where(group == 0, 1.0, a_g)
        s_g = jnp.where(group == 0, 0.0, s_g)
        k = 1
        while k < groups:
            got = lax.ppermute((a_g, s_g), axis, shift_pairs(k))
            a_c, s_c = combine(got, (a_g, s_g))
            a_g = jnp.where(group >= k, a_c, a_g)
            s_g = jnp.where(group >= k, s_c, s_g)
            k *= 2

    with_lead_own = a_own[:, None, None] * s_g + s_own
    with_lead_rcv = a_rcv[:, None, None] * s_g + s_rcv
    send = jnp.where(first, with_lead_own, s_g)
    keep = jnp.where(first, s_g, with_lead_rcv)
    other = lax.ppermute(send, axis, swap)
    result = jnp.where(
        first, jnp.concatenate([other, keep], 0), jnp.concatenate([keep, other], 0)
    )
    if tie is None:
        return result
    if extra is None:
        extra = during(tie)
    return lax.optimization_barrier((result, extra))


def butterfly_psum(parts, axis):
    count = lax.axis_size(axis)
    if count & (count - 1):
        return lax.psum(parts, axis)
    k = 1
    while k < count:
        got = lax.ppermute(parts, axis, [(i, i ^ k) for i in range(count)])
        parts = jax.tree.map(jnp.add, parts, got)
        k *= 2
    return parts


def block_step(carry_state, inputs, skip_scale):
    feat_block, step_block, decay_block, write_block, read_block = inputs
    length = decay_block.shape[1]
    cumul = jnp.cumsum(decay_block, axis=1)
    row_index = lax.broadcasted_iota(jnp.int32, (length, length), 0)
    col_index = lax.broadcasted_iota(jnp.int32, (length, length), 1)
    causal = row_index >= col_index
    gaps = jnp.where(causal[None], cumul[:, :, None] - cumul[:, None, :], 0.0)
    weights = jnp.where(causal[None], jnp.exp(gaps), 0.0)
    scores = jnp.dot(read_block, jnp.transpose(write_block), precision=highest)
    scaled = feat_block * jnp.transpose(step_block)[:, :, None]
    masked = weights * scores[None]
    within = jnp.einsum("hij,jhp->ihp", masked, scaled, precision=highest)
    carried = jnp.einsum("in,hpn->ihp", read_block, carry_state, precision=highest)
    carried = carried * jnp.transpose(jnp.exp(cumul))[:, :, None]
    output = within + carried + skip_scale[None, :, None] * feat_block
    to_end = jnp.exp(cumul[:, -1:] - cumul)
    weighted_in = scaled * jnp.transpose(to_end)[:, :, None]
    update = jnp.einsum("jhp,jn->hpn", weighted_in, write_block, precision=highest)
    new_state = jnp.exp(cumul[:, -1])[:, None, None] * carry_state + update
    return (new_state, output)


def run_mixer(
    features, step_sizes, log_decay, write_keys, read_queries, carry_state, skip_scale, block
):
    length = features.shape[0]
    head_count = step_sizes.shape[0]
    head_width = features.shape[1] // head_count
    block_total = length // block
    feat_blocks = features.reshape(block_total, block, head_count, head_width)
    step_blocks = jnp.transpose(step_sizes.reshape(head_count, block_total, block), (1, 0, 2))
    decay_blocks = jnp.transpose(log_decay.reshape(head_count, block_total, block), (1, 0, 2))
    write_blocks = write_keys.reshape(block_total, block, write_keys.shape[1])
    read_blocks = read_queries.reshape(block_total, block, read_queries.shape[1])

    def advance(carried_in, inputs):
        return block_step(carried_in, inputs, skip_scale)

    last_state, outputs = lax.scan(
        advance, carry_state, (feat_blocks, step_blocks, decay_blocks, write_blocks, read_blocks)
    )
    return (last_state, outputs.reshape(length, head_count * head_width))


def prefix_sum(decay_in):
    length = decay_in.shape[1]
    upper = (
        lax.broadcasted_iota(jnp.int32, (length, length), 0)
        <= lax.broadcasted_iota(jnp.int32, (length, length), 1)
    ).astype(decay_in.dtype)
    return jnp.dot(decay_in, upper, precision=highest)


def within_part(feat_in, step_in, decay_in, writes, read_in, skip_scale):
    head_count, length = step_in.shape
    head_width = feat_in.shape[1] // head_count
    cumul = prefix_sum(decay_in)
    row_index = lax.broadcasted_iota(jnp.int32, (length, length), 0)
    col_index = lax.broadcasted_iota(jnp.int32, (length, length), 1)
    causal = row_index >= col_index
    gaps = jnp.where(causal[None], cumul[:, :, None] - cumul[:, None, :], 0.0)
    weights = jnp.where(causal[None], jnp.exp(gaps), 0.0)
    scores = jnp.dot(read_in, jnp.transpose(writes), precision=highest)
    feat3 = feat_in.reshape(length, head_count, head_width)
    scaled = feat3 * jnp.transpose(step_in)[:, :, None]
    masked = weights * scores[None]
    within = jnp.einsum("hij,jhp->ihp", masked, scaled, precision=highest)
    return (within + skip_scale[None, :, None] * feat3).reshape(length, -1)


def carried_part(decay_in, read_in, state_in):
    length = decay_in.shape[1]
    cumul = prefix_sum(decay_in)
    carried = jnp.einsum("in,hpn->ihp", read_in, state_in, precision=highest)
    carried = carried * jnp.transpose(jnp.exp(cumul))[:, :, None]
    return carried.reshape(length, -1)


def state_update(feat_in, step_in, decay_in, writes):
    head_count, length = step_in.shape
    head_width = feat_in.shape[1] // head_count
    cumul = prefix_sum(decay_in)
    scaled = feat_in.reshape(length, head_count, head_width) * jnp.transpose(step_in)[:, :, None]
    to_end = jnp.exp(cumul[:, -1:] - cumul)
    weighted_in = scaled * jnp.transpose(to_end)[:, :, None]
    return jnp.einsum("jhp,jn->hpn", weighted_in, writes, precision=highest)


def end_part(feat_in, step_in, decay_in, writes, state_in):
    total = jnp.exp(prefix_sum(decay_in)[:, -1])
    return total[:, None, None] * state_in + state_update(feat_in, step_in, decay_in, writes)


def local(
    features,
    gate_pre,
    write_keys,
    read_queries,
    step_sizes,
    log_decay,
    skip_scale,
    norm_gain,
    out_grad,
):
    head_count, length = step_sizes.shape
    head_width = features.shape[1] // head_count
    channels = features.shape[1] * lax.axis_size("head")
    cumul = prefix_sum(log_decay)
    decay_total = jnp.exp(cumul[:, -1])
    scaled = (
        features.reshape(length, head_count, head_width) * jnp.transpose(step_sizes)[:, :, None]
    )
    to_end = jnp.exp(cumul[:, -1:] - cumul)
    weighted_in = scaled * jnp.transpose(to_end)[:, :, None]
    local_state = jnp.einsum("jhp,jn->hpn", weighted_in, write_keys, precision=highest)
    single = length == BLOCK
    if single:

        def within_vjp(args):
            return jax.vjp(lambda f, s, d, w, r: within_part(f, s, d, w, r, skip_scale), *args)

        state_in, (mixed_w, pull_w) = pair_scan(
            decay_total, local_state, "seq", False,
            tie=(features, step_sizes, log_decay, write_keys, read_queries),
            during=within_vjp,
        )
        mixed_c, pull_c = jax.vjp(
            lambda d, r: carried_part(d, r, state_in), log_decay, read_queries
        )
        mixed_out = mixed_w + mixed_c
    else:
        state_in = pair_scan(decay_total, local_state, "seq", False)

        def local_mixer(feat_in, step_in, decay_factors, writes, read_in):
            return run_mixer(
                feat_in, step_in, decay_factors, writes, read_in, state_in, skip_scale, BLOCK
            )

        primal, pullback = jax.vjp(
            local_mixer, features, step_sizes, log_decay, write_keys, read_queries
        )
        mixed_out = primal[1]
    sigmoid_gate = jax.nn.sigmoid(gate_pre)
    active = gate_pre * sigmoid_gate
    gated_out = mixed_out * active
    weighted = out_grad * norm_gain[None, :]
    square_sum, cross_sum = butterfly_psum(
        (jnp.sum(gated_out * gated_out, axis=1), jnp.sum(weighted * gated_out, axis=1)), "head"
    )
    inverse = lax.rsqrt(square_sum / channels + eps)
    grad_gated = (
        inverse[:, None] * weighted
        - (inverse * inverse * inverse * cross_sum / channels)[:, None] * gated_out
    )
    grad_mixed = grad_gated * active
    grad_gate = grad_gated * mixed_out * sigmoid_gate * (1.0 + gate_pre * (1.0 - sigmoid_gate))
    from_start = jnp.transpose(jnp.exp(cumul))
    weighted_grad = grad_mixed.reshape(length, head_count, head_width) * from_start[:, :, None]
    local_grad = jnp.einsum("jhp,jn->hpn", weighted_grad, read_queries, precision=highest)
    state_grad = pair_scan(decay_total, local_grad, "seq", True)
    if single:
        gf_w, gs_w, gd_w, gw_w, gr_w = pull_w(grad_mixed)
        gd_c, gr_c = pull_c(grad_mixed)
        grad_read = butterfly_psum(gr_w + gr_c, "head")
        _, pull_e = jax.vjp(
            lambda f, s, d, w: end_part(f, s, d, w, state_in),
            features, step_sizes, log_decay, write_keys,
        )
        gf_e, gs_e, gd_e, gw_e = pull_e(state_grad)
        grad_features = gf_w + gf_e
        grad_steps = gs_w + gs_e
        grad_decay = gd_w + gd_c + gd_e
        grad_write = butterfly_psum(gw_w + gw_e, "head")
    else:
        grad_features, grad_steps, grad_decay, grad_write, grad_read = pullback(
            (state_grad, grad_mixed)
        )
        grad_write, grad_read = butterfly_psum((grad_write, grad_read), "head")
    return (grad_features, grad_gate, grad_write, grad_read, grad_steps, grad_decay)


def solution(mesh):
    placed = (
        P("seq", "head"),
        P("seq", "head"),
        P("seq", None),
        P("seq", None),
        P("head", "seq"),
        P("head", "seq"),
        P("head"),
        P("head"),
        P("seq", "head"),
    )
    return jax.shard_map(
        local,
        mesh=mesh,
        in_specs=placed,
        out_specs=(
            P("seq", "head"),
            P("seq", "head"),
            P("seq", None),
            P("seq", None),
            P("head", "seq"),
            P("head", "seq"),
        ),
        check_vma=False,
    )
```

```python
import jax
import jax.numpy as jnp
from jax import lax
from jax.sharding import PartitionSpec as P

BLOCK = 128


eps = 1e-05
highest = lax.Precision.HIGHEST


def combine(earlier, later):
    return (earlier[0] * later[0], later[0][:, None, None] * earlier[1] + later[1])


def pair_scan(decay, state, axis, reverse):
    count = lax.axis_size(axis)
    if count == 1:
        return jnp.zeros_like(state)
    assert count % 2 == 0 and decay.shape[0] % 2 == 0
    place = lax.axis_index(axis)
    virt = count - 1 - place if reverse else place

    def phys(u):
        return count - 1 - u if reverse else u

    half = decay.shape[0] // 2
    groups = count // 2
    side = virt % 2
    group = virt // 2
    first = side == 0
    own_start = (1 - side) * half
    send_start = side * half

    def part(x, start):
        return lax.dynamic_slice_in_dim(x, start, half, 0)

    a_own, s_own = part(decay, own_start), part(state, own_start)
    a_snd, s_snd = part(decay, send_start), part(state, send_start)
    swap = [(phys(u), phys(u ^ 1)) for u in range(count)]
    a_rcv, s_rcv = lax.ppermute((a_snd, s_snd), axis, swap)
    lead = (jnp.where(first, a_own, a_rcv), jnp.where(first, s_own, s_rcv))
    trail = (jnp.where(first, a_rcv, a_own), jnp.where(first, s_rcv, s_own))
    a_tot, s_tot = combine(lead, trail)

    def shift_pairs(k):
        return [
            (phys(2 * g + x), phys(2 * (g + k) + x)) for g in range(groups - k) for x in (0, 1)
        ]

    if groups <= 4:
        a_g = jnp.ones_like(a_tot)
        s_g = jnp.zeros_like(s_tot)
        for r in range(groups - 1):
            out = combine((a_g, s_g), (a_tot, s_tot))
            pairs = [(phys(2 * r + x), phys(2 * (r + 1) + x)) for x in (0, 1)]
            if r == groups - 2:
                s_in = lax.ppermute(out[1], axis, pairs)
                a_in = a_g
            else:
                a_in, s_in = lax.ppermute(out, axis, pairs)
            dst = group == r + 1
            a_g = jnp.where(dst, a_in, a_g)
            s_g = jnp.where(dst, s_in, s_g)
    else:
        a_g, s_g = lax.ppermute((a_tot, s_tot), axis, shift_pairs(1))
        a_g = jnp.where(group == 0, 1.0, a_g)
        s_g = jnp.where(group == 0, 0.0, s_g)
        k = 1
        while k < groups:
            got = lax.ppermute((a_g, s_g), axis, shift_pairs(k))
            a_c, s_c = combine(got, (a_g, s_g))
            a_g = jnp.where(group >= k, a_c, a_g)
            s_g = jnp.where(group >= k, s_c, s_g)
            k *= 2

    with_lead_own = a_own[:, None, None] * s_g + s_own
    with_lead_rcv = a_rcv[:, None, None] * s_g + s_rcv
    send = jnp.where(first, with_lead_own, s_g)
    keep = jnp.where(first, s_g, with_lead_rcv)
    other = lax.ppermute(send, axis, swap)
    return jnp.where(
        first, jnp.concatenate([other, keep], 0), jnp.concatenate([keep, other], 0)
    )


def butterfly_psum(parts, axis):
    count = lax.axis_size(axis)
    if count & (count - 1):
        return lax.psum(parts, axis)
    got = [parts] + [
        lax.ppermute(parts, axis, [(i, i ^ m) for i in range(count)]) for m in range(1, count)
    ]
    k = 1
    while k < count:
        got = [jax.tree.map(jnp.add, got[m], got[m ^ k]) if m % (2 * k) == 0 else None
               for m in range(count)]
        k *= 2
    return got[0]


def block_step(carry_state, inputs, skip_scale):
    feat_block, step_block, decay_block, write_block, read_block = inputs
    length = decay_block.shape[1]
    cumul = jnp.cumsum(decay_block, axis=1)
    row_index = lax.broadcasted_iota(jnp.int32, (length, length), 0)
    col_index = lax.broadcasted_iota(jnp.int32, (length, length), 1)
    causal = row_index >= col_index
    gaps = jnp.where(causal[None], cumul[:, :, None] - cumul[:, None, :], 0.0)
    weights = jnp.where(causal[None], jnp.exp(gaps), 0.0)
    scores = jnp.dot(read_block, jnp.transpose(write_block), precision=highest)
    scaled = feat_block * jnp.transpose(step_block)[:, :, None]
    masked = weights * scores[None]
    within = jnp.einsum("hij,jhp->ihp", masked, scaled, precision=highest)
    carried = jnp.einsum("in,hpn->ihp", read_block, carry_state, precision=highest)
    carried = carried * jnp.transpose(jnp.exp(cumul))[:, :, None]
    output = within + carried + skip_scale[None, :, None] * feat_block
    to_end = jnp.exp(cumul[:, -1:] - cumul)
    weighted_in = scaled * jnp.transpose(to_end)[:, :, None]
    update = jnp.einsum("jhp,jn->hpn", weighted_in, write_block, precision=highest)
    new_state = jnp.exp(cumul[:, -1])[:, None, None] * carry_state + update
    return (new_state, output)


def run_mixer(
    features, step_sizes, log_decay, write_keys, read_queries, carry_state, skip_scale, block
):
    length = features.shape[0]
    head_count = step_sizes.shape[0]
    head_width = features.shape[1] // head_count
    block_total = length // block
    feat_blocks = features.reshape(block_total, block, head_count, head_width)
    step_blocks = jnp.transpose(step_sizes.reshape(head_count, block_total, block), (1, 0, 2))
    decay_blocks = jnp.transpose(log_decay.reshape(head_count, block_total, block), (1, 0, 2))
    write_blocks = write_keys.reshape(block_total, block, write_keys.shape[1])
    read_blocks = read_queries.reshape(block_total, block, read_queries.shape[1])

    def advance(carried_in, inputs):
        return block_step(carried_in, inputs, skip_scale)

    last_state, outputs = lax.scan(
        advance, carry_state, (feat_blocks, step_blocks, decay_blocks, write_blocks, read_blocks)
    )
    return (last_state, outputs.reshape(length, head_count * head_width))


def prefix_sum(decay_in):
    length = decay_in.shape[1]
    upper = (
        lax.broadcasted_iota(jnp.int32, (length, length), 0)
        <= lax.broadcasted_iota(jnp.int32, (length, length), 1)
    ).astype(decay_in.dtype)
    return jnp.dot(decay_in, upper, precision=highest)


def within_part(feat_in, step_in, decay_in, writes, read_in, skip_scale):
    head_count, length = step_in.shape
    head_width = feat_in.shape[1] // head_count
    cumul = prefix_sum(decay_in)
    row_index = lax.broadcasted_iota(jnp.int32, (length, length), 0)
    col_index = lax.broadcasted_iota(jnp.int32, (length, length), 1)
    causal = row_index >= col_index
    gaps = jnp.where(causal[None], cumul[:, :, None] - cumul[:, None, :], 0.0)
    weights = jnp.where(causal[None], jnp.exp(gaps), 0.0)
    scores = jnp.dot(read_in, jnp.transpose(writes), precision=highest)
    feat3 = feat_in.reshape(length, head_count, head_width)
    scaled = feat3 * jnp.transpose(step_in)[:, :, None]
    masked = weights * scores[None]
    within = jnp.einsum("hij,jhp->ihp", masked, scaled, precision=highest)
    return (within + skip_scale[None, :, None] * feat3).reshape(length, -1)


def carried_part(decay_in, read_in, state_in):
    length = decay_in.shape[1]
    cumul = prefix_sum(decay_in)
    carried = jnp.einsum("in,hpn->ihp", read_in, state_in, precision=highest)
    carried = carried * jnp.transpose(jnp.exp(cumul))[:, :, None]
    return carried.reshape(length, -1)


def state_update(feat_in, step_in, decay_in, writes):
    head_count, length = step_in.shape
    head_width = feat_in.shape[1] // head_count
    cumul = prefix_sum(decay_in)
    scaled = feat_in.reshape(length, head_count, head_width) * jnp.transpose(step_in)[:, :, None]
    to_end = jnp.exp(cumul[:, -1:] - cumul)
    weighted_in = scaled * jnp.transpose(to_end)[:, :, None]
    return jnp.einsum("jhp,jn->hpn", weighted_in, writes, precision=highest)


def end_part(feat_in, step_in, decay_in, writes, state_in):
    total = jnp.exp(prefix_sum(decay_in)[:, -1])
    return total[:, None, None] * state_in + state_update(feat_in, step_in, decay_in, writes)


def local(
    features,
    gate_pre,
    write_keys,
    read_queries,
    step_sizes,
    log_decay,
    skip_scale,
    norm_gain,
    out_grad,
):
    head_count, length = step_sizes.shape
    head_width = features.shape[1] // head_count
    channels = features.shape[1] * lax.axis_size("head")
    cumul = prefix_sum(log_decay)
    decay_total = jnp.exp(cumul[:, -1])
    scaled = (
        features.reshape(length, head_count, head_width) * jnp.transpose(step_sizes)[:, :, None]
    )
    to_end = jnp.exp(cumul[:, -1:] - cumul)
    weighted_in = scaled * jnp.transpose(to_end)[:, :, None]
    local_state = jnp.einsum("jhp,jn->hpn", weighted_in, write_keys, precision=highest)
    state_in = pair_scan(decay_total, local_state, "seq", False)
    single = length == BLOCK
    if single:
        mixed_w, pull_w = jax.vjp(
            lambda f, s, d, w, r: within_part(f, s, d, w, r, skip_scale),
            features, step_sizes, log_decay, write_keys, read_queries,
        )
        mixed_c, pull_c = jax.vjp(
            lambda d, r: carried_part(d, r, state_in), log_decay, read_queries
        )
        mixed_out = mixed_w + mixed_c
    else:

        def local_mixer(feat_in, step_in, decay_factors, writes, read_in):
            return run_mixer(
                feat_in, step_in, decay_factors, writes, read_in, state_in, skip_scale, BLOCK
            )

        primal, pullback = jax.vjp(
            local_mixer, features, step_sizes, log_decay, write_keys, read_queries
        )
        mixed_out = primal[1]
    sigmoid_gate = jax.nn.sigmoid(gate_pre)
    active = gate_pre * sigmoid_gate
    gated_out = mixed_out * active
    weighted = out_grad * norm_gain[None, :]
    square_sum, cross_sum = butterfly_psum(
        jnp.stack([jnp.sum(gated_out * gated_out, axis=1), jnp.sum(weighted * gated_out, axis=1)]),
        "head",
    )
    inverse = lax.rsqrt(square_sum / channels + eps)
    grad_gated = (
        inverse[:, None] * weighted
        - (inverse * inverse * inverse * cross_sum / channels)[:, None] * gated_out
    )
    grad_mixed = grad_gated * active
    grad_gate = grad_gated * mixed_out * sigmoid_gate * (1.0 + gate_pre * (1.0 - sigmoid_gate))
    from_start = jnp.transpose(jnp.exp(cumul))
    weighted_grad = grad_mixed.reshape(length, head_count, head_width) * from_start[:, :, None]
    local_grad = jnp.einsum("jhp,jn->hpn", weighted_grad, read_queries, precision=highest)
    state_grad = pair_scan(decay_total, local_grad, "seq", True)
    if single:
        gf_w, gs_w, gd_w, gw_w, gr_w = pull_w(grad_mixed)
        gd_c, gr_c = pull_c(grad_mixed)
        grad_read = butterfly_psum(gr_w + gr_c, "head")
        _, pull_e = jax.vjp(
            lambda f, s, d, w: end_part(f, s, d, w, state_in),
            features, step_sizes, log_decay, write_keys,
        )
        gf_e, gs_e, gd_e, gw_e = pull_e(state_grad)
        grad_features = gf_w + gf_e
        grad_steps = gs_w + gs_e
        grad_decay = gd_w + gd_c + gd_e
        grad_write = butterfly_psum(gw_w + gw_e, "head")
    else:
        grad_features, grad_steps, grad_decay, grad_write, grad_read = pullback(
            (state_grad, grad_mixed)
        )
        grad_write, grad_read = butterfly_psum((grad_write, grad_read), "head")
    return (grad_features, grad_gate, grad_write, grad_read, grad_steps, grad_decay)


def solution(mesh):
    placed = (
        P("seq", "head"),
        P("seq", "head"),
        P("seq", None),
        P("seq", None),
        P("head", "seq"),
        P("head", "seq"),
        P("head"),
        P("head"),
        P("seq", "head"),
    )
    return jax.shard_map(
        local,
        mesh=mesh,
        in_specs=placed,
        out_specs=(
            P("seq", "head"),
            P("seq", "head"),
            P("seq", None),
            P("seq", None),
            P("head", "seq"),
            P("head", "seq"),
        ),
        check_vma=False,
    )
```

```python
import jax
import jax.numpy as jnp
from jax import lax
from jax.sharding import PartitionSpec as P

BLOCK = 128


eps = 1e-05
highest = lax.Precision.HIGH


def combine(earlier, later):
    return (earlier[0] * later[0], later[0][:, None, None] * earlier[1] + later[1])


def pair_scan(decay, state, axis, reverse):
    count = lax.axis_size(axis)
    if count == 1:
        return jnp.zeros_like(state)
    assert count % 2 == 0 and decay.shape[0] % 2 == 0
    place = lax.axis_index(axis)
    virt = count - 1 - place if reverse else place

    def phys(u):
        return count - 1 - u if reverse else u

    half = decay.shape[0] // 2
    groups = count // 2
    side = virt % 2
    group = virt // 2
    first = side == 0
    own_start = (1 - side) * half
    send_start = side * half

    def part(x, start):
        return lax.dynamic_slice_in_dim(x, start, half, 0)

    a_own, s_own = part(decay, own_start), part(state, own_start)
    a_snd, s_snd = part(decay, send_start), part(state, send_start)
    swap = [(phys(u), phys(u ^ 1)) for u in range(count)]
    a_rcv, s_rcv = lax.ppermute((a_snd, s_snd), axis, swap)
    lead = (jnp.where(first, a_own, a_rcv), jnp.where(first, s_own, s_rcv))
    trail = (jnp.where(first, a_rcv, a_own), jnp.where(first, s_rcv, s_own))
    a_tot, s_tot = combine(lead, trail)

    def shift_pairs(k):
        return [
            (phys(2 * g + x), phys(2 * (g + k) + x)) for g in range(groups - k) for x in (0, 1)
        ]

    if groups <= 4:
        a_g = jnp.ones_like(a_tot)
        s_g = jnp.zeros_like(s_tot)
        for r in range(groups - 1):
            out = combine((a_g, s_g), (a_tot, s_tot))
            pairs = [(phys(2 * r + x), phys(2 * (r + 1) + x)) for x in (0, 1)]
            if r == groups - 2:
                s_in = lax.ppermute(out[1], axis, pairs)
                a_in = a_g
            else:
                a_in, s_in = lax.ppermute(out, axis, pairs)
            dst = group == r + 1
            a_g = jnp.where(dst, a_in, a_g)
            s_g = jnp.where(dst, s_in, s_g)
    else:
        a_g, s_g = lax.ppermute((a_tot, s_tot), axis, shift_pairs(1))
        a_g = jnp.where(group == 0, 1.0, a_g)
        s_g = jnp.where(group == 0, 0.0, s_g)
        k = 1
        while k < groups:
            got = lax.ppermute((a_g, s_g), axis, shift_pairs(k))
            a_c, s_c = combine(got, (a_g, s_g))
            a_g = jnp.where(group >= k, a_c, a_g)
            s_g = jnp.where(group >= k, s_c, s_g)
            k *= 2

    with_lead_own = a_own[:, None, None] * s_g + s_own
    with_lead_rcv = a_rcv[:, None, None] * s_g + s_rcv
    send = jnp.where(first, with_lead_own, s_g)
    keep = jnp.where(first, s_g, with_lead_rcv)
    other = lax.ppermute(send, axis, swap)
    return jnp.where(
        first, jnp.concatenate([other, keep], 0), jnp.concatenate([keep, other], 0)
    )


def butterfly_psum(parts, axis):
    count = lax.axis_size(axis)
    if count & (count - 1):
        return lax.psum(parts, axis)
    k = 1
    while k < count:
        got = lax.ppermute(parts, axis, [(i, i ^ k) for i in range(count)])
        parts = jax.tree.map(jnp.add, parts, got)
        k *= 2
    return parts


def block_step(carry_state, inputs, skip_scale):
    feat_block, step_block, decay_block, write_block, read_block = inputs
    length = decay_block.shape[1]
    cumul = jnp.cumsum(decay_block, axis=1)
    row_index = lax.broadcasted_iota(jnp.int32, (length, length), 0)
    col_index = lax.broadcasted_iota(jnp.int32, (length, length), 1)
    causal = row_index >= col_index
    gaps = jnp.where(causal[None], cumul[:, :, None] - cumul[:, None, :], 0.0)
    weights = jnp.where(causal[None], jnp.exp(gaps), 0.0)
    scores = jnp.dot(read_block, jnp.transpose(write_block), precision=highest)
    scaled = feat_block * jnp.transpose(step_block)[:, :, None]
    masked = weights * scores[None]
    within = jnp.einsum("hij,jhp->ihp", masked, scaled, precision=highest)
    carried = jnp.einsum("in,hpn->ihp", read_block, carry_state, precision=highest)
    carried = carried * jnp.transpose(jnp.exp(cumul))[:, :, None]
    output = within + carried + skip_scale[None, :, None] * feat_block
    to_end = jnp.exp(cumul[:, -1:] - cumul)
    weighted_in = scaled * jnp.transpose(to_end)[:, :, None]
    update = jnp.einsum("jhp,jn->hpn", weighted_in, write_block, precision=highest)
    new_state = jnp.exp(cumul[:, -1])[:, None, None] * carry_state + update
    return (new_state, output)


def run_mixer(
    features, step_sizes, log_decay, write_keys, read_queries, carry_state, skip_scale, block
):
    length = features.shape[0]
    head_count = step_sizes.shape[0]
    head_width = features.shape[1] // head_count
    block_total = length // block
    feat_blocks = features.reshape(block_total, block, head_count, head_width)
    step_blocks = jnp.transpose(step_sizes.reshape(head_count, block_total, block), (1, 0, 2))
    decay_blocks = jnp.transpose(log_decay.reshape(head_count, block_total, block), (1, 0, 2))
    write_blocks = write_keys.reshape(block_total, block, write_keys.shape[1])
    read_blocks = read_queries.reshape(block_total, block, read_queries.shape[1])

    def advance(carried_in, inputs):
        return block_step(carried_in, inputs, skip_scale)

    last_state, outputs = lax.scan(
        advance, carry_state, (feat_blocks, step_blocks, decay_blocks, write_blocks, read_blocks)
    )
    return (last_state, outputs.reshape(length, head_count * head_width))


def prefix_sum(decay_in):
    length = decay_in.shape[1]
    upper = (
        lax.broadcasted_iota(jnp.int32, (length, length), 0)
        <= lax.broadcasted_iota(jnp.int32, (length, length), 1)
    ).astype(decay_in.dtype)
    return jnp.dot(decay_in, upper, precision=lax.Precision.HIGHEST)


def within_part(feat_in, step_in, decay_in, writes, read_in, skip_scale):
    head_count, length = step_in.shape
    head_width = feat_in.shape[1] // head_count
    cumul = prefix_sum(decay_in)
    row_index = lax.broadcasted_iota(jnp.int32, (length, length), 0)
    col_index = lax.broadcasted_iota(jnp.int32, (length, length), 1)
    causal = row_index >= col_index
    gaps = jnp.where(causal[None], cumul[:, :, None] - cumul[:, None, :], 0.0)
    weights = jnp.where(causal[None], jnp.exp(gaps), 0.0)
    scores = jnp.dot(read_in, jnp.transpose(writes), precision=highest)
    feat3 = feat_in.reshape(length, head_count, head_width)
    scaled = feat3 * jnp.transpose(step_in)[:, :, None]
    masked = weights * scores[None]
    within = jnp.einsum("hij,jhp->ihp", masked, scaled, precision=highest)
    return (within + skip_scale[None, :, None] * feat3).reshape(length, -1)


def carried_part(decay_in, read_in, state_in):
    length = decay_in.shape[1]
    cumul = prefix_sum(decay_in)
    carried = jnp.einsum("in,hpn->ihp", read_in, state_in, precision=highest)
    carried = carried * jnp.transpose(jnp.exp(cumul))[:, :, None]
    return carried.reshape(length, -1)


def state_update(feat_in, step_in, decay_in, writes):
    head_count, length = step_in.shape
    head_width = feat_in.shape[1] // head_count
    cumul = prefix_sum(decay_in)
    scaled = feat_in.reshape(length, head_count, head_width) * jnp.transpose(step_in)[:, :, None]
    to_end = jnp.exp(cumul[:, -1:] - cumul)
    weighted_in = scaled * jnp.transpose(to_end)[:, :, None]
    return jnp.einsum("jhp,jn->hpn", weighted_in, writes, precision=highest)


def end_part(feat_in, step_in, decay_in, writes, state_in):
    total = jnp.exp(prefix_sum(decay_in)[:, -1])
    return total[:, None, None] * state_in + state_update(feat_in, step_in, decay_in, writes)


def local(
    features,
    gate_pre,
    write_keys,
    read_queries,
    step_sizes,
    log_decay,
    skip_scale,
    norm_gain,
    out_grad,
):
    head_count, length = step_sizes.shape
    head_width = features.shape[1] // head_count
    channels = features.shape[1] * lax.axis_size("head")
    cumul = prefix_sum(log_decay)
    decay_total = jnp.exp(cumul[:, -1])
    scaled = (
        features.reshape(length, head_count, head_width) * jnp.transpose(step_sizes)[:, :, None]
    )
    to_end = jnp.exp(cumul[:, -1:] - cumul)
    weighted_in = scaled * jnp.transpose(to_end)[:, :, None]
    local_state = jnp.einsum("jhp,jn->hpn", weighted_in, write_keys, precision=highest)
    state_in = pair_scan(decay_total, local_state, "seq", False)
    single = length == BLOCK
    if single:
        mixed_w, pull_w = jax.vjp(
            lambda f, s, d, w, r: within_part(f, s, d, w, r, skip_scale),
            features, step_sizes, log_decay, write_keys, read_queries,
        )
        mixed_c, pull_c = jax.vjp(
            lambda d, r: carried_part(d, r, state_in), log_decay, read_queries
        )
        mixed_out = mixed_w + mixed_c
    else:

        def local_mixer(feat_in, step_in, decay_factors, writes, read_in):
            return run_mixer(
                feat_in, step_in, decay_factors, writes, read_in, state_in, skip_scale, BLOCK
            )

        primal, pullback = jax.vjp(
            local_mixer, features, step_sizes, log_decay, write_keys, read_queries
        )
        mixed_out = primal[1]
    sigmoid_gate = jax.nn.sigmoid(gate_pre)
    active = gate_pre * sigmoid_gate
    gated_out = mixed_out * active
    weighted = out_grad * norm_gain[None, :]
    square_sum, cross_sum = butterfly_psum(
        (jnp.sum(gated_out * gated_out, axis=1), jnp.sum(weighted * gated_out, axis=1)), "head"
    )
    inverse = lax.rsqrt(square_sum / channels + eps)
    grad_gated = (
        inverse[:, None] * weighted
        - (inverse * inverse * inverse * cross_sum / channels)[:, None] * gated_out
    )
    grad_mixed = grad_gated * active
    grad_gate = grad_gated * mixed_out * sigmoid_gate * (1.0 + gate_pre * (1.0 - sigmoid_gate))
    from_start = jnp.transpose(jnp.exp(cumul))
    weighted_grad = grad_mixed.reshape(length, head_count, head_width) * from_start[:, :, None]
    local_grad = jnp.einsum("jhp,jn->hpn", weighted_grad, read_queries, precision=highest)
    state_grad = pair_scan(decay_total, local_grad, "seq", True)
    if single:
        gf_w, gs_w, gd_w, gw_w, gr_w = pull_w(grad_mixed)
        gd_c, gr_c = pull_c(grad_mixed)
        grad_read = butterfly_psum(gr_w + gr_c, "head")
        _, pull_e = jax.vjp(
            lambda f, s, d, w: end_part(f, s, d, w, state_in),
            features, step_sizes, log_decay, write_keys,
        )
        gf_e, gs_e, gd_e, gw_e = pull_e(state_grad)
        grad_features = gf_w + gf_e
        grad_steps = gs_w + gs_e
        grad_decay = gd_w + gd_c + gd_e
        grad_write = butterfly_psum(gw_w + gw_e, "head")
    else:
        grad_features, grad_steps, grad_decay, grad_write, grad_read = pullback(
            (state_grad, grad_mixed)
        )
        grad_write, grad_read = butterfly_psum((grad_write, grad_read), "head")
    return (grad_features, grad_gate, grad_write, grad_read, grad_steps, grad_decay)


def solution(mesh):
    placed = (
        P("seq", "head"),
        P("seq", "head"),
        P("seq", None),
        P("seq", None),
        P("head", "seq"),
        P("head", "seq"),
        P("head"),
        P("head"),
        P("seq", "head"),
    )
    return jax.shard_map(
        local,
        mesh=mesh,
        in_specs=placed,
        out_specs=(
            P("seq", "head"),
            P("seq", "head"),
            P("seq", None),
            P("seq", None),
            P("head", "seq"),
            P("head", "seq"),
        ),
        check_vma=False,
    )
```

```python
import jax
import jax.numpy as jnp
from jax import lax
from jax.sharding import PartitionSpec as P

BLOCK = 128


eps = 1e-05
highest = lax.Precision.HIGH


def combine(earlier, later):
    return (earlier[0] * later[0], later[0][None, :] * earlier[1] + later[1])


def pair_scan(decay, state, axis, reverse):
    count = lax.axis_size(axis)
    if count == 1:
        return jnp.zeros_like(state)
    assert count % 2 == 0 and decay.shape[0] % 2 == 0 and state.shape[1] == decay.shape[0]
    place = lax.axis_index(axis)
    virt = count - 1 - place if reverse else place

    def phys(u):
        return count - 1 - u if reverse else u

    half = decay.shape[0] // 2
    groups = count // 2
    side = virt % 2
    group = virt // 2
    first = side == 0
    own_start = (1 - side) * half
    send_start = side * half

    def part(x, start):
        return lax.dynamic_slice_in_dim(x, start, half, x.ndim - 1)

    a_own, s_own = part(decay, own_start), part(state, own_start)
    a_snd, s_snd = part(decay, send_start), part(state, send_start)
    swap = [(phys(u), phys(u ^ 1)) for u in range(count)]
    a_rcv, s_rcv = lax.ppermute((a_snd, s_snd), axis, swap)
    lead = (jnp.where(first, a_own, a_rcv), jnp.where(first, s_own, s_rcv))
    trail = (jnp.where(first, a_rcv, a_own), jnp.where(first, s_rcv, s_own))
    a_tot, s_tot = combine(lead, trail)

    def shift_pairs(k):
        return [
            (phys(2 * g + x), phys(2 * (g + k) + x)) for g in range(groups - k) for x in (0, 1)
        ]

    if groups <= 4:
        a_g = jnp.ones_like(a_tot)
        s_g = jnp.zeros_like(s_tot)
        for r in range(groups - 1):
            out = combine((a_g, s_g), (a_tot, s_tot))
            pairs = [(phys(2 * r + x), phys(2 * (r + 1) + x)) for x in (0, 1)]
            if r == groups - 2:
                s_in = lax.ppermute(out[1], axis, pairs)
                a_in = a_g
            else:
                a_in, s_in = lax.ppermute(out, axis, pairs)
            dst = group == r + 1
            a_g = jnp.where(dst, a_in, a_g)
            s_g = jnp.where(dst, s_in, s_g)
    else:
        a_g, s_g = lax.ppermute((a_tot, s_tot), axis, shift_pairs(1))
        a_g = jnp.where(group == 0, 1.0, a_g)
        s_g = jnp.where(group == 0, 0.0, s_g)
        k = 1
        while k < groups:
            got = lax.ppermute((a_g, s_g), axis, shift_pairs(k))
            a_c, s_c = combine(got, (a_g, s_g))
            a_g = jnp.where(group >= k, a_c, a_g)
            s_g = jnp.where(group >= k, s_c, s_g)
            k *= 2

    with_lead_own = a_own[None, :] * s_g + s_own
    with_lead_rcv = a_rcv[None, :] * s_g + s_rcv
    send = jnp.where(first, with_lead_own, s_g)
    keep = jnp.where(first, s_g, with_lead_rcv)
    other = lax.ppermute(send, axis, swap)
    return jnp.where(
        first, jnp.concatenate([other, keep], 1), jnp.concatenate([keep, other], 1)
    )


def butterfly_psum(parts, axis):
    count = lax.axis_size(axis)
    if count & (count - 1):
        return lax.psum(parts, axis)
    k = 1
    while k < count:
        got = lax.ppermute(parts, axis, [(i, i ^ k) for i in range(count)])
        parts = jax.tree.map(jnp.add, parts, got)
        k *= 2
    return parts


def block_step(carry_state, inputs, skip_scale):
    feat_block, step_block, decay_block, write_block, read_block = inputs
    length = decay_block.shape[1]
    cumul = jnp.cumsum(decay_block, axis=1)
    row_index = lax.broadcasted_iota(jnp.int32, (length, length), 0)
    col_index = lax.broadcasted_iota(jnp.int32, (length, length), 1)
    causal = row_index >= col_index
    gaps = jnp.where(causal[None], cumul[:, :, None] - cumul[:, None, :], 0.0)
    weights = jnp.where(causal[None], jnp.exp(gaps), 0.0)
    scores = jnp.dot(read_block, jnp.transpose(write_block), precision=highest)
    scaled = feat_block * jnp.transpose(step_block)[:, :, None]
    masked = weights * scores[None]
    within = jnp.einsum("hij,jhp->ihp", masked, scaled, precision=highest)
    carried = jnp.einsum("in,hpn->ihp", read_block, carry_state, precision=highest)
    carried = carried * jnp.transpose(jnp.exp(cumul))[:, :, None]
    output = within + carried + skip_scale[None, :, None] * feat_block
    to_end = jnp.exp(cumul[:, -1:] - cumul)
    weighted_in = scaled * jnp.transpose(to_end)[:, :, None]
    update = jnp.einsum("jhp,jn->hpn", weighted_in, write_block, precision=highest)
    new_state = jnp.exp(cumul[:, -1])[:, None, None] * carry_state + update
    return (new_state, output)


def run_mixer(
    features, step_sizes, log_decay, write_keys, read_queries, carry_state, skip_scale, block
):
    length = features.shape[0]
    head_count = step_sizes.shape[0]
    head_width = features.shape[1] // head_count
    block_total = length // block
    feat_blocks = features.reshape(block_total, block, head_count, head_width)
    step_blocks = jnp.transpose(step_sizes.reshape(head_count, block_total, block), (1, 0, 2))
    decay_blocks = jnp.transpose(log_decay.reshape(head_count, block_total, block), (1, 0, 2))
    write_blocks = write_keys.reshape(block_total, block, write_keys.shape[1])
    read_blocks = read_queries.reshape(block_total, block, read_queries.shape[1])

    def advance(carried_in, inputs):
        return block_step(carried_in, inputs, skip_scale)

    last_state, outputs = lax.scan(
        advance, carry_state, (feat_blocks, step_blocks, decay_blocks, write_blocks, read_blocks)
    )
    return (last_state, outputs.reshape(length, head_count * head_width))


def prefix_sum(decay_in):
    length = decay_in.shape[1]
    upper = (
        lax.broadcasted_iota(jnp.int32, (length, length), 0)
        <= lax.broadcasted_iota(jnp.int32, (length, length), 1)
    ).astype(decay_in.dtype)
    return jnp.dot(decay_in, upper, precision=lax.Precision.HIGHEST)


def within_part(feat_in, step_in, decay_in, writes, read_in, skip_scale):
    head_count, length = step_in.shape
    head_width = feat_in.shape[1] // head_count
    cumul = prefix_sum(decay_in)
    row_index = lax.broadcasted_iota(jnp.int32, (length, length), 0)
    col_index = lax.broadcasted_iota(jnp.int32, (length, length), 1)
    causal = row_index >= col_index
    gaps = jnp.where(causal[None], cumul[:, :, None] - cumul[:, None, :], 0.0)
    weights = jnp.where(causal[None], jnp.exp(gaps), 0.0)
    scores = jnp.dot(read_in, jnp.transpose(writes), precision=highest)
    feat3 = feat_in.reshape(length, head_count, head_width)
    scaled = feat3 * jnp.transpose(step_in)[:, :, None]
    masked = weights * scores[None]
    within = jnp.einsum("hij,jhp->ihp", masked, scaled, precision=highest)
    return (within + skip_scale[None, :, None] * feat3).reshape(length, -1)


def per_channel(factors, head_width):
    return jnp.repeat(jnp.transpose(factors), head_width, axis=1)


def carried_part(decay_in, read_in, state_in):
    head_width = state_in.shape[1] // decay_in.shape[0]
    carried = jnp.dot(read_in, state_in, precision=highest)
    return carried * per_channel(jnp.exp(prefix_sum(decay_in)), head_width)


def state_update(feat_in, step_in, decay_in, writes):
    head_count, length = step_in.shape
    head_width = feat_in.shape[1] // head_count
    cumul = prefix_sum(decay_in)
    to_end = jnp.exp(cumul[:, -1:] - cumul)
    weighted_in = feat_in * per_channel(step_in * to_end, head_width)
    return lax.dot_general(writes, weighted_in, (((0,), (0,)), ((), ())), precision=highest)


def end_part(feat_in, step_in, decay_in, writes, state_in):
    head_width = feat_in.shape[1] // step_in.shape[0]
    total = jnp.repeat(jnp.exp(prefix_sum(decay_in)[:, -1]), head_width)
    return total[None, :] * state_in + state_update(feat_in, step_in, decay_in, writes)


def to_heads(state, head_count):
    return jnp.transpose(state).reshape(head_count, -1, state.shape[0])


def local(
    features,
    gate_pre,
    write_keys,
    read_queries,
    step_sizes,
    log_decay,
    skip_scale,
    norm_gain,
    out_grad,
):
    head_count, length = step_sizes.shape
    head_width = features.shape[1] // head_count
    channels = features.shape[1] * lax.axis_size("head")
    cumul = prefix_sum(log_decay)
    decay_total = jnp.exp(cumul[:, -1])
    decay_channels = jnp.repeat(decay_total, head_width)
    local_state = state_update(features, step_sizes, log_decay, write_keys)
    state_in = pair_scan(decay_channels, local_state, "seq", False)
    single = length == BLOCK
    if single:
        mixed_w, pull_w = jax.vjp(
            lambda f, s, d, w, r: within_part(f, s, d, w, r, skip_scale),
            features, step_sizes, log_decay, write_keys, read_queries,
        )
        mixed_c, pull_c = jax.vjp(
            lambda d, r: carried_part(d, r, state_in), log_decay, read_queries
        )
        mixed_out = mixed_w + mixed_c
    else:

        def local_mixer(feat_in, step_in, decay_factors, writes, read_in):
            return run_mixer(
                feat_in, step_in, decay_factors, writes, read_in,
                to_heads(state_in, head_count), skip_scale, BLOCK,
            )

        primal, pullback = jax.vjp(
            local_mixer, features, step_sizes, log_decay, write_keys, read_queries
        )
        mixed_out = primal[1]
    sigmoid_gate = jax.nn.sigmoid(gate_pre)
    active = gate_pre * sigmoid_gate
    gated_out = mixed_out * active
    weighted = out_grad * norm_gain[None, :]
    square_sum, cross_sum = butterfly_psum(
        (jnp.sum(gated_out * gated_out, axis=1), jnp.sum(weighted * gated_out, axis=1)), "head"
    )
    inverse = lax.rsqrt(square_sum / channels + eps)
    grad_gated = (
        inverse[:, None] * weighted
        - (inverse * inverse * inverse * cross_sum / channels)[:, None] * gated_out
    )
    grad_mixed = grad_gated * active
    grad_gate = grad_gated * mixed_out * sigmoid_gate * (1.0 + gate_pre * (1.0 - sigmoid_gate))
    weighted_grad = grad_mixed * per_channel(jnp.exp(cumul), head_width)
    local_grad = lax.dot_general(
        read_queries, weighted_grad, (((0,), (0,)), ((), ())), precision=highest
    )
    state_grad = pair_scan(decay_channels, local_grad, "seq", True)
    if single:
        gf_w, gs_w, gd_w, gw_w, gr_w = pull_w(grad_mixed)
        gd_c, gr_c = pull_c(grad_mixed)
        grad_read = butterfly_psum(gr_w + gr_c, "head")
        _, pull_e = jax.vjp(
            lambda f, s, d, w: end_part(f, s, d, w, state_in),
            features, step_sizes, log_decay, write_keys,
        )
        gf_e, gs_e, gd_e, gw_e = pull_e(state_grad)
        grad_features = gf_w + gf_e
        grad_steps = gs_w + gs_e
        grad_decay = gd_w + gd_c + gd_e
        grad_write = butterfly_psum(gw_w + gw_e, "head")
    else:
        grad_features, grad_steps, grad_decay, grad_write, grad_read = pullback(
            (to_heads(state_grad, head_count), grad_mixed)
        )
        grad_write, grad_read = butterfly_psum((grad_write, grad_read), "head")
    return (grad_features, grad_gate, grad_write, grad_read, grad_steps, grad_decay)


def solution(mesh):
    placed = (
        P("seq", "head"),
        P("seq", "head"),
        P("seq", None),
        P("seq", None),
        P("head", "seq"),
        P("head", "seq"),
        P("head"),
        P("head"),
        P("seq", "head"),
    )
    return jax.shard_map(
        local,
        mesh=mesh,
        in_specs=placed,
        out_specs=(
            P("seq", "head"),
            P("seq", "head"),
            P("seq", None),
            P("seq", None),
            P("head", "seq"),
            P("head", "seq"),
        ),
        check_vma=False,
    )
```

```python
import jax
import jax.numpy as jnp
from jax import lax
from jax.sharding import PartitionSpec as P

BLOCK = 128


eps = 1e-05
highest = lax.Precision.HIGH


def combine(earlier, later):
    return (earlier[0] * later[0], later[0][:, None, None] * earlier[1] + later[1])


def pair_scan(decay, state, axis, reverse):
    count = lax.axis_size(axis)
    if count == 1:
        return jnp.zeros_like(state)
    assert count % 2 == 0 and decay.shape[0] % 2 == 0
    place = lax.axis_index(axis)
    virt = count - 1 - place if reverse else place

    def phys(u):
        return count - 1 - u if reverse else u

    half = decay.shape[0] // 2
    groups = count // 2
    side = virt % 2
    group = virt // 2
    first = side == 0
    own_start = (1 - side) * half
    send_start = side * half

    def part(x, start):
        return lax.dynamic_slice_in_dim(x, start, half, 0)

    a_own, s_own = part(decay, own_start), part(state, own_start)
    a_snd, s_snd = part(decay, send_start), part(state, send_start)
    swap = [(phys(u), phys(u ^ 1)) for u in range(count)]
    a_rcv, s_rcv = lax.ppermute((a_snd, s_snd), axis, swap)
    lead = (jnp.where(first, a_own, a_rcv), jnp.where(first, s_own, s_rcv))
    trail = (jnp.where(first, a_rcv, a_own), jnp.where(first, s_rcv, s_own))
    a_tot, s_tot = combine(lead, trail)

    def shift_pairs(k):
        return [
            (phys(2 * g + x), phys(2 * (g + k) + x)) for g in range(groups - k) for x in (0, 1)
        ]

    if groups <= 4:
        a_g = jnp.ones_like(a_tot)
        s_g = jnp.zeros_like(s_tot)
        for r in range(groups - 1):
            out = combine((a_g, s_g), (a_tot, s_tot))
            pairs = [(phys(2 * r + x), phys(2 * (r + 1) + x)) for x in (0, 1)]
            if r == groups - 2:
                s_in = lax.ppermute(out[1], axis, pairs)
                a_in = a_g
            else:
                a_in, s_in = lax.ppermute(out, axis, pairs)
            dst = group == r + 1
            a_g = jnp.where(dst, a_in, a_g)
            s_g = jnp.where(dst, s_in, s_g)
    else:
        a_g, s_g = lax.ppermute((a_tot, s_tot), axis, shift_pairs(1))
        a_g = jnp.where(group == 0, 1.0, a_g)
        s_g = jnp.where(group == 0, 0.0, s_g)
        k = 1
        while k < groups:
            got = lax.ppermute((a_g, s_g), axis, shift_pairs(k))
            a_c, s_c = combine(got, (a_g, s_g))
            a_g = jnp.where(group >= k, a_c, a_g)
            s_g = jnp.where(group >= k, s_c, s_g)
            k *= 2

    with_lead_own = a_own[:, None, None] * s_g + s_own
    with_lead_rcv = a_rcv[:, None, None] * s_g + s_rcv
    send = jnp.where(first, with_lead_own, s_g)
    keep = jnp.where(first, s_g, with_lead_rcv)
    other = lax.ppermute(send, axis, swap)
    return jnp.where(
        first, jnp.concatenate([other, keep], 0), jnp.concatenate([keep, other], 0)
    )


def butterfly_psum(parts, axis):
    count = lax.axis_size(axis)
    if count & (count - 1):
        return lax.psum(parts, axis)
    k = 1
    while k < count:
        got = lax.ppermute(parts, axis, [(i, i ^ k) for i in range(count)])
        parts = jax.tree.map(jnp.add, parts, got)
        k *= 2
    return parts


def fan_psum(parts, axis):
    count = lax.axis_size(axis)
    if count & (count - 1):
        return lax.psum(parts, axis)
    got = [parts] + [
        lax.ppermute(parts, axis, [(i, i ^ m) for i in range(count)]) for m in range(1, count)
    ]
    k = 1
    while k < count:
        got = [got[m] + got[m ^ k] if m % (2 * k) == 0 else None for m in range(count)]
        k *= 2
    return got[0]


def block_step(carry_state, inputs, skip_scale):
    feat_block, step_block, decay_block, write_block, read_block = inputs
    length = decay_block.shape[1]
    cumul = jnp.cumsum(decay_block, axis=1)
    row_index = lax.broadcasted_iota(jnp.int32, (length, length), 0)
    col_index = lax.broadcasted_iota(jnp.int32, (length, length), 1)
    causal = row_index >= col_index
    gaps = jnp.where(causal[None], cumul[:, :, None] - cumul[:, None, :], 0.0)
    weights = jnp.where(causal[None], jnp.exp(gaps), 0.0)
    scores = jnp.dot(read_block, jnp.transpose(write_block), precision=highest)
    scaled = feat_block * jnp.transpose(step_block)[:, :, None]
    masked = weights * scores[None]
    within = jnp.einsum("hij,jhp->ihp", masked, scaled, precision=highest)
    carried = jnp.einsum("in,hpn->ihp", read_block, carry_state, precision=highest)
    carried = carried * jnp.transpose(jnp.exp(cumul))[:, :, None]
    output = within + carried + skip_scale[None, :, None] * feat_block
    to_end = jnp.exp(cumul[:, -1:] - cumul)
    weighted_in = scaled * jnp.transpose(to_end)[:, :, None]
    update = jnp.einsum("jhp,jn->hpn", weighted_in, write_block, precision=highest)
    new_state = jnp.exp(cumul[:, -1])[:, None, None] * carry_state + update
    return (new_state, output)


def run_mixer(
    features, step_sizes, log_decay, write_keys, read_queries, carry_state, skip_scale, block
):
    length = features.shape[0]
    head_count = step_sizes.shape[0]
    head_width = features.shape[1] // head_count
    block_total = length // block
    feat_blocks = features.reshape(block_total, block, head_count, head_width)
    step_blocks = jnp.transpose(step_sizes.reshape(head_count, block_total, block), (1, 0, 2))
    decay_blocks = jnp.transpose(log_decay.reshape(head_count, block_total, block), (1, 0, 2))
    write_blocks = write_keys.reshape(block_total, block, write_keys.shape[1])
    read_blocks = read_queries.reshape(block_total, block, read_queries.shape[1])

    def advance(carried_in, inputs):
        return block_step(carried_in, inputs, skip_scale)

    last_state, outputs = lax.scan(
        advance, carry_state, (feat_blocks, step_blocks, decay_blocks, write_blocks, read_blocks)
    )
    return (last_state, outputs.reshape(length, head_count * head_width))


def prefix_sum(decay_in):
    length = decay_in.shape[1]
    upper = (
        lax.broadcasted_iota(jnp.int32, (length, length), 0)
        <= lax.broadcasted_iota(jnp.int32, (length, length), 1)
    ).astype(decay_in.dtype)
    return jnp.dot(decay_in, upper, precision=lax.Precision.HIGHEST)


def within_part(feat_in, step_in, decay_in, writes, read_in, skip_scale):
    head_count, length = step_in.shape
    head_width = feat_in.shape[1] // head_count
    cumul = prefix_sum(decay_in)
    row_index = lax.broadcasted_iota(jnp.int32, (length, length), 0)
    col_index = lax.broadcasted_iota(jnp.int32, (length, length), 1)
    causal = row_index >= col_index
    gaps = jnp.where(causal[None], cumul[:, :, None] - cumul[:, None, :], 0.0)
    weights = jnp.where(causal[None], jnp.exp(gaps), 0.0)
    scores = jnp.dot(read_in, jnp.transpose(writes), precision=highest)
    feat3 = feat_in.reshape(length, head_count, head_width)
    scaled = feat3 * jnp.transpose(step_in)[:, :, None]
    masked = weights * scores[None]
    within = jnp.einsum("hij,jhp->ihp", masked, scaled, precision=highest)
    return (within + skip_scale[None, :, None] * feat3).reshape(length, -1)


def carried_part(decay_in, read_in, state_in):
    length = decay_in.shape[1]
    cumul = prefix_sum(decay_in)
    carried = jnp.einsum("in,hpn->ihp", read_in, state_in, precision=highest)
    carried = carried * jnp.transpose(jnp.exp(cumul))[:, :, None]
    return carried.reshape(length, -1)


def state_update(feat_in, step_in, decay_in, writes):
    head_count, length = step_in.shape
    head_width = feat_in.shape[1] // head_count
    cumul = prefix_sum(decay_in)
    scaled = feat_in.reshape(length, head_count, head_width) * jnp.transpose(step_in)[:, :, None]
    to_end = jnp.exp(cumul[:, -1:] - cumul)
    weighted_in = scaled * jnp.transpose(to_end)[:, :, None]
    return jnp.einsum("jhp,jn->hpn", weighted_in, writes, precision=highest)


def end_part(feat_in, step_in, decay_in, writes, state_in):
    total = jnp.exp(prefix_sum(decay_in)[:, -1])
    return total[:, None, None] * state_in + state_update(feat_in, step_in, decay_in, writes)


def local(
    features,
    gate_pre,
    write_keys,
    read_queries,
    step_sizes,
    log_decay,
    skip_scale,
    norm_gain,
    out_grad,
):
    head_count, length = step_sizes.shape
    head_width = features.shape[1] // head_count
    channels = features.shape[1] * lax.axis_size("head")
    cumul = prefix_sum(log_decay)
    decay_total = jnp.exp(cumul[:, -1])
    scaled = (
        features.reshape(length, head_count, head_width) * jnp.transpose(step_sizes)[:, :, None]
    )
    to_end = jnp.exp(cumul[:, -1:] - cumul)
    weighted_in = scaled * jnp.transpose(to_end)[:, :, None]
    local_state = jnp.einsum("jhp,jn->hpn", weighted_in, write_keys, precision=highest)
    state_in = pair_scan(decay_total, local_state, "seq", False)
    single = length == BLOCK
    if single:
        mixed_w, pull_w = jax.vjp(
            lambda f, s, d, w, r: within_part(f, s, d, w, r, skip_scale),
            features, step_sizes, log_decay, write_keys, read_queries,
        )
        mixed_c, pull_c = jax.vjp(
            lambda d, r: carried_part(d, r, state_in), log_decay, read_queries
        )
        mixed_out = mixed_w + mixed_c
    else:

        def local_mixer(feat_in, step_in, decay_factors, writes, read_in):
            return run_mixer(
                feat_in, step_in, decay_factors, writes, read_in, state_in, skip_scale, BLOCK
            )

        primal, pullback = jax.vjp(
            local_mixer, features, step_sizes, log_decay, write_keys, read_queries
        )
        mixed_out = primal[1]
    sigmoid_gate = jax.nn.sigmoid(gate_pre)
    active = gate_pre * sigmoid_gate
    gated_out = mixed_out * active
    weighted = out_grad * norm_gain[None, :]
    square_sum, cross_sum = fan_psum(
        jnp.stack([jnp.sum(gated_out * gated_out, axis=1), jnp.sum(weighted * gated_out, axis=1)]),
        "head",
    )
    inverse = lax.rsqrt(square_sum / channels + eps)
    grad_gated = (
        inverse[:, None] * weighted
        - (inverse * inverse * inverse * cross_sum / channels)[:, None] * gated_out
    )
    grad_mixed = grad_gated * active
    grad_gate = grad_gated * mixed_out * sigmoid_gate * (1.0 + gate_pre * (1.0 - sigmoid_gate))
    from_start = jnp.transpose(jnp.exp(cumul))
    weighted_grad = grad_mixed.reshape(length, head_count, head_width) * from_start[:, :, None]
    local_grad = jnp.einsum("jhp,jn->hpn", weighted_grad, read_queries, precision=highest)
    state_grad = pair_scan(decay_total, local_grad, "seq", True)
    if single:
        gf_w, gs_w, gd_w, gw_w, gr_w = pull_w(grad_mixed)
        gd_c, gr_c = pull_c(grad_mixed)
        grad_read = butterfly_psum(gr_w + gr_c, "head")
        _, pull_e = jax.vjp(
            lambda f, s, d, w: end_part(f, s, d, w, state_in),
            features, step_sizes, log_decay, write_keys,
        )
        gf_e, gs_e, gd_e, gw_e = pull_e(state_grad)
        grad_features = gf_w + gf_e
        grad_steps = gs_w + gs_e
        grad_decay = gd_w + gd_c + gd_e
        grad_write = butterfly_psum(gw_w + gw_e, "head")
    else:
        grad_features, grad_steps, grad_decay, grad_write, grad_read = pullback(
            (state_grad, grad_mixed)
        )
        grad_write, grad_read = butterfly_psum((grad_write, grad_read), "head")
    return (grad_features, grad_gate, grad_write, grad_read, grad_steps, grad_decay)


def solution(mesh):
    placed = (
        P("seq", "head"),
        P("seq", "head"),
        P("seq", None),
        P("seq", None),
        P("head", "seq"),
        P("head", "seq"),
        P("head"),
        P("head"),
        P("seq", "head"),
    )
    return jax.shard_map(
        local,
        mesh=mesh,
        in_specs=placed,
        out_specs=(
            P("seq", "head"),
            P("seq", "head"),
            P("seq", None),
            P("seq", None),
            P("head", "seq"),
            P("head", "seq"),
        ),
        check_vma=False,
    )
```

```python
import jax
import jax.numpy as jnp
from jax import lax
from jax.sharding import PartitionSpec as P

BLOCK = 128


eps = 1e-05
highest = lax.Precision.HIGH


def combine(earlier, later):
    return (earlier[0] * later[0], later[0][:, None, None] * earlier[1] + later[1])


def pair_scan(decay, state, axis, reverse):
    count = lax.axis_size(axis)
    if count == 1:
        return jnp.zeros_like(state)
    assert count % 2 == 0 and decay.shape[0] % 2 == 0
    place = lax.axis_index(axis)
    virt = count - 1 - place if reverse else place

    def phys(u):
        return count - 1 - u if reverse else u

    half = decay.shape[0] // 2
    groups = count // 2
    side = virt % 2
    group = virt // 2
    first = side == 0
    own_start = (1 - side) * half
    send_start = side * half

    def part(x, start):
        return lax.dynamic_slice_in_dim(x, start, half, 0)

    a_own, s_own = part(decay, own_start), part(state, own_start)
    a_snd, s_snd = part(decay, send_start), part(state, send_start)
    swap = [(phys(u), phys(u ^ 1)) for u in range(count)]
    a_rcv, s_rcv = lax.ppermute((a_snd, s_snd), axis, swap)
    lead = (jnp.where(first, a_own, a_rcv), jnp.where(first, s_own, s_rcv))
    trail = (jnp.where(first, a_rcv, a_own), jnp.where(first, s_rcv, s_own))
    a_tot, s_tot = combine(lead, trail)

    def shift_pairs(k):
        return [
            (phys(2 * g + x), phys(2 * (g + k) + x)) for g in range(groups - k) for x in (0, 1)
        ]

    if groups <= 4:
        a_g = jnp.ones_like(a_tot)
        s_g = jnp.zeros_like(s_tot)
        for r in range(groups - 1):
            out = combine((a_g, s_g), (a_tot, s_tot))
            pairs = [(phys(2 * r + x), phys(2 * (r + 1) + x)) for x in (0, 1)]
            if r == groups - 2:
                s_in = lax.ppermute(out[1], axis, pairs)
                a_in = a_g
            else:
                a_in, s_in = lax.ppermute(out, axis, pairs)
            dst = group == r + 1
            a_g = jnp.where(dst, a_in, a_g)
            s_g = jnp.where(dst, s_in, s_g)
    else:
        a_g, s_g = lax.ppermute((a_tot, s_tot), axis, shift_pairs(1))
        a_g = jnp.where(group == 0, 1.0, a_g)
        s_g = jnp.where(group == 0, 0.0, s_g)
        k = 1
        while k < groups:
            got = lax.ppermute((a_g, s_g), axis, shift_pairs(k))
            a_c, s_c = combine(got, (a_g, s_g))
            a_g = jnp.where(group >= k, a_c, a_g)
            s_g = jnp.where(group >= k, s_c, s_g)
            k *= 2

    with_lead_own = a_own[:, None, None] * s_g + s_own
    with_lead_rcv = a_rcv[:, None, None] * s_g + s_rcv
    send = jnp.where(first, with_lead_own, s_g)
    keep = jnp.where(first, s_g, with_lead_rcv)
    other = lax.ppermute(send, axis, swap)
    return jnp.where(
        first, jnp.concatenate([other, keep], 0), jnp.concatenate([keep, other], 0)
    )


def butterfly_psum(parts, axis):
    count = lax.axis_size(axis)
    if count & (count - 1):
        return lax.psum(parts, axis)
    k = 1
    while k < count:
        got = lax.ppermute(parts, axis, [(i, i ^ k) for i in range(count)])
        parts = jax.tree.map(jnp.add, parts, got)
        k *= 2
    return parts


def block_step(carry_state, inputs, skip_scale):
    feat_block, step_block, decay_block, write_block, read_block = inputs
    length = decay_block.shape[1]
    cumul = jnp.cumsum(decay_block, axis=1)
    row_index = lax.broadcasted_iota(jnp.int32, (length, length), 0)
    col_index = lax.broadcasted_iota(jnp.int32, (length, length), 1)
    causal = row_index >= col_index
    gaps = jnp.where(causal[None], cumul[:, :, None] - cumul[:, None, :], 0.0)
    weights = jnp.where(causal[None], jnp.exp(gaps), 0.0)
    scores = jnp.dot(read_block, jnp.transpose(write_block), precision=highest)
    scaled = feat_block * jnp.transpose(step_block)[:, :, None]
    masked = weights * scores[None]
    within = jnp.einsum("hij,jhp->ihp", masked, scaled, precision=highest)
    carried = jnp.einsum("in,hpn->ihp", read_block, carry_state, precision=highest)
    carried = carried * jnp.transpose(jnp.exp(cumul))[:, :, None]
    output = within + carried + skip_scale[None, :, None] * feat_block
    to_end = jnp.exp(cumul[:, -1:] - cumul)
    weighted_in = scaled * jnp.transpose(to_end)[:, :, None]
    update = jnp.einsum("jhp,jn->hpn", weighted_in, write_block, precision=highest)
    new_state = jnp.exp(cumul[:, -1])[:, None, None] * carry_state + update
    return (new_state, output)


def run_mixer(
    features, step_sizes, log_decay, write_keys, read_queries, carry_state, skip_scale, block
):
    length = features.shape[0]
    head_count = step_sizes.shape[0]
    head_width = features.shape[1] // head_count
    block_total = length // block
    feat_blocks = features.reshape(block_total, block, head_count, head_width)
    step_blocks = jnp.transpose(step_sizes.reshape(head_count, block_total, block), (1, 0, 2))
    decay_blocks = jnp.transpose(log_decay.reshape(head_count, block_total, block), (1, 0, 2))
    write_blocks = write_keys.reshape(block_total, block, write_keys.shape[1])
    read_blocks = read_queries.reshape(block_total, block, read_queries.shape[1])

    def advance(carried_in, inputs):
        return block_step(carried_in, inputs, skip_scale)

    last_state, outputs = lax.scan(
        advance, carry_state, (feat_blocks, step_blocks, decay_blocks, write_blocks, read_blocks)
    )
    return (last_state, outputs.reshape(length, head_count * head_width))


def prefix_sum(decay_in):
    length = decay_in.shape[1]
    upper = (
        lax.broadcasted_iota(jnp.int32, (length, length), 0)
        <= lax.broadcasted_iota(jnp.int32, (length, length), 1)
    ).astype(decay_in.dtype)
    return jnp.dot(decay_in, upper, precision=lax.Precision.HIGHEST)


def within_part(feat_in, step_in, decay_in, writes, read_in, skip_scale):
    head_count, length = step_in.shape
    head_width = feat_in.shape[1] // head_count
    cumul = prefix_sum(decay_in)
    row_index = lax.broadcasted_iota(jnp.int32, (length, length), 0)
    col_index = lax.broadcasted_iota(jnp.int32, (length, length), 1)
    causal = row_index >= col_index
    gaps = jnp.where(causal[None], cumul[:, :, None] - cumul[:, None, :], 0.0)
    weights = jnp.where(causal[None], jnp.exp(gaps), 0.0)
    scores = jnp.dot(read_in, jnp.transpose(writes), precision=highest)
    feat3 = feat_in.reshape(length, head_count, head_width)
    scaled = feat3 * jnp.transpose(step_in)[:, :, None]
    masked = weights * scores[None]
    within = jnp.einsum("hij,jhp->ihp", masked, scaled, precision=highest)
    return (within + skip_scale[None, :, None] * feat3).reshape(length, -1)


def carried_part(decay_in, read_in, state_in):
    length = decay_in.shape[1]
    cumul = prefix_sum(decay_in)
    carried = jnp.einsum("in,hpn->ihp", read_in, state_in, precision=highest)
    carried = carried * jnp.transpose(jnp.exp(cumul))[:, :, None]
    return carried.reshape(length, -1)


def state_update(feat_in, step_in, decay_in, writes):
    head_count, length = step_in.shape
    head_width = feat_in.shape[1] // head_count
    cumul = prefix_sum(decay_in)
    scaled = feat_in.reshape(length, head_count, head_width) * jnp.transpose(step_in)[:, :, None]
    to_end = jnp.exp(cumul[:, -1:] - cumul)
    weighted_in = scaled * jnp.transpose(to_end)[:, :, None]
    return jnp.einsum("jhp,jn->hpn", weighted_in, writes, precision=highest)


def end_part(feat_in, step_in, decay_in, writes, state_in):
    total = jnp.exp(prefix_sum(decay_in)[:, -1])
    return total[:, None, None] * state_in + state_update(feat_in, step_in, decay_in, writes)


def local(
    features,
    gate_pre,
    write_keys,
    read_queries,
    step_sizes,
    log_decay,
    skip_scale,
    norm_gain,
    out_grad,
):
    head_count, length = step_sizes.shape
    head_width = features.shape[1] // head_count
    channels = features.shape[1] * lax.axis_size("head")
    cumul = prefix_sum(log_decay)
    decay_total = jnp.exp(cumul[:, -1])
    scaled = (
        features.reshape(length, head_count, head_width) * jnp.transpose(step_sizes)[:, :, None]
    )
    to_end = jnp.exp(cumul[:, -1:] - cumul)
    weighted_in = scaled * jnp.transpose(to_end)[:, :, None]
    local_state = jnp.einsum("jhp,jn->hpn", weighted_in, write_keys, precision=highest)
    state_in = pair_scan(decay_total, local_state, "seq", False)
    single = length == BLOCK
    if single:
        mixed_w, pull_w = jax.vjp(
            lambda f, s, d, w, r: within_part(f, s, d, w, r, skip_scale),
            features, step_sizes, log_decay, write_keys, read_queries,
        )
        mixed_c, pull_c = jax.vjp(
            lambda d, r: carried_part(d, r, state_in), log_decay, read_queries
        )
        mixed_w = lax.optimization_barrier(mixed_w)
        mixed_out = mixed_w + mixed_c
    else:

        def local_mixer(feat_in, step_in, decay_factors, writes, read_in):
            return run_mixer(
                feat_in, step_in, decay_factors, writes, read_in, state_in, skip_scale, BLOCK
            )

        primal, pullback = jax.vjp(
            local_mixer, features, step_sizes, log_decay, write_keys, read_queries
        )
        mixed_out = primal[1]
    sigmoid_gate = jax.nn.sigmoid(gate_pre)
    active = gate_pre * sigmoid_gate
    gated_out = mixed_out * active
    weighted = out_grad * norm_gain[None, :]
    square_sum, cross_sum = butterfly_psum(
        (jnp.sum(gated_out * gated_out, axis=1), jnp.sum(weighted * gated_out, axis=1)), "head"
    )
    inverse = lax.rsqrt(square_sum / channels + eps)
    grad_gated = (
        inverse[:, None] * weighted
        - (inverse * inverse * inverse * cross_sum / channels)[:, None] * gated_out
    )
    grad_mixed = grad_gated * active
    grad_gate = grad_gated * mixed_out * sigmoid_gate * (1.0 + gate_pre * (1.0 - sigmoid_gate))
    from_start = jnp.transpose(jnp.exp(cumul))
    weighted_grad = grad_mixed.reshape(length, head_count, head_width) * from_start[:, :, None]
    local_grad = jnp.einsum("jhp,jn->hpn", weighted_grad, read_queries, precision=highest)
    state_grad = pair_scan(decay_total, local_grad, "seq", True)
    if single:
        gf_w, gs_w, gd_w, gw_w, gr_w = pull_w(grad_mixed)
        gd_c, gr_c = pull_c(grad_mixed)
        grad_read = butterfly_psum(gr_w + gr_c, "head")
        _, pull_e = jax.vjp(
            lambda f, s, d, w: end_part(f, s, d, w, state_in),
            features, step_sizes, log_decay, write_keys,
        )
        gf_e, gs_e, gd_e, gw_e = pull_e(state_grad)
        grad_features = gf_w + gf_e
        grad_steps = gs_w + gs_e
        grad_decay = gd_w + gd_c + gd_e
        grad_write = butterfly_psum(gw_w + gw_e, "head")
    else:
        grad_features, grad_steps, grad_decay, grad_write, grad_read = pullback(
            (state_grad, grad_mixed)
        )
        grad_write, grad_read = butterfly_psum((grad_write, grad_read), "head")
    return (grad_features, grad_gate, grad_write, grad_read, grad_steps, grad_decay)


def solution(mesh):
    placed = (
        P("seq", "head"),
        P("seq", "head"),
        P("seq", None),
        P("seq", None),
        P("head", "seq"),
        P("head", "seq"),
        P("head"),
        P("head"),
        P("seq", "head"),
    )
    return jax.shard_map(
        local,
        mesh=mesh,
        in_specs=placed,
        out_specs=(
            P("seq", "head"),
            P("seq", "head"),
            P("seq", None),
            P("seq", None),
            P("head", "seq"),
            P("head", "seq"),
        ),
        check_vma=False,
    )
```

```python
import jax
import jax.numpy as jnp
from jax import lax
from jax.sharding import PartitionSpec as P

BLOCK = 128


eps = 1e-05
highest = lax.Precision.HIGH


def combine(earlier, later):
    return (earlier[0] * later[0], later[0][:, None, None] * earlier[1] + later[1])


def pair_scan(decay, state, axis, reverse):
    count = lax.axis_size(axis)
    if count == 1:
        return jnp.zeros_like(state)
    assert count % 2 == 0 and decay.shape[0] % 2 == 0
    place = lax.axis_index(axis)
    virt = count - 1 - place if reverse else place

    def phys(u):
        return count - 1 - u if reverse else u

    half = decay.shape[0] // 2
    groups = count // 2
    side = virt % 2
    group = virt // 2
    first = side == 0
    own_start = (1 - side) * half
    send_start = side * half

    def part(x, start):
        return lax.dynamic_slice_in_dim(x, start, half, 0)

    a_own, s_own = part(decay, own_start), part(state, own_start)
    a_snd, s_snd = part(decay, send_start), part(state, send_start)
    swap = [(phys(u), phys(u ^ 1)) for u in range(count)]
    a_rcv, s_rcv = lax.ppermute((a_snd, s_snd), axis, swap)
    lead = (jnp.where(first, a_own, a_rcv), jnp.where(first, s_own, s_rcv))
    trail = (jnp.where(first, a_rcv, a_own), jnp.where(first, s_rcv, s_own))
    a_tot, s_tot = combine(lead, trail)

    def shift_pairs(k):
        return [
            (phys(2 * g + x), phys(2 * (g + k) + x)) for g in range(groups - k) for x in (0, 1)
        ]

    if groups <= 4:
        a_g = jnp.ones_like(a_tot)
        s_g = jnp.zeros_like(s_tot)
        for r in range(groups - 1):
            out = combine((a_g, s_g), (a_tot, s_tot))
            pairs = [(phys(2 * r + x), phys(2 * (r + 1) + x)) for x in (0, 1)]
            if r == groups - 2:
                s_in = lax.ppermute(out[1], axis, pairs)
                a_in = a_g
            else:
                a_in, s_in = lax.ppermute(out, axis, pairs)
            dst = group == r + 1
            a_g = jnp.where(dst, a_in, a_g)
            s_g = jnp.where(dst, s_in, s_g)
    else:
        a_g, s_g = lax.ppermute((a_tot, s_tot), axis, shift_pairs(1))
        a_g = jnp.where(group == 0, 1.0, a_g)
        s_g = jnp.where(group == 0, 0.0, s_g)
        k = 1
        while k < groups:
            got = lax.ppermute((a_g, s_g), axis, shift_pairs(k))
            a_c, s_c = combine(got, (a_g, s_g))
            a_g = jnp.where(group >= k, a_c, a_g)
            s_g = jnp.where(group >= k, s_c, s_g)
            k *= 2

    with_lead_own = a_own[:, None, None] * s_g + s_own
    with_lead_rcv = a_rcv[:, None, None] * s_g + s_rcv
    send = jnp.where(first, with_lead_own, s_g)
    keep = jnp.where(first, s_g, with_lead_rcv)
    other = lax.ppermute(send, axis, swap)
    return jnp.where(
        first, jnp.concatenate([other, keep], 0), jnp.concatenate([keep, other], 0)
    )


def butterfly_psum(parts, axis):
    count = lax.axis_size(axis)
    if count & (count - 1):
        return lax.psum(parts, axis)
    k = 1
    while k < count:
        got = lax.ppermute(parts, axis, [(i, i ^ k) for i in range(count)])
        parts = jax.tree.map(jnp.add, parts, got)
        k *= 2
    return parts


def block_step(carry_state, inputs, skip_scale):
    feat_block, step_block, decay_block, write_block, read_block = inputs
    length = decay_block.shape[1]
    cumul = jnp.cumsum(decay_block, axis=1)
    row_index = lax.broadcasted_iota(jnp.int32, (length, length), 0)
    col_index = lax.broadcasted_iota(jnp.int32, (length, length), 1)
    causal = row_index >= col_index
    gaps = jnp.where(causal[None], cumul[:, :, None] - cumul[:, None, :], 0.0)
    weights = jnp.where(causal[None], jnp.exp(gaps), 0.0)
    scores = jnp.dot(read_block, jnp.transpose(write_block), precision=highest)
    scaled = feat_block * jnp.transpose(step_block)[:, :, None]
    masked = weights * scores[None]
    within = jnp.einsum("hij,jhp->ihp", masked, scaled, precision=highest)
    carried = jnp.einsum("in,hpn->ihp", read_block, carry_state, precision=highest)
    carried = carried * jnp.transpose(jnp.exp(cumul))[:, :, None]
    output = within + carried + skip_scale[None, :, None] * feat_block
    to_end = jnp.exp(cumul[:, -1:] - cumul)
    weighted_in = scaled * jnp.transpose(to_end)[:, :, None]
    update = jnp.einsum("jhp,jn->hpn", weighted_in, write_block, precision=highest)
    new_state = jnp.exp(cumul[:, -1])[:, None, None] * carry_state + update
    return (new_state, output)


def run_mixer(
    features, step_sizes, log_decay, write_keys, read_queries, carry_state, skip_scale, block
):
    length = features.shape[0]
    head_count = step_sizes.shape[0]
    head_width = features.shape[1] // head_count
    block_total = length // block
    feat_blocks = features.reshape(block_total, block, head_count, head_width)
    step_blocks = jnp.transpose(step_sizes.reshape(head_count, block_total, block), (1, 0, 2))
    decay_blocks = jnp.transpose(log_decay.reshape(head_count, block_total, block), (1, 0, 2))
    write_blocks = write_keys.reshape(block_total, block, write_keys.shape[1])
    read_blocks = read_queries.reshape(block_total, block, read_queries.shape[1])

    def advance(carried_in, inputs):
        return block_step(carried_in, inputs, skip_scale)

    last_state, outputs = lax.scan(
        advance, carry_state, (feat_blocks, step_blocks, decay_blocks, write_blocks, read_blocks)
    )
    return (last_state, outputs.reshape(length, head_count * head_width))


def prefix_sum(decay_in):
    length = decay_in.shape[1]
    upper = (
        lax.broadcasted_iota(jnp.int32, (length, length), 0)
        <= lax.broadcasted_iota(jnp.int32, (length, length), 1)
    ).astype(decay_in.dtype)
    return jnp.dot(decay_in, upper, precision=lax.Precision.HIGHEST)


def within_part(feat_in, step_in, decay_in, writes, read_in, skip_scale):
    head_count, length = step_in.shape
    head_width = feat_in.shape[1] // head_count
    cumul = prefix_sum(decay_in)
    row_index = lax.broadcasted_iota(jnp.int32, (length, length), 0)
    col_index = lax.broadcasted_iota(jnp.int32, (length, length), 1)
    causal = row_index >= col_index
    gaps = jnp.where(causal[None], cumul[:, :, None] - cumul[:, None, :], 0.0)
    weights = jnp.where(causal[None], jnp.exp(gaps), 0.0)
    scores = jnp.dot(read_in, jnp.transpose(writes), precision=highest)
    feat3 = feat_in.reshape(length, head_count, head_width)
    scaled = feat3 * jnp.transpose(step_in)[:, :, None]
    masked = weights * scores[None]
    within = jnp.einsum("hij,jhp->ihp", masked, scaled, precision=highest)
    return (within + skip_scale[None, :, None] * feat3).reshape(length, -1)


def carried_part(decay_in, read_in, state_in):
    length = decay_in.shape[1]
    cumul = prefix_sum(decay_in)
    carried = jnp.einsum("in,hpn->ihp", read_in, state_in, precision=highest)
    carried = carried * jnp.transpose(jnp.exp(cumul))[:, :, None]
    return carried.reshape(length, -1)


def state_update(feat_in, step_in, decay_in, writes):
    head_count, length = step_in.shape
    head_width = feat_in.shape[1] // head_count
    cumul = prefix_sum(decay_in)
    scaled = feat_in.reshape(length, head_count, head_width) * jnp.transpose(step_in)[:, :, None]
    to_end = jnp.exp(cumul[:, -1:] - cumul)
    weighted_in = scaled * jnp.transpose(to_end)[:, :, None]
    return jnp.einsum("jhp,jn->hpn", weighted_in, writes, precision=highest)


def end_part(feat_in, step_in, decay_in, writes, state_in):
    total = jnp.exp(prefix_sum(decay_in)[:, -1])
    return total[:, None, None] * state_in + state_update(feat_in, step_in, decay_in, writes)


def local(
    features,
    gate_pre,
    write_keys,
    read_queries,
    step_sizes,
    log_decay,
    skip_scale,
    norm_gain,
    out_grad,
):
    head_count, length = step_sizes.shape
    head_width = features.shape[1] // head_count
    channels = features.shape[1] * lax.axis_size("head")
    cumul = prefix_sum(log_decay)
    decay_total = jnp.exp(cumul[:, -1])
    scaled = (
        features.reshape(length, head_count, head_width) * jnp.transpose(step_sizes)[:, :, None]
    )
    to_end = jnp.exp(cumul[:, -1:] - cumul)
    weighted_in = scaled * jnp.transpose(to_end)[:, :, None]
    local_state = jnp.einsum("jhp,jn->hpn", weighted_in, write_keys, precision=highest)
    state_in = pair_scan(decay_total, local_state, "seq", False)
    single = length == BLOCK
    if single:
        mixed_w, pull_w = jax.vjp(
            lambda f, s, d, w, r: within_part(f, s, d, w, r, skip_scale),
            features, step_sizes, log_decay, write_keys, read_queries,
        )
        mixed_c, pull_c = jax.vjp(
            lambda d, r: carried_part(d, r, state_in), log_decay, read_queries
        )
        mixed_w = lax.optimization_barrier(mixed_w)
        mixed_out = mixed_w + mixed_c
    else:

        def local_mixer(feat_in, step_in, decay_factors, writes, read_in):
            return run_mixer(
                feat_in, step_in, decay_factors, writes, read_in, state_in, skip_scale, BLOCK
            )

        primal, pullback = jax.vjp(
            local_mixer, features, step_sizes, log_decay, write_keys, read_queries
        )
        mixed_out = primal[1]
    sigmoid_gate = jax.nn.sigmoid(gate_pre)
    active = gate_pre * sigmoid_gate
    gated_out = mixed_out * active
    weighted = out_grad * norm_gain[None, :]
    square_sum, cross_sum = butterfly_psum(
        (jnp.sum(gated_out * gated_out, axis=1), jnp.sum(weighted * gated_out, axis=1)), "head"
    )
    inverse = lax.rsqrt(square_sum / channels + eps)
    grad_gated = (
        inverse[:, None] * weighted
        - (inverse * inverse * inverse * cross_sum / channels)[:, None] * gated_out
    )
    grad_mixed = grad_gated * active
    grad_gate = grad_gated * mixed_out * sigmoid_gate * (1.0 + gate_pre * (1.0 - sigmoid_gate))
    from_start = jnp.transpose(jnp.exp(cumul))
    weighted_grad = grad_mixed.reshape(length, head_count, head_width) * from_start[:, :, None]
    local_grad = jnp.einsum("jhp,jn->hpn", weighted_grad, read_queries, precision=highest)
    state_grad = pair_scan(decay_total, local_grad, "seq", True)
    if single:
        (gf_w, gs_w, gd_w, gw_w, gr_w), (gd_c, gr_c) = lax.optimization_barrier(
            (pull_w(grad_mixed), pull_c(grad_mixed))
        )
        grad_read = butterfly_psum(gr_w + gr_c, "head")
        _, pull_e = jax.vjp(
            lambda f, s, d, w: end_part(f, s, d, w, state_in),
            features, step_sizes, log_decay, write_keys,
        )
        gf_e, gs_e, gd_e, gw_e = pull_e(state_grad)
        grad_features = gf_w + gf_e
        grad_steps = gs_w + gs_e
        grad_decay = gd_w + gd_c + gd_e
        grad_write = butterfly_psum(gw_w + gw_e, "head")
    else:
        grad_features, grad_steps, grad_decay, grad_write, grad_read = pullback(
            (state_grad, grad_mixed)
        )
        grad_write, grad_read = butterfly_psum((grad_write, grad_read), "head")
    return (grad_features, grad_gate, grad_write, grad_read, grad_steps, grad_decay)


def solution(mesh):
    placed = (
        P("seq", "head"),
        P("seq", "head"),
        P("seq", None),
        P("seq", None),
        P("head", "seq"),
        P("head", "seq"),
        P("head"),
        P("head"),
        P("seq", "head"),
    )
    return jax.shard_map(
        local,
        mesh=mesh,
        in_specs=placed,
        out_specs=(
            P("seq", "head"),
            P("seq", "head"),
            P("seq", None),
            P("seq", None),
            P("head", "seq"),
            P("head", "seq"),
        ),
        check_vma=False,
    )
```

```python
import jax
import jax.numpy as jnp
from jax import lax
from jax.sharding import PartitionSpec as P

BLOCK = 128


eps = 1e-05
highest = lax.Precision.HIGH


def combine(earlier, later):
    return (earlier[0] * later[0], later[0][:, None, None] * earlier[1] + later[1])


def pair_scan(decay, state, axis, reverse):
    count = lax.axis_size(axis)
    if count == 1:
        return jnp.zeros_like(state)
    assert count % 2 == 0 and decay.shape[0] % 2 == 0
    place = lax.axis_index(axis)
    virt = count - 1 - place if reverse else place

    def phys(u):
        return count - 1 - u if reverse else u

    half = decay.shape[0] // 2
    groups = count // 2
    side = virt % 2
    group = virt // 2
    first = side == 0
    own_start = (1 - side) * half
    send_start = side * half

    def part(x, start):
        return lax.dynamic_slice_in_dim(x, start, half, 0)

    a_own, s_own = part(decay, own_start), part(state, own_start)
    a_snd, s_snd = part(decay, send_start), part(state, send_start)
    swap = [(phys(u), phys(u ^ 1)) for u in range(count)]
    a_rcv, s_rcv = lax.ppermute((a_snd, s_snd), axis, swap)
    lead = (jnp.where(first, a_own, a_rcv), jnp.where(first, s_own, s_rcv))
    trail = (jnp.where(first, a_rcv, a_own), jnp.where(first, s_rcv, s_own))
    a_tot, s_tot = combine(lead, trail)

    def shift_pairs(k):
        return [
            (phys(2 * g + x), phys(2 * (g + k) + x)) for g in range(groups - k) for x in (0, 1)
        ]

    if groups <= 4:
        a_g = jnp.ones_like(a_tot)
        s_g = jnp.zeros_like(s_tot)
        for r in range(groups - 1):
            out = combine((a_g, s_g), (a_tot, s_tot))
            pairs = [(phys(2 * r + x), phys(2 * (r + 1) + x)) for x in (0, 1)]
            if r == groups - 2:
                s_in = lax.ppermute(out[1], axis, pairs)
                a_in = a_g
            else:
                a_in, s_in = lax.ppermute(out, axis, pairs)
            dst = group == r + 1
            a_g = jnp.where(dst, a_in, a_g)
            s_g = jnp.where(dst, s_in, s_g)
    else:
        a_g, s_g = lax.ppermute((a_tot, s_tot), axis, shift_pairs(1))
        a_g = jnp.where(group == 0, 1.0, a_g)
        s_g = jnp.where(group == 0, 0.0, s_g)
        k = 1
        while k < groups:
            got = lax.ppermute((a_g, s_g), axis, shift_pairs(k))
            a_c, s_c = combine(got, (a_g, s_g))
            a_g = jnp.where(group >= k, a_c, a_g)
            s_g = jnp.where(group >= k, s_c, s_g)
            k *= 2

    with_lead_own = a_own[:, None, None] * s_g + s_own
    with_lead_rcv = a_rcv[:, None, None] * s_g + s_rcv
    send = jnp.where(first, with_lead_own, s_g)
    keep = jnp.where(first, s_g, with_lead_rcv)
    other = lax.ppermute(send, axis, swap)
    return jnp.where(
        first, jnp.concatenate([other, keep], 0), jnp.concatenate([keep, other], 0)
    )


def butterfly_psum(parts, axis):
    count = lax.axis_size(axis)
    if count & (count - 1):
        return lax.psum(parts, axis)
    k = 1
    while k < count:
        got = lax.ppermute(parts, axis, [(i, i ^ k) for i in range(count)])
        parts = jax.tree.map(jnp.add, parts, got)
        k *= 2
    return parts


def block_step(carry_state, inputs, skip_scale):
    feat_block, step_block, decay_block, write_block, read_block = inputs
    length = decay_block.shape[1]
    cumul = jnp.cumsum(decay_block, axis=1)
    row_index = lax.broadcasted_iota(jnp.int32, (length, length), 0)
    col_index = lax.broadcasted_iota(jnp.int32, (length, length), 1)
    causal = row_index >= col_index
    gaps = jnp.where(causal[None], cumul[:, :, None] - cumul[:, None, :], 0.0)
    weights = jnp.where(causal[None], jnp.exp(gaps), 0.0)
    scores = jnp.dot(read_block, jnp.transpose(write_block), precision=highest)
    scaled = feat_block * jnp.transpose(step_block)[:, :, None]
    masked = weights * scores[None]
    within = jnp.einsum("hij,jhp->ihp", masked, scaled, precision=highest)
    carried = jnp.einsum("in,hpn->ihp", read_block, carry_state, precision=highest)
    carried = carried * jnp.transpose(jnp.exp(cumul))[:, :, None]
    output = within + carried + skip_scale[None, :, None] * feat_block
    to_end = jnp.exp(cumul[:, -1:] - cumul)
    weighted_in = scaled * jnp.transpose(to_end)[:, :, None]
    update = jnp.einsum("jhp,jn->hpn", weighted_in, write_block, precision=highest)
    new_state = jnp.exp(cumul[:, -1])[:, None, None] * carry_state + update
    return (new_state, output)


def run_mixer(
    features, step_sizes, log_decay, write_keys, read_queries, carry_state, skip_scale, block
):
    length = features.shape[0]
    head_count = step_sizes.shape[0]
    head_width = features.shape[1] // head_count
    block_total = length // block
    feat_blocks = features.reshape(block_total, block, head_count, head_width)
    step_blocks = jnp.transpose(step_sizes.reshape(head_count, block_total, block), (1, 0, 2))
    decay_blocks = jnp.transpose(log_decay.reshape(head_count, block_total, block), (1, 0, 2))
    write_blocks = write_keys.reshape(block_total, block, write_keys.shape[1])
    read_blocks = read_queries.reshape(block_total, block, read_queries.shape[1])

    def advance(carried_in, inputs):
        return block_step(carried_in, inputs, skip_scale)

    last_state, outputs = lax.scan(
        advance, carry_state, (feat_blocks, step_blocks, decay_blocks, write_blocks, read_blocks)
    )
    return (last_state, outputs.reshape(length, head_count * head_width))


def prefix_sum(decay_in):
    length = decay_in.shape[1]
    upper = (
        lax.broadcasted_iota(jnp.int32, (length, length), 0)
        <= lax.broadcasted_iota(jnp.int32, (length, length), 1)
    ).astype(decay_in.dtype)
    return jnp.dot(decay_in, upper, precision=lax.Precision.HIGHEST)


def within_part(feat_in, step_in, decay_in, writes, read_in, skip_scale):
    head_count, length = step_in.shape
    head_width = feat_in.shape[1] // head_count
    cumul = prefix_sum(decay_in)
    row_index = lax.broadcasted_iota(jnp.int32, (length, length), 0)
    col_index = lax.broadcasted_iota(jnp.int32, (length, length), 1)
    causal = row_index >= col_index
    gaps = jnp.where(causal[None], cumul[:, :, None] - cumul[:, None, :], 0.0)
    weights = jnp.where(causal[None], jnp.exp(gaps), 0.0)
    scores = jnp.dot(read_in, jnp.transpose(writes), precision=highest)
    feat3 = feat_in.reshape(length, head_count, head_width)
    scaled = feat3 * jnp.transpose(step_in)[:, :, None]
    masked = weights * scores[None]
    within = jnp.einsum("hij,jhp->ihp", masked, scaled, precision=highest)
    return (within + skip_scale[None, :, None] * feat3).reshape(length, -1)


def carried_part(decay_in, read_in, state_in):
    length = decay_in.shape[1]
    cumul = prefix_sum(decay_in)
    carried = jnp.einsum("in,hpn->ihp", read_in, state_in, precision=highest)
    carried = carried * jnp.transpose(jnp.exp(cumul))[:, :, None]
    return carried.reshape(length, -1)


def state_update(feat_in, step_in, decay_in, writes):
    head_count, length = step_in.shape
    head_width = feat_in.shape[1] // head_count
    cumul = prefix_sum(decay_in)
    scaled = feat_in.reshape(length, head_count, head_width) * jnp.transpose(step_in)[:, :, None]
    to_end = jnp.exp(cumul[:, -1:] - cumul)
    weighted_in = scaled * jnp.transpose(to_end)[:, :, None]
    return jnp.einsum("jhp,jn->hpn", weighted_in, writes, precision=highest)


def end_part(feat_in, step_in, decay_in, writes, state_in):
    total = jnp.exp(prefix_sum(decay_in)[:, -1])
    return total[:, None, None] * state_in + state_update(feat_in, step_in, decay_in, writes)


def local(
    features,
    gate_pre,
    write_keys,
    read_queries,
    step_sizes,
    log_decay,
    skip_scale,
    norm_gain,
    out_grad,
):
    head_count, length = step_sizes.shape
    head_width = features.shape[1] // head_count
    channels = features.shape[1] * lax.axis_size("head")
    cumul = prefix_sum(log_decay)
    decay_total = jnp.exp(cumul[:, -1])
    scaled = (
        features.reshape(length, head_count, head_width) * jnp.transpose(step_sizes)[:, :, None]
    )
    to_end = jnp.exp(cumul[:, -1:] - cumul)
    weighted_in = scaled * jnp.transpose(to_end)[:, :, None]
    local_state = jnp.einsum("jhp,jn->hpn", weighted_in, write_keys, precision=highest)
    state_in = pair_scan(decay_total, local_state, "seq", False)
    single = length == BLOCK
    if single:
        mixed_w, pull_w = jax.vjp(
            lambda f, s, d, w, r: within_part(f, s, d, w, r, skip_scale),
            features, step_sizes, log_decay, write_keys, read_queries,
        )
        mixed_c, pull_c = jax.vjp(
            lambda d, r: carried_part(d, r, state_in), log_decay, read_queries
        )
        mixed_w = lax.optimization_barrier(mixed_w)
        mixed_out = mixed_w + mixed_c
    else:

        def local_mixer(feat_in, step_in, decay_factors, writes, read_in):
            return run_mixer(
                feat_in, step_in, decay_factors, writes, read_in, state_in, skip_scale, BLOCK
            )

        primal, pullback = jax.vjp(
            local_mixer, features, step_sizes, log_decay, write_keys, read_queries
        )
        mixed_out = primal[1]
    sigmoid_gate = jax.nn.sigmoid(gate_pre)
    active = gate_pre * sigmoid_gate
    gated_out = mixed_out * active
    weighted = out_grad * norm_gain[None, :]
    square_sum, cross_sum = butterfly_psum(
        jnp.stack([jnp.sum(gated_out * gated_out, axis=1), jnp.sum(weighted * gated_out, axis=1)]),
        "head",
    )
    inverse = lax.rsqrt(square_sum / channels + eps)
    grad_gated = (
        inverse[:, None] * weighted
        - (inverse * inverse * inverse * cross_sum / channels)[:, None] * gated_out
    )
    grad_mixed = grad_gated * active
    grad_gate = grad_gated * mixed_out * sigmoid_gate * (1.0 + gate_pre * (1.0 - sigmoid_gate))
    from_start = jnp.transpose(jnp.exp(cumul))
    weighted_grad = grad_mixed.reshape(length, head_count, head_width) * from_start[:, :, None]
    local_grad = jnp.einsum("jhp,jn->hpn", weighted_grad, read_queries, precision=highest)
    state_grad = pair_scan(decay_total, local_grad, "seq", True)
    if single:
        gf_w, gs_w, gd_w, gw_w, gr_w = pull_w(grad_mixed)
        gd_c, gr_c = pull_c(grad_mixed)
        grad_read = butterfly_psum(gr_w + gr_c, "head")
        _, pull_e = jax.vjp(
            lambda f, s, d, w: end_part(f, s, d, w, state_in),
            features, step_sizes, log_decay, write_keys,
        )
        gf_e, gs_e, gd_e, gw_e = pull_e(state_grad)
        grad_features = gf_w + gf_e
        grad_steps = gs_w + gs_e
        grad_decay = gd_w + gd_c + gd_e
        grad_write = butterfly_psum(gw_w + gw_e, "head")
    else:
        grad_features, grad_steps, grad_decay, grad_write, grad_read = pullback(
            (state_grad, grad_mixed)
        )
        grad_write, grad_read = butterfly_psum((grad_write, grad_read), "head")
    return (grad_features, grad_gate, grad_write, grad_read, grad_steps, grad_decay)


def solution(mesh):
    placed = (
        P("seq", "head"),
        P("seq", "head"),
        P("seq", None),
        P("seq", None),
        P("head", "seq"),
        P("head", "seq"),
        P("head"),
        P("head"),
        P("seq", "head"),
    )
    return jax.shard_map(
        local,
        mesh=mesh,
        in_specs=placed,
        out_specs=(
            P("seq", "head"),
            P("seq", "head"),
            P("seq", None),
            P("seq", None),
            P("head", "seq"),
            P("head", "seq"),
        ),
        check_vma=False,
    )
```

```python
import jax
import jax.numpy as jnp
from jax import lax
from jax.sharding import PartitionSpec as P

BLOCK = 128


eps = 1e-05
highest = lax.Precision.HIGH


def combine(earlier, later):
    return (earlier[0] * later[0], later[0][:, None, None] * earlier[1] + later[1])


def pair_scan(decay, state_of, axis, reverse):
    count = lax.axis_size(axis)
    if count == 1:
        return jnp.zeros_like(state_of(0, decay.shape[0]))
    assert count % 2 == 0 and decay.shape[0] % 2 == 0
    place = lax.axis_index(axis)
    virt = count - 1 - place if reverse else place

    def phys(u):
        return count - 1 - u if reverse else u

    half = decay.shape[0] // 2
    groups = count // 2
    side = virt % 2
    group = virt // 2
    first = side == 0
    own_start = (1 - side) * half
    send_start = side * half

    def part(x, start):
        return lax.dynamic_slice_in_dim(x, start, half, 0)

    a_snd, s_snd = part(decay, send_start), state_of(send_start, half)
    row = jnp.broadcast_to(a_snd[:, None, None], (half, 1, s_snd.shape[2]))
    swap = [(phys(u), phys(u ^ 1)) for u in range(count)]
    got = lax.ppermute(jnp.concatenate([s_snd, row], 1), axis, swap)
    s_rcv, a_rcv = got[:, : s_snd.shape[1]], got[:, s_snd.shape[1], 0]
    a_own, s_own = part(decay, own_start), state_of(own_start, half)
    lead = (jnp.where(first, a_own, a_rcv), jnp.where(first, s_own, s_rcv))
    trail = (jnp.where(first, a_rcv, a_own), jnp.where(first, s_rcv, s_own))
    a_tot, s_tot = combine(lead, trail)

    def shift_pairs(k):
        return [
            (phys(2 * g + x), phys(2 * (g + k) + x)) for g in range(groups - k) for x in (0, 1)
        ]

    if groups <= 4:
        a_g = jnp.ones_like(a_tot)
        s_g = jnp.zeros_like(s_tot)
        for r in range(groups - 1):
            out = combine((a_g, s_g), (a_tot, s_tot))
            pairs = [(phys(2 * r + x), phys(2 * (r + 1) + x)) for x in (0, 1)]
            if r == groups - 2:
                s_in = lax.ppermute(out[1], axis, pairs)
                a_in = a_g
            else:
                a_in, s_in = lax.ppermute(out, axis, pairs)
            dst = group == r + 1
            a_g = jnp.where(dst, a_in, a_g)
            s_g = jnp.where(dst, s_in, s_g)
    else:
        a_g, s_g = lax.ppermute((a_tot, s_tot), axis, shift_pairs(1))
        a_g = jnp.where(group == 0, 1.0, a_g)
        s_g = jnp.where(group == 0, 0.0, s_g)
        k = 1
        while k < groups:
            got = lax.ppermute((a_g, s_g), axis, shift_pairs(k))
            a_c, s_c = combine(got, (a_g, s_g))
            a_g = jnp.where(group >= k, a_c, a_g)
            s_g = jnp.where(group >= k, s_c, s_g)
            k *= 2

    with_lead_own = a_own[:, None, None] * s_g + s_own
    with_lead_rcv = a_rcv[:, None, None] * s_g + s_rcv
    send = jnp.where(first, with_lead_own, s_g)
    keep = jnp.where(first, s_g, with_lead_rcv)
    other = lax.ppermute(send, axis, swap)
    return jnp.where(
        first, jnp.concatenate([other, keep], 0), jnp.concatenate([keep, other], 0)
    )


def butterfly_psum(parts, axis):
    count = lax.axis_size(axis)
    if count & (count - 1):
        return lax.psum(parts, axis)
    k = 1
    while k < count:
        got = lax.ppermute(parts, axis, [(i, i ^ k) for i in range(count)])
        parts = jax.tree.map(jnp.add, parts, got)
        k *= 2
    return parts


def block_step(carry_state, inputs, skip_scale):
    feat_block, step_block, decay_block, write_block, read_block = inputs
    length = decay_block.shape[1]
    cumul = jnp.cumsum(decay_block, axis=1)
    row_index = lax.broadcasted_iota(jnp.int32, (length, length), 0)
    col_index = lax.broadcasted_iota(jnp.int32, (length, length), 1)
    causal = row_index >= col_index
    gaps = jnp.where(causal[None], cumul[:, :, None] - cumul[:, None, :], 0.0)
    weights = jnp.where(causal[None], jnp.exp(gaps), 0.0)
    scores = jnp.dot(read_block, jnp.transpose(write_block), precision=highest)
    scaled = feat_block * jnp.transpose(step_block)[:, :, None]
    masked = weights * scores[None]
    within = jnp.einsum("hij,jhp->ihp", masked, scaled, precision=highest)
    carried = jnp.einsum("in,hpn->ihp", read_block, carry_state, precision=highest)
    carried = carried * jnp.transpose(jnp.exp(cumul))[:, :, None]
    output = within + carried + skip_scale[None, :, None] * feat_block
    to_end = jnp.exp(cumul[:, -1:] - cumul)
    weighted_in = scaled * jnp.transpose(to_end)[:, :, None]
    update = jnp.einsum("jhp,jn->hpn", weighted_in, write_block, precision=highest)
    new_state = jnp.exp(cumul[:, -1])[:, None, None] * carry_state + update
    return (new_state, output)


def run_mixer(
    features, step_sizes, log_decay, write_keys, read_queries, carry_state, skip_scale, block
):
    length = features.shape[0]
    head_count = step_sizes.shape[0]
    head_width = features.shape[1] // head_count
    block_total = length // block
    feat_blocks = features.reshape(block_total, block, head_count, head_width)
    step_blocks = jnp.transpose(step_sizes.reshape(head_count, block_total, block), (1, 0, 2))
    decay_blocks = jnp.transpose(log_decay.reshape(head_count, block_total, block), (1, 0, 2))
    write_blocks = write_keys.reshape(block_total, block, write_keys.shape[1])
    read_blocks = read_queries.reshape(block_total, block, read_queries.shape[1])

    def advance(carried_in, inputs):
        return block_step(carried_in, inputs, skip_scale)

    last_state, outputs = lax.scan(
        advance, carry_state, (feat_blocks, step_blocks, decay_blocks, write_blocks, read_blocks)
    )
    return (last_state, outputs.reshape(length, head_count * head_width))


def prefix_sum(decay_in):
    length = decay_in.shape[1]
    upper = (
        lax.broadcasted_iota(jnp.int32, (length, length), 0)
        <= lax.broadcasted_iota(jnp.int32, (length, length), 1)
    ).astype(decay_in.dtype)
    return jnp.dot(decay_in, upper, precision=lax.Precision.HIGHEST)


def within_part(feat_in, step_in, decay_in, writes, read_in, skip_scale):
    head_count, length = step_in.shape
    head_width = feat_in.shape[1] // head_count
    cumul = prefix_sum(decay_in)
    row_index = lax.broadcasted_iota(jnp.int32, (length, length), 0)
    col_index = lax.broadcasted_iota(jnp.int32, (length, length), 1)
    causal = row_index >= col_index
    gaps = jnp.where(causal[None], cumul[:, :, None] - cumul[:, None, :], 0.0)
    weights = jnp.where(causal[None], jnp.exp(gaps), 0.0)
    scores = jnp.dot(read_in, jnp.transpose(writes), precision=highest)
    feat3 = feat_in.reshape(length, head_count, head_width)
    scaled = feat3 * jnp.transpose(step_in)[:, :, None]
    masked = weights * scores[None]
    within = jnp.einsum("hij,jhp->ihp", masked, scaled, precision=highest)
    return (within + skip_scale[None, :, None] * feat3).reshape(length, -1)


def carried_part(decay_in, read_in, state_in):
    length = decay_in.shape[1]
    cumul = prefix_sum(decay_in)
    carried = jnp.einsum("in,hpn->ihp", read_in, state_in, precision=highest)
    carried = carried * jnp.transpose(jnp.exp(cumul))[:, :, None]
    return carried.reshape(length, -1)


def state_update(feat_in, step_in, decay_in, writes):
    head_count, length = step_in.shape
    head_width = feat_in.shape[1] // head_count
    cumul = prefix_sum(decay_in)
    scaled = feat_in.reshape(length, head_count, head_width) * jnp.transpose(step_in)[:, :, None]
    to_end = jnp.exp(cumul[:, -1:] - cumul)
    weighted_in = scaled * jnp.transpose(to_end)[:, :, None]
    return jnp.einsum("jhp,jn->hpn", weighted_in, writes, precision=highest)


def end_part(feat_in, step_in, decay_in, writes, state_in):
    total = jnp.exp(prefix_sum(decay_in)[:, -1])
    return total[:, None, None] * state_in + state_update(feat_in, step_in, decay_in, writes)


def local(
    features,
    gate_pre,
    write_keys,
    read_queries,
    step_sizes,
    log_decay,
    skip_scale,
    norm_gain,
    out_grad,
):
    head_count, length = step_sizes.shape
    head_width = features.shape[1] // head_count
    channels = features.shape[1] * lax.axis_size("head")
    cumul = prefix_sum(log_decay)
    decay_total = jnp.exp(cumul[:, -1])
    scaled = (
        features.reshape(length, head_count, head_width) * jnp.transpose(step_sizes)[:, :, None]
    )
    to_end = jnp.exp(cumul[:, -1:] - cumul)
    weighted_in = scaled * jnp.transpose(to_end)[:, :, None]

    def local_state(start, size):
        part = lax.dynamic_slice_in_dim(weighted_in, start, size, 1)
        return jnp.einsum("jhp,jn->hpn", part, write_keys, precision=highest)

    state_in = pair_scan(decay_total, local_state, "seq", False)
    single = length == BLOCK
    if single:
        mixed_w, pull_w = jax.vjp(
            lambda f, s, d, w, r: within_part(f, s, d, w, r, skip_scale),
            features, step_sizes, log_decay, write_keys, read_queries,
        )
        mixed_c, pull_c = jax.vjp(
            lambda d, r: carried_part(d, r, state_in), log_decay, read_queries
        )
        mixed_w = lax.optimization_barrier(mixed_w)
        mixed_out = mixed_w + mixed_c
    else:

        def local_mixer(feat_in, step_in, decay_factors, writes, read_in):
            return run_mixer(
                feat_in, step_in, decay_factors, writes, read_in, state_in, skip_scale, BLOCK
            )

        primal, pullback = jax.vjp(
            local_mixer, features, step_sizes, log_decay, write_keys, read_queries
        )
        mixed_out = primal[1]
    sigmoid_gate = jax.nn.sigmoid(gate_pre)
    active = gate_pre * sigmoid_gate
    gated_out = mixed_out * active
    weighted = out_grad * norm_gain[None, :]
    square_sum, cross_sum = butterfly_psum(
        jnp.stack([jnp.sum(gated_out * gated_out, axis=1), jnp.sum(weighted * gated_out, axis=1)]),
        "head",
    )
    inverse = lax.rsqrt(square_sum / channels + eps)
    grad_gated = (
        inverse[:, None] * weighted
        - (inverse * inverse * inverse * cross_sum / channels)[:, None] * gated_out
    )
    grad_mixed = grad_gated * active
    grad_gate = grad_gated * mixed_out * sigmoid_gate * (1.0 + gate_pre * (1.0 - sigmoid_gate))
    from_start = jnp.transpose(jnp.exp(cumul))
    weighted_grad = grad_mixed.reshape(length, head_count, head_width) * from_start[:, :, None]

    def local_grad(start, size):
        part = lax.dynamic_slice_in_dim(weighted_grad, start, size, 1)
        return jnp.einsum("jhp,jn->hpn", part, read_queries, precision=highest)

    state_grad = pair_scan(decay_total, local_grad, "seq", True)
    if single:
        gf_w, gs_w, gd_w, gw_w, gr_w = pull_w(grad_mixed)
        gd_c, gr_c = pull_c(grad_mixed)
        grad_read = butterfly_psum(gr_w + gr_c, "head")
        _, pull_e = jax.vjp(
            lambda f, s, d, w: end_part(f, s, d, w, state_in),
            features, step_sizes, log_decay, write_keys,
        )
        gf_e, gs_e, gd_e, gw_e = pull_e(state_grad)
        grad_features = gf_w + gf_e
        grad_steps = gs_w + gs_e
        grad_decay = gd_w + gd_c + gd_e
        grad_write = butterfly_psum(gw_w + gw_e, "head")
    else:
        grad_features, grad_steps, grad_decay, grad_write, grad_read = pullback(
            (state_grad, grad_mixed)
        )
        grad_write, grad_read = butterfly_psum((grad_write, grad_read), "head")
    return (grad_features, grad_gate, grad_write, grad_read, grad_steps, grad_decay)


def solution(mesh):
    placed = (
        P("seq", "head"),
        P("seq", "head"),
        P("seq", None),
        P("seq", None),
        P("head", "seq"),
        P("head", "seq"),
        P("head"),
        P("head"),
        P("seq", "head"),
    )
    return jax.shard_map(
        local,
        mesh=mesh,
        in_specs=placed,
        out_specs=(
            P("seq", "head"),
            P("seq", "head"),
            P("seq", None),
            P("seq", None),
            P("head", "seq"),
            P("head", "seq"),
        ),
        check_vma=False,
    )
```

```python
import jax
import jax.numpy as jnp
from jax import lax
from jax.sharding import PartitionSpec as P

BLOCK = 128


eps = 1e-05
highest = lax.Precision.HIGH


def combine(earlier, later):
    return (earlier[0] * later[0], later[0][:, None, None] * earlier[1] + later[1])


def pair_scan(decay, state, axis, reverse):
    count = lax.axis_size(axis)
    if count == 1:
        return jnp.zeros_like(state)
    assert count % 2 == 0 and decay.shape[0] % 2 == 0
    place = lax.axis_index(axis)
    virt = count - 1 - place if reverse else place

    def phys(u):
        return count - 1 - u if reverse else u

    half = decay.shape[0] // 2
    groups = count // 2
    side = virt % 2
    group = virt // 2
    first = side == 0
    own_start = (1 - side) * half
    send_start = side * half

    def part(x, start):
        return lax.dynamic_slice_in_dim(x, start, half, 0)

    a_own, s_own = part(decay, own_start), part(state, own_start)
    a_snd, s_snd = part(decay, send_start), part(state, send_start)
    swap = [(phys(u), phys(u ^ 1)) for u in range(count)]
    a_rcv, s_rcv = lax.ppermute((a_snd, s_snd), axis, swap)
    lead = (jnp.where(first, a_own, a_rcv), jnp.where(first, s_own, s_rcv))
    trail = (jnp.where(first, a_rcv, a_own), jnp.where(first, s_rcv, s_own))
    a_tot, s_tot = combine(lead, trail)

    def shift_pairs(k):
        return [
            (phys(2 * g + x), phys(2 * (g + k) + x)) for g in range(groups - k) for x in (0, 1)
        ]

    if groups <= 4:
        a_g = jnp.ones_like(a_tot)
        s_g = jnp.zeros_like(s_tot)
        for r in range(groups - 1):
            out = combine((a_g, s_g), (a_tot, s_tot))
            pairs = [(phys(2 * r + x), phys(2 * (r + 1) + x)) for x in (0, 1)]
            if r == groups - 2:
                s_in = lax.ppermute(out[1], axis, pairs)
                a_in = a_g
            else:
                a_in, s_in = lax.ppermute(out, axis, pairs)
            dst = group == r + 1
            a_g = jnp.where(dst, a_in, a_g)
            s_g = jnp.where(dst, s_in, s_g)
    else:
        a_g, s_g = lax.ppermute((a_tot, s_tot), axis, shift_pairs(1))
        a_g = jnp.where(group == 0, 1.0, a_g)
        s_g = jnp.where(group == 0, 0.0, s_g)
        k = 1
        while k < groups:
            got = lax.ppermute((a_g, s_g), axis, shift_pairs(k))
            a_c, s_c = combine(got, (a_g, s_g))
            a_g = jnp.where(group >= k, a_c, a_g)
            s_g = jnp.where(group >= k, s_c, s_g)
            k *= 2

    with_lead_own = a_own[:, None, None] * s_g + s_own
    with_lead_rcv = a_rcv[:, None, None] * s_g + s_rcv
    send = jnp.where(first, with_lead_own, s_g)
    keep = jnp.where(first, s_g, with_lead_rcv)
    other = lax.ppermute(send, axis, swap)
    return jnp.where(
        first, jnp.concatenate([other, keep], 0), jnp.concatenate([keep, other], 0)
    )


def butterfly_psum(parts, axis):
    count = lax.axis_size(axis)
    if count & (count - 1):
        return lax.psum(parts, axis)
    k = 1
    while k < count:
        got = lax.ppermute(parts, axis, [(i, i ^ k) for i in range(count)])
        parts = jax.tree.map(jnp.add, parts, got)
        k *= 2
    return parts


def block_step(carry_state, inputs, skip_scale):
    feat_block, step_block, decay_block, write_block, read_block = inputs
    length = decay_block.shape[1]
    cumul = jnp.cumsum(decay_block, axis=1)
    row_index = lax.broadcasted_iota(jnp.int32, (length, length), 0)
    col_index = lax.broadcasted_iota(jnp.int32, (length, length), 1)
    causal = row_index >= col_index
    gaps = jnp.where(causal[None], cumul[:, :, None] - cumul[:, None, :], 0.0)
    weights = jnp.where(causal[None], jnp.exp(gaps), 0.0)
    scores = jnp.dot(read_block, jnp.transpose(write_block), precision=highest)
    scaled = feat_block * jnp.transpose(step_block)[:, :, None]
    masked = weights * scores[None]
    within = jnp.einsum("hij,jhp->ihp", masked, scaled, precision=highest)
    carried = jnp.einsum("in,hpn->ihp", read_block, carry_state, precision=highest)
    carried = carried * jnp.transpose(jnp.exp(cumul))[:, :, None]
    output = within + carried + skip_scale[None, :, None] * feat_block
    to_end = jnp.exp(cumul[:, -1:] - cumul)
    weighted_in = scaled * jnp.transpose(to_end)[:, :, None]
    update = jnp.einsum("jhp,jn->hpn", weighted_in, write_block, precision=highest)
    new_state = jnp.exp(cumul[:, -1])[:, None, None] * carry_state + update
    return (new_state, output)


def run_mixer(
    features, step_sizes, log_decay, write_keys, read_queries, carry_state, skip_scale, block
):
    length = features.shape[0]
    head_count = step_sizes.shape[0]
    head_width = features.shape[1] // head_count
    block_total = length // block
    feat_blocks = features.reshape(block_total, block, head_count, head_width)
    step_blocks = jnp.transpose(step_sizes.reshape(head_count, block_total, block), (1, 0, 2))
    decay_blocks = jnp.transpose(log_decay.reshape(head_count, block_total, block), (1, 0, 2))
    write_blocks = write_keys.reshape(block_total, block, write_keys.shape[1])
    read_blocks = read_queries.reshape(block_total, block, read_queries.shape[1])

    def advance(carried_in, inputs):
        return block_step(carried_in, inputs, skip_scale)

    last_state, outputs = lax.scan(
        advance, carry_state, (feat_blocks, step_blocks, decay_blocks, write_blocks, read_blocks)
    )
    return (last_state, outputs.reshape(length, head_count * head_width))


def prefix_sum(decay_in):
    length = decay_in.shape[1]
    upper = (
        lax.broadcasted_iota(jnp.int32, (length, length), 0)
        <= lax.broadcasted_iota(jnp.int32, (length, length), 1)
    ).astype(decay_in.dtype)
    return jnp.dot(decay_in, upper, precision=lax.Precision.HIGHEST)


def within_part(feat_in, step_in, decay_in, writes, read_in, skip_scale):
    head_count, length = step_in.shape
    head_width = feat_in.shape[1] // head_count
    cumul = prefix_sum(decay_in)
    row_index = lax.broadcasted_iota(jnp.int32, (length, length), 0)
    col_index = lax.broadcasted_iota(jnp.int32, (length, length), 1)
    causal = row_index >= col_index
    gaps = jnp.where(causal[None], cumul[:, :, None] - cumul[:, None, :], 0.0)
    weights = jnp.where(causal[None], jnp.exp(gaps), 0.0)
    scores = jnp.dot(read_in, jnp.transpose(writes), precision=highest)
    feat3 = feat_in.reshape(length, head_count, head_width)
    scaled = feat3 * jnp.transpose(step_in)[:, :, None]
    masked = weights * scores[None]
    within = jnp.einsum("hij,jhp->ihp", masked, scaled, precision=highest)
    return (within + skip_scale[None, :, None] * feat3).reshape(length, -1)


def carried_part(decay_in, read_in, state_in):
    length = decay_in.shape[1]
    cumul = prefix_sum(decay_in)
    carried = jnp.einsum("in,hpn->ihp", read_in, state_in, precision=highest)
    carried = carried * jnp.transpose(jnp.exp(cumul))[:, :, None]
    return carried.reshape(length, -1)


def state_update(feat_in, step_in, decay_in, writes):
    head_count, length = step_in.shape
    head_width = feat_in.shape[1] // head_count
    cumul = prefix_sum(decay_in)
    scaled = feat_in.reshape(length, head_count, head_width) * jnp.transpose(step_in)[:, :, None]
    to_end = jnp.exp(cumul[:, -1:] - cumul)
    weighted_in = scaled * jnp.transpose(to_end)[:, :, None]
    return jnp.einsum("jhp,jn->hpn", weighted_in, writes, precision=highest)


def end_part(feat_in, step_in, decay_in, writes, state_in):
    total = jnp.exp(prefix_sum(decay_in)[:, -1])
    return total[:, None, None] * state_in + state_update(feat_in, step_in, decay_in, writes)


def local(
    features,
    gate_pre,
    write_keys,
    read_queries,
    step_sizes,
    log_decay,
    skip_scale,
    norm_gain,
    out_grad,
):
    head_count, length = step_sizes.shape
    head_width = features.shape[1] // head_count
    channels = features.shape[1] * lax.axis_size("head")
    cumul = prefix_sum(log_decay)
    decay_total = jnp.exp(cumul[:, -1])
    scaled = (
        features.reshape(length, head_count, head_width) * jnp.transpose(step_sizes)[:, :, None]
    )
    to_end = jnp.exp(cumul[:, -1:] - cumul)
    weighted_in = scaled * jnp.transpose(to_end)[:, :, None]
    local_state = jnp.einsum("jhp,jn->hpn", weighted_in, write_keys, precision=highest)
    state_in = pair_scan(decay_total, local_state, "seq", False)
    single = length == BLOCK
    if single:
        mixed_w, pull_w = jax.vjp(
            lambda f, s, d, w, r: within_part(f, s, d, w, r, skip_scale),
            features, step_sizes, log_decay, write_keys, read_queries,
        )
        mixed_c, pull_c = jax.vjp(
            lambda d, r: carried_part(d, r, state_in), log_decay, read_queries
        )
        mixed_w = lax.optimization_barrier(mixed_w)
        mixed_out = mixed_w + mixed_c
    else:

        def local_mixer(feat_in, step_in, decay_factors, writes, read_in):
            return run_mixer(
                feat_in, step_in, decay_factors, writes, read_in, state_in, skip_scale, BLOCK
            )

        primal, pullback = jax.vjp(
            local_mixer, features, step_sizes, log_decay, write_keys, read_queries
        )
        mixed_out = primal[1]
    sigmoid_gate = jax.nn.sigmoid(gate_pre)
    active = gate_pre * sigmoid_gate
    gated_out = mixed_out * active
    weighted = out_grad * norm_gain[None, :]
    square_sum, cross_sum = butterfly_psum(
        jnp.stack([jnp.sum(gated_out * gated_out, axis=1), jnp.sum(weighted * gated_out, axis=1)]),
        "head",
    )
    inverse = lax.rsqrt(square_sum / channels + eps)
    grad_gated = (
        inverse[:, None] * weighted
        - (inverse * inverse * inverse * cross_sum / channels)[:, None] * gated_out
    )
    grad_mixed = grad_gated * active
    grad_gate = grad_gated * mixed_out * sigmoid_gate * (1.0 + gate_pre * (1.0 - sigmoid_gate))
    from_start = jnp.transpose(jnp.exp(cumul))
    weighted_grad = grad_mixed.reshape(length, head_count, head_width) * from_start[:, :, None]
    local_grad = jnp.einsum("jhp,jn->hpn", weighted_grad, read_queries, precision=highest)
    state_grad = pair_scan(decay_total, local_grad, "seq", True)
    if single:
        gf_w, gs_w, gd_w, gw_w, gr_w = pull_w(grad_mixed)
        gd_c, gr_c = pull_c(grad_mixed)
        grad_read = butterfly_psum(gr_w + gr_c, "head")
        gw_e = jnp.dot(
            weighted_in.reshape(length, -1),
            state_grad.reshape(-1, state_grad.shape[2]),
            precision=highest,
        )
        write_part = gw_w + gw_e
        grad_write = butterfly_psum(write_part, "head")
        state_grad, write_part = lax.optimization_barrier((state_grad, write_part))
        _, pull_e = jax.vjp(
            lambda f, s, d: end_part(f, s, d, write_keys, state_in),
            features, step_sizes, log_decay,
        )
        gf_e, gs_e, gd_e = pull_e(state_grad)
        grad_features = gf_w + gf_e
        grad_steps = gs_w + gs_e
        grad_decay = gd_w + gd_c + gd_e
    else:
        grad_features, grad_steps, grad_decay, grad_write, grad_read = pullback(
            (state_grad, grad_mixed)
        )
        grad_write, grad_read = butterfly_psum((grad_write, grad_read), "head")
    return (grad_features, grad_gate, grad_write, grad_read, grad_steps, grad_decay)


def solution(mesh):
    placed = (
        P("seq", "head"),
        P("seq", "head"),
        P("seq", None),
        P("seq", None),
        P("head", "seq"),
        P("head", "seq"),
        P("head"),
        P("head"),
        P("seq", "head"),
    )
    return jax.shard_map(
        local,
        mesh=mesh,
        in_specs=placed,
        out_specs=(
            P("seq", "head"),
            P("seq", "head"),
            P("seq", None),
            P("seq", None),
            P("head", "seq"),
            P("head", "seq"),
        ),
        check_vma=False,
    )
```

```python
import jax
import jax.numpy as jnp
from jax import lax
from jax.sharding import PartitionSpec as P

BLOCK = 128


eps = 1e-05
highest = lax.Precision.HIGH


def combine(earlier, later):
    return (earlier[0] * later[0], later[0][:, None, None] * earlier[1] + later[1])


def pair_scan(decay, state, axis, reverse, split=False):
    count = lax.axis_size(axis)
    if count == 1:
        return jnp.zeros_like(state)
    assert count % 2 == 0 and decay.shape[0] % 2 == 0
    place = lax.axis_index(axis)
    virt = count - 1 - place if reverse else place

    def phys(u):
        return count - 1 - u if reverse else u

    half = decay.shape[0] // 2
    groups = count // 2
    side = virt % 2
    group = virt // 2
    first = side == 0
    own_start = (1 - side) * half
    send_start = side * half

    def part(x, start):
        return lax.dynamic_slice_in_dim(x, start, half, 0)

    a_own, s_own = part(decay, own_start), part(state, own_start)
    a_snd, s_snd = part(decay, send_start), part(state, send_start)
    swap = [(phys(u), phys(u ^ 1)) for u in range(count)]
    a_rcv, s_rcv = lax.ppermute((a_snd, s_snd), axis, swap)
    lead = (jnp.where(first, a_own, a_rcv), jnp.where(first, s_own, s_rcv))
    trail = (jnp.where(first, a_rcv, a_own), jnp.where(first, s_rcv, s_own))
    a_tot, s_tot = combine(lead, trail)

    def shift_pairs(k):
        return [
            (phys(2 * g + x), phys(2 * (g + k) + x)) for g in range(groups - k) for x in (0, 1)
        ]

    if groups <= 4:
        a_g = jnp.ones_like(a_tot)
        s_g = jnp.zeros_like(s_tot)
        for r in range(groups - 1):
            out = combine((a_g, s_g), (a_tot, s_tot))
            pairs = [(phys(2 * r + x), phys(2 * (r + 1) + x)) for x in (0, 1)]
            if r == groups - 2:
                s_in = lax.ppermute(out[1], axis, pairs)
                a_in = a_g
            else:
                a_in, s_in = lax.ppermute(out, axis, pairs)
            dst = group == r + 1
            a_g = jnp.where(dst, a_in, a_g)
            s_g = jnp.where(dst, s_in, s_g)
    else:
        a_g, s_g = lax.ppermute((a_tot, s_tot), axis, shift_pairs(1))
        a_g = jnp.where(group == 0, 1.0, a_g)
        s_g = jnp.where(group == 0, 0.0, s_g)
        k = 1
        while k < groups:
            got = lax.ppermute((a_g, s_g), axis, shift_pairs(k))
            a_c, s_c = combine(got, (a_g, s_g))
            a_g = jnp.where(group >= k, a_c, a_g)
            s_g = jnp.where(group >= k, s_c, s_g)
            k *= 2

    with_lead_own = a_own[:, None, None] * s_g + s_own
    with_lead_rcv = a_rcv[:, None, None] * s_g + s_rcv
    send = jnp.where(first, with_lead_own, s_g)
    keep = jnp.where(first, s_g, with_lead_rcv)
    other = lax.ppermute(send, axis, swap)
    if split:
        return keep, other, own_start, send_start, first
    return jnp.where(
        first, jnp.concatenate([other, keep], 0), jnp.concatenate([keep, other], 0)
    )


def butterfly_psum(parts, axis):
    count = lax.axis_size(axis)
    if count & (count - 1):
        return lax.psum(parts, axis)
    k = 1
    while k < count:
        got = lax.ppermute(parts, axis, [(i, i ^ k) for i in range(count)])
        parts = jax.tree.map(jnp.add, parts, got)
        k *= 2
    return parts


def block_step(carry_state, inputs, skip_scale):
    feat_block, step_block, decay_block, write_block, read_block = inputs
    length = decay_block.shape[1]
    cumul = jnp.cumsum(decay_block, axis=1)
    row_index = lax.broadcasted_iota(jnp.int32, (length, length), 0)
    col_index = lax.broadcasted_iota(jnp.int32, (length, length), 1)
    causal = row_index >= col_index
    gaps = jnp.where(causal[None], cumul[:, :, None] - cumul[:, None, :], 0.0)
    weights = jnp.where(causal[None], jnp.exp(gaps), 0.0)
    scores = jnp.dot(read_block, jnp.transpose(write_block), precision=highest)
    scaled = feat_block * jnp.transpose(step_block)[:, :, None]
    masked = weights * scores[None]
    within = jnp.einsum("hij,jhp->ihp", masked, scaled, precision=highest)
    carried = jnp.einsum("in,hpn->ihp", read_block, carry_state, precision=highest)
    carried = carried * jnp.transpose(jnp.exp(cumul))[:, :, None]
    output = within + carried + skip_scale[None, :, None] * feat_block
    to_end = jnp.exp(cumul[:, -1:] - cumul)
    weighted_in = scaled * jnp.transpose(to_end)[:, :, None]
    update = jnp.einsum("jhp,jn->hpn", weighted_in, write_block, precision=highest)
    new_state = jnp.exp(cumul[:, -1])[:, None, None] * carry_state + update
    return (new_state, output)


def run_mixer(
    features, step_sizes, log_decay, write_keys, read_queries, carry_state, skip_scale, block
):
    length = features.shape[0]
    head_count = step_sizes.shape[0]
    head_width = features.shape[1] // head_count
    block_total = length // block
    feat_blocks = features.reshape(block_total, block, head_count, head_width)
    step_blocks = jnp.transpose(step_sizes.reshape(head_count, block_total, block), (1, 0, 2))
    decay_blocks = jnp.transpose(log_decay.reshape(head_count, block_total, block), (1, 0, 2))
    write_blocks = write_keys.reshape(block_total, block, write_keys.shape[1])
    read_blocks = read_queries.reshape(block_total, block, read_queries.shape[1])

    def advance(carried_in, inputs):
        return block_step(carried_in, inputs, skip_scale)

    last_state, outputs = lax.scan(
        advance, carry_state, (feat_blocks, step_blocks, decay_blocks, write_blocks, read_blocks)
    )
    return (last_state, outputs.reshape(length, head_count * head_width))


def prefix_sum(decay_in):
    length = decay_in.shape[1]
    upper = (
        lax.broadcasted_iota(jnp.int32, (length, length), 0)
        <= lax.broadcasted_iota(jnp.int32, (length, length), 1)
    ).astype(decay_in.dtype)
    return jnp.dot(decay_in, upper, precision=lax.Precision.HIGHEST)


def within_part(feat_in, step_in, decay_in, writes, read_in, skip_scale):
    head_count, length = step_in.shape
    head_width = feat_in.shape[1] // head_count
    cumul = prefix_sum(decay_in)
    row_index = lax.broadcasted_iota(jnp.int32, (length, length), 0)
    col_index = lax.broadcasted_iota(jnp.int32, (length, length), 1)
    causal = row_index >= col_index
    gaps = jnp.where(causal[None], cumul[:, :, None] - cumul[:, None, :], 0.0)
    weights = jnp.where(causal[None], jnp.exp(gaps), 0.0)
    scores = jnp.dot(read_in, jnp.transpose(writes), precision=highest)
    feat3 = feat_in.reshape(length, head_count, head_width)
    scaled = feat3 * jnp.transpose(step_in)[:, :, None]
    masked = weights * scores[None]
    within = jnp.einsum("hij,jhp->ihp", masked, scaled, precision=highest)
    return (within + skip_scale[None, :, None] * feat3).reshape(length, -1)


def carried_part(decay_in, read_in, state_in):
    length = decay_in.shape[1]
    cumul = prefix_sum(decay_in)
    carried = jnp.einsum("in,hpn->ihp", read_in, state_in, precision=highest)
    carried = carried * jnp.transpose(jnp.exp(cumul))[:, :, None]
    return carried.reshape(length, -1)


def state_update(feat_in, step_in, decay_in, writes):
    head_count, length = step_in.shape
    head_width = feat_in.shape[1] // head_count
    cumul = prefix_sum(decay_in)
    scaled = feat_in.reshape(length, head_count, head_width) * jnp.transpose(step_in)[:, :, None]
    to_end = jnp.exp(cumul[:, -1:] - cumul)
    weighted_in = scaled * jnp.transpose(to_end)[:, :, None]
    return jnp.einsum("jhp,jn->hpn", weighted_in, writes, precision=highest)


def end_part(feat_in, step_in, decay_in, writes, state_in):
    total = jnp.exp(prefix_sum(decay_in)[:, -1])
    return total[:, None, None] * state_in + state_update(feat_in, step_in, decay_in, writes)


def local(
    features,
    gate_pre,
    write_keys,
    read_queries,
    step_sizes,
    log_decay,
    skip_scale,
    norm_gain,
    out_grad,
):
    head_count, length = step_sizes.shape
    head_width = features.shape[1] // head_count
    channels = features.shape[1] * lax.axis_size("head")
    cumul = prefix_sum(log_decay)
    decay_total = jnp.exp(cumul[:, -1])
    scaled = (
        features.reshape(length, head_count, head_width) * jnp.transpose(step_sizes)[:, :, None]
    )
    to_end = jnp.exp(cumul[:, -1:] - cumul)
    weighted_in = scaled * jnp.transpose(to_end)[:, :, None]
    local_state = jnp.einsum("jhp,jn->hpn", weighted_in, write_keys, precision=highest)
    state_in = pair_scan(decay_total, local_state, "seq", False)
    single = length == BLOCK
    if single:
        mixed_w, pull_w = jax.vjp(
            lambda f, s, d, w, r: within_part(f, s, d, w, r, skip_scale),
            features, step_sizes, log_decay, write_keys, read_queries,
        )
        mixed_c, pull_c = jax.vjp(
            lambda d, r: carried_part(d, r, state_in), log_decay, read_queries
        )
        mixed_w = lax.optimization_barrier(mixed_w)
        mixed_out = mixed_w + mixed_c
    else:

        def local_mixer(feat_in, step_in, decay_factors, writes, read_in):
            return run_mixer(
                feat_in, step_in, decay_factors, writes, read_in, state_in, skip_scale, BLOCK
            )

        primal, pullback = jax.vjp(
            local_mixer, features, step_sizes, log_decay, write_keys, read_queries
        )
        mixed_out = primal[1]
    sigmoid_gate = jax.nn.sigmoid(gate_pre)
    active = gate_pre * sigmoid_gate
    gated_out = mixed_out * active
    weighted = out_grad * norm_gain[None, :]
    square_sum, cross_sum = butterfly_psum(
        jnp.stack([jnp.sum(gated_out * gated_out, axis=1), jnp.sum(weighted * gated_out, axis=1)]),
        "head",
    )
    inverse = lax.rsqrt(square_sum / channels + eps)
    grad_gated = (
        inverse[:, None] * weighted
        - (inverse * inverse * inverse * cross_sum / channels)[:, None] * gated_out
    )
    grad_mixed = grad_gated * active
    grad_gate = grad_gated * mixed_out * sigmoid_gate * (1.0 + gate_pre * (1.0 - sigmoid_gate))
    from_start = jnp.transpose(jnp.exp(cumul))
    weighted_grad = grad_mixed.reshape(length, head_count, head_width) * from_start[:, :, None]
    local_grad = jnp.einsum("jhp,jn->hpn", weighted_grad, read_queries, precision=highest)
    if single:
        sg_keep, sg_other, own_start, send_start, first = pair_scan(
            decay_total, local_grad, "seq", True, split=True
        )
        gf_w, gs_w, gd_w, gw_w, gr_w = pull_w(grad_mixed)
        gd_c, gr_c = pull_c(grad_mixed)
        grad_read = butterfly_psum(gr_w + gr_c, "head")
        half = sg_keep.shape[0]

        def end_half(start, grad_half):
            feat_h = lax.dynamic_slice_in_dim(features, start * head_width, half * head_width, 1)
            step_h = lax.dynamic_slice_in_dim(step_sizes, start, half, 0)
            decay_h = lax.dynamic_slice_in_dim(log_decay, start, half, 0)
            state_h = lax.dynamic_slice_in_dim(state_in, start, half, 0)
            _, pull_h = jax.vjp(
                lambda f, s, d, w: end_part(f, s, d, w, state_h),
                feat_h, step_h, decay_h, write_keys,
            )
            return pull_h(grad_half)

        own = end_half(own_start, sg_keep)
        rest = end_half(send_start, sg_other)

        def join(a, b, axis):
            return jnp.where(
                first, jnp.concatenate([b, a], axis), jnp.concatenate([a, b], axis)
            )

        gf_e = join(own[0], rest[0], 1)
        gs_e = join(own[1], rest[1], 0)
        gd_e = join(own[2], rest[2], 0)
        gw_e = own[3] + rest[3]
        grad_features = gf_w + gf_e
        grad_steps = gs_w + gs_e
        grad_decay = gd_w + gd_c + gd_e
        grad_write = butterfly_psum(gw_w + gw_e, "head")
    else:
        state_grad = pair_scan(decay_total, local_grad, "seq", True)
        grad_features, grad_steps, grad_decay, grad_write, grad_read = pullback(
            (state_grad, grad_mixed)
        )
        grad_write, grad_read = butterfly_psum((grad_write, grad_read), "head")
    return (grad_features, grad_gate, grad_write, grad_read, grad_steps, grad_decay)


def solution(mesh):
    placed = (
        P("seq", "head"),
        P("seq", "head"),
        P("seq", None),
        P("seq", None),
        P("head", "seq"),
        P("head", "seq"),
        P("head"),
        P("head"),
        P("seq", "head"),
    )
    return jax.shard_map(
        local,
        mesh=mesh,
        in_specs=placed,
        out_specs=(
            P("seq", "head"),
            P("seq", "head"),
            P("seq", None),
            P("seq", None),
            P("head", "seq"),
            P("head", "seq"),
        ),
        check_vma=False,
    )
```

```python
import jax
import jax.numpy as jnp
from jax import lax
from jax.sharding import PartitionSpec as P

BLOCK = 128


eps = 1e-05
highest = lax.Precision.HIGH


def combine(earlier, later):
    return (earlier[0] * later[0], later[0][:, None, None] * earlier[1] + later[1])


def pair_scan(decay, state, axis, reverse, split=False):
    count = lax.axis_size(axis)
    if count == 1:
        return jnp.zeros_like(state)
    assert count % 2 == 0 and decay.shape[0] % 2 == 0
    place = lax.axis_index(axis)
    virt = count - 1 - place if reverse else place

    def phys(u):
        return count - 1 - u if reverse else u

    half = decay.shape[0] // 2
    groups = count // 2
    side = virt % 2
    group = virt // 2
    first = side == 0
    own_start = (1 - side) * half
    send_start = side * half

    def part(x, start):
        return lax.dynamic_slice_in_dim(x, start, half, 0)

    a_own, s_own = part(decay, own_start), part(state, own_start)
    a_snd, s_snd = part(decay, send_start), part(state, send_start)
    swap = [(phys(u), phys(u ^ 1)) for u in range(count)]
    a_rcv, s_rcv = lax.ppermute((a_snd, s_snd), axis, swap)
    lead = (jnp.where(first, a_own, a_rcv), jnp.where(first, s_own, s_rcv))
    trail = (jnp.where(first, a_rcv, a_own), jnp.where(first, s_rcv, s_own))
    a_tot, s_tot = combine(lead, trail)

    def shift_pairs(k):
        return [
            (phys(2 * g + x), phys(2 * (g + k) + x)) for g in range(groups - k) for x in (0, 1)
        ]

    if groups <= 4:
        a_g = jnp.ones_like(a_tot)
        s_g = jnp.zeros_like(s_tot)
        for r in range(groups - 1):
            out = combine((a_g, s_g), (a_tot, s_tot))
            pairs = [(phys(2 * r + x), phys(2 * (r + 1) + x)) for x in (0, 1)]
            if r == groups - 2:
                s_in = lax.ppermute(out[1], axis, pairs)
                a_in = a_g
            else:
                a_in, s_in = lax.ppermute(out, axis, pairs)
            dst = group == r + 1
            a_g = jnp.where(dst, a_in, a_g)
            s_g = jnp.where(dst, s_in, s_g)
    else:
        a_g, s_g = lax.ppermute((a_tot, s_tot), axis, shift_pairs(1))
        a_g = jnp.where(group == 0, 1.0, a_g)
        s_g = jnp.where(group == 0, 0.0, s_g)
        k = 1
        while k < groups:
            got = lax.ppermute((a_g, s_g), axis, shift_pairs(k))
            a_c, s_c = combine(got, (a_g, s_g))
            a_g = jnp.where(group >= k, a_c, a_g)
            s_g = jnp.where(group >= k, s_c, s_g)
            k *= 2

    with_lead_own = a_own[:, None, None] * s_g + s_own
    with_lead_rcv = a_rcv[:, None, None] * s_g + s_rcv
    send = jnp.where(first, with_lead_own, s_g)
    keep = jnp.where(first, s_g, with_lead_rcv)
    other = lax.ppermute(send, axis, swap)
    if split:
        return keep, other, own_start, send_start, first
    return jnp.where(
        first, jnp.concatenate([other, keep], 0), jnp.concatenate([keep, other], 0)
    )


def butterfly_psum(parts, axis):
    count = lax.axis_size(axis)
    if count & (count - 1):
        return lax.psum(parts, axis)
    k = 1
    while k < count:
        got = lax.ppermute(parts, axis, [(i, i ^ k) for i in range(count)])
        parts = jax.tree.map(jnp.add, parts, got)
        k *= 2
    return parts


def block_step(carry_state, inputs, skip_scale):
    feat_block, step_block, decay_block, write_block, read_block = inputs
    length = decay_block.shape[1]
    cumul = jnp.cumsum(decay_block, axis=1)
    row_index = lax.broadcasted_iota(jnp.int32, (length, length), 0)
    col_index = lax.broadcasted_iota(jnp.int32, (length, length), 1)
    causal = row_index >= col_index
    gaps = jnp.where(causal[None], cumul[:, :, None] - cumul[:, None, :], 0.0)
    weights = jnp.where(causal[None], jnp.exp(gaps), 0.0)
    scores = jnp.dot(read_block, jnp.transpose(write_block), precision=highest)
    scaled = feat_block * jnp.transpose(step_block)[:, :, None]
    masked = weights * scores[None]
    within = jnp.einsum("hij,jhp->ihp", masked, scaled, precision=highest)
    carried = jnp.einsum("in,hpn->ihp", read_block, carry_state, precision=highest)
    carried = carried * jnp.transpose(jnp.exp(cumul))[:, :, None]
    output = within + carried + skip_scale[None, :, None] * feat_block
    to_end = jnp.exp(cumul[:, -1:] - cumul)
    weighted_in = scaled * jnp.transpose(to_end)[:, :, None]
    update = jnp.einsum("jhp,jn->hpn", weighted_in, write_block, precision=highest)
    new_state = jnp.exp(cumul[:, -1])[:, None, None] * carry_state + update
    return (new_state, output)


def run_mixer(
    features, step_sizes, log_decay, write_keys, read_queries, carry_state, skip_scale, block
):
    length = features.shape[0]
    head_count = step_sizes.shape[0]
    head_width = features.shape[1] // head_count
    block_total = length // block
    feat_blocks = features.reshape(block_total, block, head_count, head_width)
    step_blocks = jnp.transpose(step_sizes.reshape(head_count, block_total, block), (1, 0, 2))
    decay_blocks = jnp.transpose(log_decay.reshape(head_count, block_total, block), (1, 0, 2))
    write_blocks = write_keys.reshape(block_total, block, write_keys.shape[1])
    read_blocks = read_queries.reshape(block_total, block, read_queries.shape[1])

    def advance(carried_in, inputs):
        return block_step(carried_in, inputs, skip_scale)

    last_state, outputs = lax.scan(
        advance, carry_state, (feat_blocks, step_blocks, decay_blocks, write_blocks, read_blocks)
    )
    return (last_state, outputs.reshape(length, head_count * head_width))


def prefix_sum(decay_in):
    length = decay_in.shape[1]
    upper = (
        lax.broadcasted_iota(jnp.int32, (length, length), 0)
        <= lax.broadcasted_iota(jnp.int32, (length, length), 1)
    ).astype(decay_in.dtype)
    return jnp.dot(decay_in, upper, precision=lax.Precision.HIGHEST)


def within_part(feat_in, step_in, decay_in, writes, read_in, skip_scale):
    head_count, length = step_in.shape
    head_width = feat_in.shape[1] // head_count
    cumul = prefix_sum(decay_in)
    row_index = lax.broadcasted_iota(jnp.int32, (length, length), 0)
    col_index = lax.broadcasted_iota(jnp.int32, (length, length), 1)
    causal = row_index >= col_index
    gaps = jnp.where(causal[None], cumul[:, :, None] - cumul[:, None, :], 0.0)
    weights = jnp.where(causal[None], jnp.exp(gaps), 0.0)
    scores = jnp.dot(read_in, jnp.transpose(writes), precision=highest)
    feat3 = feat_in.reshape(length, head_count, head_width)
    scaled = feat3 * jnp.transpose(step_in)[:, :, None]
    masked = weights * scores[None]
    within = jnp.einsum("hij,jhp->ihp", masked, scaled, precision=highest)
    return (within + skip_scale[None, :, None] * feat3).reshape(length, -1)


def carried_part(decay_in, read_in, state_in):
    length = decay_in.shape[1]
    cumul = prefix_sum(decay_in)
    carried = jnp.einsum("in,hpn->ihp", read_in, state_in, precision=highest)
    carried = carried * jnp.transpose(jnp.exp(cumul))[:, :, None]
    return carried.reshape(length, -1)


def state_update(feat_in, step_in, decay_in, writes):
    head_count, length = step_in.shape
    head_width = feat_in.shape[1] // head_count
    cumul = prefix_sum(decay_in)
    scaled = feat_in.reshape(length, head_count, head_width) * jnp.transpose(step_in)[:, :, None]
    to_end = jnp.exp(cumul[:, -1:] - cumul)
    weighted_in = scaled * jnp.transpose(to_end)[:, :, None]
    return jnp.einsum("jhp,jn->hpn", weighted_in, writes, precision=highest)


def end_part(feat_in, step_in, decay_in, writes, state_in):
    total = jnp.exp(prefix_sum(decay_in)[:, -1])
    return total[:, None, None] * state_in + state_update(feat_in, step_in, decay_in, writes)


def local(
    features,
    gate_pre,
    write_keys,
    read_queries,
    step_sizes,
    log_decay,
    skip_scale,
    norm_gain,
    out_grad,
):
    head_count, length = step_sizes.shape
    head_width = features.shape[1] // head_count
    channels = features.shape[1] * lax.axis_size("head")
    cumul = prefix_sum(log_decay)
    decay_total = jnp.exp(cumul[:, -1])
    scaled = (
        features.reshape(length, head_count, head_width) * jnp.transpose(step_sizes)[:, :, None]
    )
    to_end = jnp.exp(cumul[:, -1:] - cumul)
    weighted_in = scaled * jnp.transpose(to_end)[:, :, None]
    local_state = jnp.einsum("jhp,jn->hpn", weighted_in, write_keys, precision=highest)
    single = length == BLOCK
    sigmoid_gate = jax.nn.sigmoid(gate_pre)
    active = gate_pre * sigmoid_gate
    weighted = out_grad * norm_gain[None, :]
    if single:
        keep_f, other_f, own_f, send_f, first_f = pair_scan(
            decay_total, local_state, "seq", False, split=True
        )
        half_f = keep_f.shape[0]

        def join_f(a, b, axis):
            return jnp.where(
                first_f, jnp.concatenate([b, a], axis), jnp.concatenate([a, b], axis)
            )

        def cols(x, start):
            return lax.dynamic_slice_in_dim(x, start * head_width, half_f * head_width, 1)

        state_in = join_f(keep_f, other_f, 0)
        mixed_w, pull_w = jax.vjp(
            lambda f, s, d, w, r: within_part(f, s, d, w, r, skip_scale),
            features, step_sizes, log_decay, write_keys, read_queries,
        )
        mixed_w = lax.optimization_barrier(mixed_w)

        def carried_half(start, state_h):
            decay_h = lax.dynamic_slice_in_dim(log_decay, start, half_f, 0)
            out_h, pull_h = jax.vjp(
                lambda d, r: carried_part(d, r, state_h), decay_h, read_queries
            )
            return cols(mixed_w, start) + out_h, pull_h

        mixed_own, pull_c_own = carried_half(own_f, keep_f)
        mixed_oth, pull_c_oth = carried_half(send_f, other_f)
        mixed_out = join_f(mixed_own, mixed_oth, 1)
        gated_own = mixed_own * cols(active, own_f)
        gated_oth = mixed_oth * cols(active, send_f)
        sums = jnp.stack([
            jnp.sum(gated_own * gated_own, axis=1) + jnp.sum(gated_oth * gated_oth, axis=1),
            jnp.sum(cols(weighted, own_f) * gated_own, axis=1)
            + jnp.sum(cols(weighted, send_f) * gated_oth, axis=1),
        ])
    else:
        state_in = pair_scan(decay_total, local_state, "seq", False)

        def local_mixer(feat_in, step_in, decay_factors, writes, read_in):
            return run_mixer(
                feat_in, step_in, decay_factors, writes, read_in, state_in, skip_scale, BLOCK
            )

        primal, pullback = jax.vjp(
            local_mixer, features, step_sizes, log_decay, write_keys, read_queries
        )
        mixed_out = primal[1]
        gated_full = mixed_out * active
        sums = jnp.stack(
            [jnp.sum(gated_full * gated_full, axis=1), jnp.sum(weighted * gated_full, axis=1)]
        )
    gated_out = mixed_out * active
    square_sum, cross_sum = butterfly_psum(sums, "head")
    inverse = lax.rsqrt(square_sum / channels + eps)
    grad_gated = (
        inverse[:, None] * weighted
        - (inverse * inverse * inverse * cross_sum / channels)[:, None] * gated_out
    )
    grad_mixed = grad_gated * active
    grad_gate = grad_gated * mixed_out * sigmoid_gate * (1.0 + gate_pre * (1.0 - sigmoid_gate))
    from_start = jnp.transpose(jnp.exp(cumul))
    weighted_grad = grad_mixed.reshape(length, head_count, head_width) * from_start[:, :, None]
    local_grad = jnp.einsum("jhp,jn->hpn", weighted_grad, read_queries, precision=highest)
    if single:
        sg_keep, sg_other, own_start, send_start, first = pair_scan(
            decay_total, local_grad, "seq", True, split=True
        )
        gf_w, gs_w, gd_w, gw_w, gr_w = pull_w(grad_mixed)
        gd_own, gr_own = pull_c_own(cols(grad_mixed, own_f))
        gd_oth, gr_oth = pull_c_oth(cols(grad_mixed, send_f))
        gd_c = join_f(gd_own, gd_oth, 0)
        gr_c = gr_own + gr_oth
        grad_read = butterfly_psum(gr_w + gr_c, "head")
        half = sg_keep.shape[0]

        def end_half(start, grad_half):
            feat_h = lax.dynamic_slice_in_dim(features, start * head_width, half * head_width, 1)
            step_h = lax.dynamic_slice_in_dim(step_sizes, start, half, 0)
            decay_h = lax.dynamic_slice_in_dim(log_decay, start, half, 0)
            state_h = lax.dynamic_slice_in_dim(state_in, start, half, 0)
            _, pull_h = jax.vjp(
                lambda f, s, d, w: end_part(f, s, d, w, state_h),
                feat_h, step_h, decay_h, write_keys,
            )
            return pull_h(grad_half)

        own = end_half(own_start, sg_keep)
        rest = end_half(send_start, sg_other)

        def join(a, b, axis):
            return jnp.where(
                first, jnp.concatenate([b, a], axis), jnp.concatenate([a, b], axis)
            )

        gf_e = join(own[0], rest[0], 1)
        gs_e = join(own[1], rest[1], 0)
        gd_e = join(own[2], rest[2], 0)
        gw_e = own[3] + rest[3]
        grad_features = gf_w + gf_e
        grad_steps = gs_w + gs_e
        grad_decay = gd_w + gd_c + gd_e
        grad_write = butterfly_psum(gw_w + gw_e, "head")
    else:
        state_grad = pair_scan(decay_total, local_grad, "seq", True)
        grad_features, grad_steps, grad_decay, grad_write, grad_read = pullback(
            (state_grad, grad_mixed)
        )
        grad_write, grad_read = butterfly_psum((grad_write, grad_read), "head")
    return (grad_features, grad_gate, grad_write, grad_read, grad_steps, grad_decay)


def solution(mesh):
    placed = (
        P("seq", "head"),
        P("seq", "head"),
        P("seq", None),
        P("seq", None),
        P("head", "seq"),
        P("head", "seq"),
        P("head"),
        P("head"),
        P("seq", "head"),
    )
    return jax.shard_map(
        local,
        mesh=mesh,
        in_specs=placed,
        out_specs=(
            P("seq", "head"),
            P("seq", "head"),
            P("seq", None),
            P("seq", None),
            P("head", "seq"),
            P("head", "seq"),
        ),
        check_vma=False,
    )
```

```python
import jax
import jax.numpy as jnp
from jax import lax
from jax.sharding import PartitionSpec as P

BLOCK = 128


eps = 1e-05
highest = lax.Precision.HIGH


def combine(earlier, later):
    return (earlier[0] * later[0], later[0][:, None, None] * earlier[1] + later[1])


def pair_scan(decay, state, axis, reverse, split=False):
    count = lax.axis_size(axis)
    if count == 1:
        return jnp.zeros_like(state)
    assert count % 2 == 0 and decay.shape[0] % 2 == 0
    place = lax.axis_index(axis)
    virt = count - 1 - place if reverse else place

    def phys(u):
        return count - 1 - u if reverse else u

    half = decay.shape[0] // 2
    groups = count // 2
    side = virt % 2
    group = virt // 2
    first = side == 0
    own_start = (1 - side) * half
    send_start = side * half

    def part(x, start):
        return lax.dynamic_slice_in_dim(x, start, half, 0)

    a_own, s_own = part(decay, own_start), part(state, own_start)
    a_snd, s_snd = part(decay, send_start), part(state, send_start)
    swap = [(phys(u), phys(u ^ 1)) for u in range(count)]
    a_rcv, s_rcv = lax.ppermute((a_snd, s_snd), axis, swap)
    lead = (jnp.where(first, a_own, a_rcv), jnp.where(first, s_own, s_rcv))
    trail = (jnp.where(first, a_rcv, a_own), jnp.where(first, s_rcv, s_own))
    a_tot, s_tot = combine(lead, trail)

    def shift_pairs(k):
        return [
            (phys(2 * g + x), phys(2 * (g + k) + x)) for g in range(groups - k) for x in (0, 1)
        ]

    if groups <= 4:
        a_g = jnp.ones_like(a_tot)
        s_g = jnp.zeros_like(s_tot)
        for r in range(groups - 1):
            out = combine((a_g, s_g), (a_tot, s_tot))
            pairs = [(phys(2 * r + x), phys(2 * (r + 1) + x)) for x in (0, 1)]
            if r == groups - 2:
                s_in = lax.ppermute(out[1], axis, pairs)
                a_in = a_g
            else:
                a_in, s_in = lax.ppermute(out, axis, pairs)
            dst = group == r + 1
            a_g = jnp.where(dst, a_in, a_g)
            s_g = jnp.where(dst, s_in, s_g)
    else:
        a_g, s_g = lax.ppermute((a_tot, s_tot), axis, shift_pairs(1))
        a_g = jnp.where(group == 0, 1.0, a_g)
        s_g = jnp.where(group == 0, 0.0, s_g)
        k = 1
        while k < groups:
            got = lax.ppermute((a_g, s_g), axis, shift_pairs(k))
            a_c, s_c = combine(got, (a_g, s_g))
            a_g = jnp.where(group >= k, a_c, a_g)
            s_g = jnp.where(group >= k, s_c, s_g)
            k *= 2

    with_lead_own = a_own[:, None, None] * s_g + s_own
    with_lead_rcv = a_rcv[:, None, None] * s_g + s_rcv
    send = jnp.where(first, with_lead_own, s_g)
    keep = jnp.where(first, s_g, with_lead_rcv)
    other = lax.ppermute(send, axis, swap)
    if split:
        return keep, other, own_start, send_start, first
    return jnp.where(
        first, jnp.concatenate([other, keep], 0), jnp.concatenate([keep, other], 0)
    )


def butterfly_psum(parts, axis):
    count = lax.axis_size(axis)
    if count & (count - 1):
        return lax.psum(parts, axis)
    k = 1
    while k < count:
        got = lax.ppermute(parts, axis, [(i, i ^ k) for i in range(count)])
        parts = jax.tree.map(jnp.add, parts, got)
        k *= 2
    return parts


def block_step(carry_state, inputs, skip_scale):
    feat_block, step_block, decay_block, write_block, read_block = inputs
    length = decay_block.shape[1]
    cumul = jnp.cumsum(decay_block, axis=1)
    row_index = lax.broadcasted_iota(jnp.int32, (length, length), 0)
    col_index = lax.broadcasted_iota(jnp.int32, (length, length), 1)
    causal = row_index >= col_index
    gaps = jnp.where(causal[None], cumul[:, :, None] - cumul[:, None, :], 0.0)
    weights = jnp.where(causal[None], jnp.exp(gaps), 0.0)
    scores = jnp.dot(read_block, jnp.transpose(write_block), precision=highest)
    scaled = feat_block * jnp.transpose(step_block)[:, :, None]
    masked = weights * scores[None]
    within = jnp.einsum("hij,jhp->ihp", masked, scaled, precision=highest)
    carried = jnp.einsum("in,hpn->ihp", read_block, carry_state, precision=highest)
    carried = carried * jnp.transpose(jnp.exp(cumul))[:, :, None]
    output = within + carried + skip_scale[None, :, None] * feat_block
    to_end = jnp.exp(cumul[:, -1:] - cumul)
    weighted_in = scaled * jnp.transpose(to_end)[:, :, None]
    update = jnp.einsum("jhp,jn->hpn", weighted_in, write_block, precision=highest)
    new_state = jnp.exp(cumul[:, -1])[:, None, None] * carry_state + update
    return (new_state, output)


def run_mixer(
    features, step_sizes, log_decay, write_keys, read_queries, carry_state, skip_scale, block
):
    length = features.shape[0]
    head_count = step_sizes.shape[0]
    head_width = features.shape[1] // head_count
    block_total = length // block
    feat_blocks = features.reshape(block_total, block, head_count, head_width)
    step_blocks = jnp.transpose(step_sizes.reshape(head_count, block_total, block), (1, 0, 2))
    decay_blocks = jnp.transpose(log_decay.reshape(head_count, block_total, block), (1, 0, 2))
    write_blocks = write_keys.reshape(block_total, block, write_keys.shape[1])
    read_blocks = read_queries.reshape(block_total, block, read_queries.shape[1])

    def advance(carried_in, inputs):
        return block_step(carried_in, inputs, skip_scale)

    last_state, outputs = lax.scan(
        advance, carry_state, (feat_blocks, step_blocks, decay_blocks, write_blocks, read_blocks)
    )
    return (last_state, outputs.reshape(length, head_count * head_width))


def prefix_sum(decay_in):
    length = decay_in.shape[1]
    upper = (
        lax.broadcasted_iota(jnp.int32, (length, length), 0)
        <= lax.broadcasted_iota(jnp.int32, (length, length), 1)
    ).astype(decay_in.dtype)
    return jnp.dot(decay_in, upper, precision=lax.Precision.HIGHEST)


def within_part(feat_in, step_in, decay_in, writes, read_in, skip_scale):
    head_count, length = step_in.shape
    head_width = feat_in.shape[1] // head_count
    cumul = prefix_sum(decay_in)
    row_index = lax.broadcasted_iota(jnp.int32, (length, length), 0)
    col_index = lax.broadcasted_iota(jnp.int32, (length, length), 1)
    causal = row_index >= col_index
    gaps = jnp.where(causal[None], cumul[:, :, None] - cumul[:, None, :], 0.0)
    weights = jnp.where(causal[None], jnp.exp(gaps), 0.0)
    scores = jnp.dot(read_in, jnp.transpose(writes), precision=highest)
    feat3 = feat_in.reshape(length, head_count, head_width)
    scaled = feat3 * jnp.transpose(step_in)[:, :, None]
    masked = weights * scores[None]
    within = jnp.einsum("hij,jhp->ihp", masked, scaled, precision=highest)
    return (within + skip_scale[None, :, None] * feat3).reshape(length, -1)


def carried_part(decay_in, read_in, state_in):
    length = decay_in.shape[1]
    cumul = prefix_sum(decay_in)
    carried = jnp.einsum("in,hpn->ihp", read_in, state_in, precision=highest)
    carried = carried * jnp.transpose(jnp.exp(cumul))[:, :, None]
    return carried.reshape(length, -1)


def state_update(feat_in, step_in, decay_in, writes):
    head_count, length = step_in.shape
    head_width = feat_in.shape[1] // head_count
    cumul = prefix_sum(decay_in)
    scaled = feat_in.reshape(length, head_count, head_width) * jnp.transpose(step_in)[:, :, None]
    to_end = jnp.exp(cumul[:, -1:] - cumul)
    weighted_in = scaled * jnp.transpose(to_end)[:, :, None]
    return jnp.einsum("jhp,jn->hpn", weighted_in, writes, precision=highest)


def end_part(feat_in, step_in, decay_in, writes, state_in):
    total = jnp.exp(prefix_sum(decay_in)[:, -1])
    return total[:, None, None] * state_in + state_update(feat_in, step_in, decay_in, writes)


def local(
    features,
    gate_pre,
    write_keys,
    read_queries,
    step_sizes,
    log_decay,
    skip_scale,
    norm_gain,
    out_grad,
):
    head_count, length = step_sizes.shape
    head_width = features.shape[1] // head_count
    channels = features.shape[1] * lax.axis_size("head")
    cumul = prefix_sum(log_decay)
    decay_total = jnp.exp(cumul[:, -1])
    scaled = (
        features.reshape(length, head_count, head_width) * jnp.transpose(step_sizes)[:, :, None]
    )
    to_end = jnp.exp(cumul[:, -1:] - cumul)
    weighted_in = scaled * jnp.transpose(to_end)[:, :, None]
    local_state = jnp.einsum("jhp,jn->hpn", weighted_in, write_keys, precision=highest)
    state_in = pair_scan(decay_total, local_state, "seq", False)
    single = length == BLOCK
    if single:
        mixed_w, pull_w = jax.vjp(
            lambda f, s, d, w, r: within_part(f, s, d, w, r, skip_scale),
            features, step_sizes, log_decay, write_keys, read_queries,
        )
        mixed_c, pull_c = jax.vjp(
            lambda d, r: carried_part(d, r, state_in), log_decay, read_queries
        )
        mixed_w = lax.optimization_barrier(mixed_w)
        mixed_out = mixed_w + mixed_c
    else:

        def local_mixer(feat_in, step_in, decay_factors, writes, read_in):
            return run_mixer(
                feat_in, step_in, decay_factors, writes, read_in, state_in, skip_scale, BLOCK
            )

        primal, pullback = jax.vjp(
            local_mixer, features, step_sizes, log_decay, write_keys, read_queries
        )
        mixed_out = primal[1]
    sigmoid_gate = jax.nn.sigmoid(gate_pre)
    active = gate_pre * sigmoid_gate
    gated_out = mixed_out * active
    weighted = out_grad * norm_gain[None, :]
    square_sum, cross_sum = butterfly_psum(
        jnp.stack([jnp.sum(gated_out * gated_out, axis=1), jnp.sum(weighted * gated_out, axis=1)]),
        "head",
    )
    inverse = lax.rsqrt(square_sum / channels + eps)
    grad_gated = (
        inverse[:, None] * weighted
        - (inverse * inverse * inverse * cross_sum / channels)[:, None] * gated_out
    )
    grad_mixed = grad_gated * active
    grad_gate = grad_gated * mixed_out * sigmoid_gate * (1.0 + gate_pre * (1.0 - sigmoid_gate))
    from_start = jnp.transpose(jnp.exp(cumul))
    weighted_grad = grad_mixed.reshape(length, head_count, head_width) * from_start[:, :, None]
    local_grad = jnp.einsum("jhp,jn->hpn", weighted_grad, read_queries, precision=highest)
    if single:
        sg_keep, sg_other, own_start, send_start, first = pair_scan(
            decay_total, local_grad, "seq", True, split=True
        )
        gf_w, gs_w, gd_w, gw_w, gr_w = pull_w(grad_mixed)
        gd_c, gr_c = pull_c(grad_mixed)
        grad_read = butterfly_psum(gr_w + gr_c, "head")
        half = sg_keep.shape[0]

        def end_half(start, grad_half):
            feat_h = lax.dynamic_slice_in_dim(features, start * head_width, half * head_width, 1)
            step_h = lax.dynamic_slice_in_dim(step_sizes, start, half, 0)
            decay_h = lax.dynamic_slice_in_dim(log_decay, start, half, 0)
            state_h = lax.dynamic_slice_in_dim(state_in, start, half, 0)
            _, pull_h = jax.vjp(
                lambda f, s, d: end_part(f, s, d, write_keys, state_h),
                feat_h, step_h, decay_h,
            )
            return pull_h(grad_half)

        def write_half(start, grad_half):
            wi_h = lax.dynamic_slice_in_dim(weighted_in, start, half, 1)
            return jnp.dot(
                wi_h.reshape(length, -1), grad_half.reshape(-1, grad_half.shape[2]),
                precision=highest,
            )

        write_part = gw_w + (write_half(own_start, sg_keep) + write_half(send_start, sg_other))
        grad_write = butterfly_psum(write_part, "head")
        sg_keep, sg_other, write_part = lax.optimization_barrier((sg_keep, sg_other, write_part))
        own = end_half(own_start, sg_keep)
        rest = end_half(send_start, sg_other)

        def join(a, b, axis):
            return jnp.where(
                first, jnp.concatenate([b, a], axis), jnp.concatenate([a, b], axis)
            )

        gf_e = join(own[0], rest[0], 1)
        gs_e = join(own[1], rest[1], 0)
        gd_e = join(own[2], rest[2], 0)
        grad_features = gf_w + gf_e
        grad_steps = gs_w + gs_e
        grad_decay = gd_w + gd_c + gd_e
    else:
        state_grad = pair_scan(decay_total, local_grad, "seq", True)
        grad_features, grad_steps, grad_decay, grad_write, grad_read = pullback(
            (state_grad, grad_mixed)
        )
        grad_write, grad_read = butterfly_psum((grad_write, grad_read), "head")
    return (grad_features, grad_gate, grad_write, grad_read, grad_steps, grad_decay)


def solution(mesh):
    placed = (
        P("seq", "head"),
        P("seq", "head"),
        P("seq", None),
        P("seq", None),
        P("head", "seq"),
        P("head", "seq"),
        P("head"),
        P("head"),
        P("seq", "head"),
    )
    return jax.shard_map(
        local,
        mesh=mesh,
        in_specs=placed,
        out_specs=(
            P("seq", "head"),
            P("seq", "head"),
            P("seq", None),
            P("seq", None),
            P("head", "seq"),
            P("head", "seq"),
        ),
        check_vma=False,
    )
```

```python
import jax
import jax.numpy as jnp
from jax import lax
from jax.sharding import PartitionSpec as P

BLOCK = 128


eps = 1e-05
highest = lax.Precision.HIGH


def combine(earlier, later):
    return (earlier[0] * later[0], later[0][:, None, None] * earlier[1] + later[1])


def pair_scan(decay, state, axis, reverse, split=False):
    count = lax.axis_size(axis)
    if count == 1:
        return jnp.zeros_like(state)
    assert count % 2 == 0 and decay.shape[0] % 2 == 0
    place = lax.axis_index(axis)
    virt = count - 1 - place if reverse else place

    def phys(u):
        return count - 1 - u if reverse else u

    half = decay.shape[0] // 2
    groups = count // 2
    side = virt % 2
    group = virt // 2
    first = side == 0
    own_start = (1 - side) * half
    send_start = side * half

    def part(x, start):
        return lax.dynamic_slice_in_dim(x, start, half, 0)

    a_own, s_own = part(decay, own_start), part(state, own_start)
    a_snd, s_snd = part(decay, send_start), part(state, send_start)
    swap = [(phys(u), phys(u ^ 1)) for u in range(count)]
    a_rcv, s_rcv = lax.ppermute((a_snd, s_snd), axis, swap)
    lead = (jnp.where(first, a_own, a_rcv), jnp.where(first, s_own, s_rcv))
    trail = (jnp.where(first, a_rcv, a_own), jnp.where(first, s_rcv, s_own))
    a_tot, s_tot = combine(lead, trail)

    def shift_pairs(k):
        return [
            (phys(2 * g + x), phys(2 * (g + k) + x)) for g in range(groups - k) for x in (0, 1)
        ]

    if groups <= 4:
        got = None
        s_g = jnp.zeros_like(s_tot)
        for r in range(groups - 1):
            out = (a_tot, s_tot) if got is None else combine(got, (a_tot, s_tot))
            pairs = [(phys(2 * r + x), phys(2 * (r + 1) + x)) for x in (0, 1)]
            if r == groups - 2:
                got = (a_tot, lax.ppermute(out[1], axis, pairs))
            else:
                got = lax.ppermute(out, axis, pairs)
            s_g = jnp.where(group == r + 1, got[1], s_g)
    else:
        a_g, s_g = lax.ppermute((a_tot, s_tot), axis, shift_pairs(1))
        a_g = jnp.where(group == 0, 1.0, a_g)
        s_g = jnp.where(group == 0, 0.0, s_g)
        k = 1
        while k < groups:
            got = lax.ppermute((a_g, s_g), axis, shift_pairs(k))
            a_c, s_c = combine(got, (a_g, s_g))
            a_g = jnp.where(group >= k, a_c, a_g)
            s_g = jnp.where(group >= k, s_c, s_g)
            k *= 2

    with_lead_own = a_own[:, None, None] * s_g + s_own
    with_lead_rcv = a_rcv[:, None, None] * s_g + s_rcv
    send = jnp.where(first, with_lead_own, s_g)
    keep = jnp.where(first, s_g, with_lead_rcv)
    other = lax.ppermute(send, axis, swap)
    if split:
        return keep, other, own_start, send_start, first
    return jnp.where(
        first, jnp.concatenate([other, keep], 0), jnp.concatenate([keep, other], 0)
    )


def butterfly_psum(parts, axis):
    count = lax.axis_size(axis)
    if count & (count - 1):
        return lax.psum(parts, axis)
    k = 1
    while k < count:
        got = lax.ppermute(parts, axis, [(i, i ^ k) for i in range(count)])
        parts = jax.tree.map(jnp.add, parts, got)
        k *= 2
    return parts


def block_step(carry_state, inputs, skip_scale):
    feat_block, step_block, decay_block, write_block, read_block = inputs
    length = decay_block.shape[1]
    cumul = jnp.cumsum(decay_block, axis=1)
    row_index = lax.broadcasted_iota(jnp.int32, (length, length), 0)
    col_index = lax.broadcasted_iota(jnp.int32, (length, length), 1)
    causal = row_index >= col_index
    gaps = jnp.where(causal[None], cumul[:, :, None] - cumul[:, None, :], 0.0)
    weights = jnp.where(causal[None], jnp.exp(gaps), 0.0)
    scores = jnp.dot(read_block, jnp.transpose(write_block), precision=highest)
    scaled = feat_block * jnp.transpose(step_block)[:, :, None]
    masked = weights * scores[None]
    within = jnp.einsum("hij,jhp->ihp", masked, scaled, precision=highest)
    carried = jnp.einsum("in,hpn->ihp", read_block, carry_state, precision=highest)
    carried = carried * jnp.transpose(jnp.exp(cumul))[:, :, None]
    output = within + carried + skip_scale[None, :, None] * feat_block
    to_end = jnp.exp(cumul[:, -1:] - cumul)
    weighted_in = scaled * jnp.transpose(to_end)[:, :, None]
    update = jnp.einsum("jhp,jn->hpn", weighted_in, write_block, precision=highest)
    new_state = jnp.exp(cumul[:, -1])[:, None, None] * carry_state + update
    return (new_state, output)


def run_mixer(
    features, step_sizes, log_decay, write_keys, read_queries, carry_state, skip_scale, block
):
    length = features.shape[0]
    head_count = step_sizes.shape[0]
    head_width = features.shape[1] // head_count
    block_total = length // block
    feat_blocks = features.reshape(block_total, block, head_count, head_width)
    step_blocks = jnp.transpose(step_sizes.reshape(head_count, block_total, block), (1, 0, 2))
    decay_blocks = jnp.transpose(log_decay.reshape(head_count, block_total, block), (1, 0, 2))
    write_blocks = write_keys.reshape(block_total, block, write_keys.shape[1])
    read_blocks = read_queries.reshape(block_total, block, read_queries.shape[1])

    def advance(carried_in, inputs):
        return block_step(carried_in, inputs, skip_scale)

    last_state, outputs = lax.scan(
        advance, carry_state, (feat_blocks, step_blocks, decay_blocks, write_blocks, read_blocks)
    )
    return (last_state, outputs.reshape(length, head_count * head_width))


def prefix_sum(decay_in):
    length = decay_in.shape[1]
    upper = (
        lax.broadcasted_iota(jnp.int32, (length, length), 0)
        <= lax.broadcasted_iota(jnp.int32, (length, length), 1)
    ).astype(decay_in.dtype)
    return jnp.dot(decay_in, upper, precision=lax.Precision.HIGHEST)


def within_part(feat_in, step_in, decay_in, writes, read_in, skip_scale):
    head_count, length = step_in.shape
    head_width = feat_in.shape[1] // head_count
    cumul = prefix_sum(decay_in)
    row_index = lax.broadcasted_iota(jnp.int32, (length, length), 0)
    col_index = lax.broadcasted_iota(jnp.int32, (length, length), 1)
    causal = row_index >= col_index
    gaps = jnp.where(causal[None], cumul[:, :, None] - cumul[:, None, :], 0.0)
    weights = jnp.where(causal[None], jnp.exp(gaps), 0.0)
    scores = jnp.dot(read_in, jnp.transpose(writes), precision=highest)
    feat3 = feat_in.reshape(length, head_count, head_width)
    scaled = feat3 * jnp.transpose(step_in)[:, :, None]
    masked = weights * scores[None]
    within = jnp.einsum("hij,jhp->ihp", masked, scaled, precision=highest)
    return (within + skip_scale[None, :, None] * feat3).reshape(length, -1)


def carried_part(decay_in, read_in, state_in):
    length = decay_in.shape[1]
    cumul = prefix_sum(decay_in)
    carried = jnp.einsum("in,hpn->ihp", read_in, state_in, precision=highest)
    carried = carried * jnp.transpose(jnp.exp(cumul))[:, :, None]
    return carried.reshape(length, -1)


def state_update(feat_in, step_in, decay_in, writes):
    head_count, length = step_in.shape
    head_width = feat_in.shape[1] // head_count
    cumul = prefix_sum(decay_in)
    scaled = feat_in.reshape(length, head_count, head_width) * jnp.transpose(step_in)[:, :, None]
    to_end = jnp.exp(cumul[:, -1:] - cumul)
    weighted_in = scaled * jnp.transpose(to_end)[:, :, None]
    return jnp.einsum("jhp,jn->hpn", weighted_in, writes, precision=highest)


def end_part(feat_in, step_in, decay_in, writes, state_in):
    total = jnp.exp(prefix_sum(decay_in)[:, -1])
    return total[:, None, None] * state_in + state_update(feat_in, step_in, decay_in, writes)


def local(
    features,
    gate_pre,
    write_keys,
    read_queries,
    step_sizes,
    log_decay,
    skip_scale,
    norm_gain,
    out_grad,
):
    head_count, length = step_sizes.shape
    head_width = features.shape[1] // head_count
    channels = features.shape[1] * lax.axis_size("head")
    cumul = prefix_sum(log_decay)
    decay_total = jnp.exp(cumul[:, -1])
    scaled = (
        features.reshape(length, head_count, head_width) * jnp.transpose(step_sizes)[:, :, None]
    )
    to_end = jnp.exp(cumul[:, -1:] - cumul)
    weighted_in = scaled * jnp.transpose(to_end)[:, :, None]
    local_state = jnp.einsum("jhp,jn->hpn", weighted_in, write_keys, precision=highest)
    state_in = pair_scan(decay_total, local_state, "seq", False)
    single = length == BLOCK
    if single:
        mixed_w, pull_w = jax.vjp(
            lambda f, s, d, w, r: within_part(f, s, d, w, r, skip_scale),
            features, step_sizes, log_decay, write_keys, read_queries,
        )
        mixed_c, pull_c = jax.vjp(
            lambda d, r: carried_part(d, r, state_in), log_decay, read_queries
        )
        mixed_w = lax.optimization_barrier(mixed_w)
        mixed_out = mixed_w + mixed_c
    else:

        def local_mixer(feat_in, step_in, decay_factors, writes, read_in):
            return run_mixer(
                feat_in, step_in, decay_factors, writes, read_in, state_in, skip_scale, BLOCK
            )

        primal, pullback = jax.vjp(
            local_mixer, features, step_sizes, log_decay, write_keys, read_queries
        )
        mixed_out = primal[1]
    sigmoid_gate = jax.nn.sigmoid(gate_pre)
    active = gate_pre * sigmoid_gate
    gated_out = mixed_out * active
    weighted = out_grad * norm_gain[None, :]
    square_sum, cross_sum = butterfly_psum(
        jnp.stack([jnp.sum(gated_out * gated_out, axis=1), jnp.sum(weighted * gated_out, axis=1)]),
        "head",
    )
    inverse = lax.rsqrt(square_sum / channels + eps)
    grad_gated = (
        inverse[:, None] * weighted
        - (inverse * inverse * inverse * cross_sum / channels)[:, None] * gated_out
    )
    grad_mixed = grad_gated * active
    grad_gate = grad_gated * mixed_out * sigmoid_gate * (1.0 + gate_pre * (1.0 - sigmoid_gate))
    from_start = jnp.transpose(jnp.exp(cumul))
    weighted_grad = grad_mixed.reshape(length, head_count, head_width) * from_start[:, :, None]
    local_grad = jnp.einsum("jhp,jn->hpn", weighted_grad, read_queries, precision=highest)
    if single:
        sg_keep, sg_other, own_start, send_start, first = pair_scan(
            decay_total, local_grad, "seq", True, split=True
        )
        gf_w, gs_w, gd_w, gw_w, gr_w = pull_w(grad_mixed)
        gd_c, gr_c = pull_c(grad_mixed)
        grad_read = butterfly_psum(gr_w + gr_c, "head")
        half = sg_keep.shape[0]

        def end_half(start, grad_half):
            feat_h = lax.dynamic_slice_in_dim(features, start * head_width, half * head_width, 1)
            step_h = lax.dynamic_slice_in_dim(step_sizes, start, half, 0)
            decay_h = lax.dynamic_slice_in_dim(log_decay, start, half, 0)
            state_h = lax.dynamic_slice_in_dim(state_in, start, half, 0)
            _, pull_h = jax.vjp(
                lambda f, s, d, w: end_part(f, s, d, w, state_h),
                feat_h, step_h, decay_h, write_keys,
            )
            return pull_h(grad_half)

        own = end_half(own_start, sg_keep)
        rest = end_half(send_start, sg_other)

        def join(a, b, axis):
            return jnp.where(
                first, jnp.concatenate([b, a], axis), jnp.concatenate([a, b], axis)
            )

        gf_e = join(own[0], rest[0], 1)
        gs_e = join(own[1], rest[1], 0)
        gd_e = join(own[2], rest[2], 0)
        gw_e = own[3] + rest[3]
        grad_features = gf_w + gf_e
        grad_steps = gs_w + gs_e
        grad_decay = gd_w + gd_c + gd_e
        grad_write = butterfly_psum(gw_w + gw_e, "head")
    else:
        state_grad = pair_scan(decay_total, local_grad, "seq", True)
        grad_features, grad_steps, grad_decay, grad_write, grad_read = pullback(
            (state_grad, grad_mixed)
        )
        grad_write, grad_read = butterfly_psum((grad_write, grad_read), "head")
    return (grad_features, grad_gate, grad_write, grad_read, grad_steps, grad_decay)


def solution(mesh):
    placed = (
        P("seq", "head"),
        P("seq", "head"),
        P("seq", None),
        P("seq", None),
        P("head", "seq"),
        P("head", "seq"),
        P("head"),
        P("head"),
        P("seq", "head"),
    )
    return jax.shard_map(
        local,
        mesh=mesh,
        in_specs=placed,
        out_specs=(
            P("seq", "head"),
            P("seq", "head"),
            P("seq", None),
            P("seq", None),
            P("head", "seq"),
            P("head", "seq"),
        ),
        check_vma=False,
    )
```

```python
import jax
import jax.numpy as jnp
from jax import lax
from jax.sharding import PartitionSpec as P

BLOCK = 128


eps = 1e-05
highest = lax.Precision.HIGH


def combine(earlier, later):
    return (earlier[0] * later[0], later[0][:, None, None] * earlier[1] + later[1])


def pair_scan(decay, state, axis, reverse, split=False):
    count = lax.axis_size(axis)
    if count == 1:
        return jnp.zeros_like(state)
    assert count % 2 == 0 and decay.shape[0] % 2 == 0
    place = lax.axis_index(axis)
    virt = count - 1 - place if reverse else place

    def phys(u):
        return count - 1 - u if reverse else u

    half = decay.shape[0] // 2
    groups = count // 2
    side = virt % 2
    group = virt // 2
    first = side == 0
    own_start = (1 - side) * half
    send_start = side * half

    def part(x, start):
        return lax.dynamic_slice_in_dim(x, start, half, 0)

    a_own, s_own = part(decay, own_start), part(state, own_start)
    a_snd, s_snd = part(decay, send_start), part(state, send_start)
    swap = [(phys(u), phys(u ^ 1)) for u in range(count)]
    row = jnp.broadcast_to(a_snd[:, None, None], (half, 1, s_snd.shape[2]))
    got = lax.ppermute(jnp.concatenate([s_snd, row], 1), axis, swap)
    s_rcv, a_rcv = got[:, : s_snd.shape[1]], got[:, s_snd.shape[1], 0]
    lead = (jnp.where(first, a_own, a_rcv), jnp.where(first, s_own, s_rcv))
    trail = (jnp.where(first, a_rcv, a_own), jnp.where(first, s_rcv, s_own))
    a_tot, s_tot = combine(lead, trail)

    def shift_pairs(k):
        return [
            (phys(2 * g + x), phys(2 * (g + k) + x)) for g in range(groups - k) for x in (0, 1)
        ]

    if groups <= 4:
        a_g = jnp.ones_like(a_tot)
        s_g = jnp.zeros_like(s_tot)
        for r in range(groups - 1):
            out = combine((a_g, s_g), (a_tot, s_tot))
            pairs = [(phys(2 * r + x), phys(2 * (r + 1) + x)) for x in (0, 1)]
            if r == groups - 2:
                s_in = lax.ppermute(out[1], axis, pairs)
                a_in = a_g
            else:
                a_in, s_in = lax.ppermute(out, axis, pairs)
            dst = group == r + 1
            a_g = jnp.where(dst, a_in, a_g)
            s_g = jnp.where(dst, s_in, s_g)
    else:
        a_g, s_g = lax.ppermute((a_tot, s_tot), axis, shift_pairs(1))
        a_g = jnp.where(group == 0, 1.0, a_g)
        s_g = jnp.where(group == 0, 0.0, s_g)
        k = 1
        while k < groups:
            got = lax.ppermute((a_g, s_g), axis, shift_pairs(k))
            a_c, s_c = combine(got, (a_g, s_g))
            a_g = jnp.where(group >= k, a_c, a_g)
            s_g = jnp.where(group >= k, s_c, s_g)
            k *= 2

    with_lead_own = a_own[:, None, None] * s_g + s_own
    with_lead_rcv = a_rcv[:, None, None] * s_g + s_rcv
    send = jnp.where(first, with_lead_own, s_g)
    keep = jnp.where(first, s_g, with_lead_rcv)
    other = lax.ppermute(send, axis, swap)
    if split:
        return keep, other, own_start, send_start, first
    return jnp.where(
        first, jnp.concatenate([other, keep], 0), jnp.concatenate([keep, other], 0)
    )


def butterfly_psum(parts, axis):
    count = lax.axis_size(axis)
    if count & (count - 1):
        return lax.psum(parts, axis)
    k = 1
    while k < count:
        got = lax.ppermute(parts, axis, [(i, i ^ k) for i in range(count)])
        parts = jax.tree.map(jnp.add, parts, got)
        k *= 2
    return parts


def block_step(carry_state, inputs, skip_scale):
    feat_block, step_block, decay_block, write_block, read_block = inputs
    length = decay_block.shape[1]
    cumul = jnp.cumsum(decay_block, axis=1)
    row_index = lax.broadcasted_iota(jnp.int32, (length, length), 0)
    col_index = lax.broadcasted_iota(jnp.int32, (length, length), 1)
    causal = row_index >= col_index
    gaps = jnp.where(causal[None], cumul[:, :, None] - cumul[:, None, :], 0.0)
    weights = jnp.where(causal[None], jnp.exp(gaps), 0.0)
    scores = jnp.dot(read_block, jnp.transpose(write_block), precision=highest)
    scaled = feat_block * jnp.transpose(step_block)[:, :, None]
    masked = weights * scores[None]
    within = jnp.einsum("hij,jhp->ihp", masked, scaled, precision=highest)
    carried = jnp.einsum("in,hpn->ihp", read_block, carry_state, precision=highest)
    carried = carried * jnp.transpose(jnp.exp(cumul))[:, :, None]
    output = within + carried + skip_scale[None, :, None] * feat_block
    to_end = jnp.exp(cumul[:, -1:] - cumul)
    weighted_in = scaled * jnp.transpose(to_end)[:, :, None]
    update = jnp.einsum("jhp,jn->hpn", weighted_in, write_block, precision=highest)
    new_state = jnp.exp(cumul[:, -1])[:, None, None] * carry_state + update
    return (new_state, output)


def run_mixer(
    features, step_sizes, log_decay, write_keys, read_queries, carry_state, skip_scale, block
):
    length = features.shape[0]
    head_count = step_sizes.shape[0]
    head_width = features.shape[1] // head_count
    block_total = length // block
    feat_blocks = features.reshape(block_total, block, head_count, head_width)
    step_blocks = jnp.transpose(step_sizes.reshape(head_count, block_total, block), (1, 0, 2))
    decay_blocks = jnp.transpose(log_decay.reshape(head_count, block_total, block), (1, 0, 2))
    write_blocks = write_keys.reshape(block_total, block, write_keys.shape[1])
    read_blocks = read_queries.reshape(block_total, block, read_queries.shape[1])

    def advance(carried_in, inputs):
        return block_step(carried_in, inputs, skip_scale)

    last_state, outputs = lax.scan(
        advance, carry_state, (feat_blocks, step_blocks, decay_blocks, write_blocks, read_blocks)
    )
    return (last_state, outputs.reshape(length, head_count * head_width))


def prefix_sum(decay_in):
    length = decay_in.shape[1]
    upper = (
        lax.broadcasted_iota(jnp.int32, (length, length), 0)
        <= lax.broadcasted_iota(jnp.int32, (length, length), 1)
    ).astype(decay_in.dtype)
    return jnp.dot(decay_in, upper, precision=lax.Precision.HIGHEST)


def within_part(feat_in, step_in, decay_in, writes, read_in, skip_scale):
    head_count, length = step_in.shape
    head_width = feat_in.shape[1] // head_count
    cumul = prefix_sum(decay_in)
    row_index = lax.broadcasted_iota(jnp.int32, (length, length), 0)
    col_index = lax.broadcasted_iota(jnp.int32, (length, length), 1)
    causal = row_index >= col_index
    gaps = jnp.where(causal[None], cumul[:, :, None] - cumul[:, None, :], 0.0)
    weights = jnp.where(causal[None], jnp.exp(gaps), 0.0)
    scores = jnp.dot(read_in, jnp.transpose(writes), precision=highest)
    feat3 = feat_in.reshape(length, head_count, head_width)
    scaled = feat3 * jnp.transpose(step_in)[:, :, None]
    masked = weights * scores[None]
    within = jnp.einsum("hij,jhp->ihp", masked, scaled, precision=highest)
    return (within + skip_scale[None, :, None] * feat3).reshape(length, -1)


def carried_part(decay_in, read_in, state_in):
    length = decay_in.shape[1]
    cumul = prefix_sum(decay_in)
    carried = jnp.einsum("in,hpn->ihp", read_in, state_in, precision=highest)
    carried = carried * jnp.transpose(jnp.exp(cumul))[:, :, None]
    return carried.reshape(length, -1)


def state_update(feat_in, step_in, decay_in, writes):
    head_count, length = step_in.shape
    head_width = feat_in.shape[1] // head_count
    cumul = prefix_sum(decay_in)
    scaled = feat_in.reshape(length, head_count, head_width) * jnp.transpose(step_in)[:, :, None]
    to_end = jnp.exp(cumul[:, -1:] - cumul)
    weighted_in = scaled * jnp.transpose(to_end)[:, :, None]
    return jnp.einsum("jhp,jn->hpn", weighted_in, writes, precision=highest)


def end_part(feat_in, step_in, decay_in, writes, state_in):
    total = jnp.exp(prefix_sum(decay_in)[:, -1])
    return total[:, None, None] * state_in + state_update(feat_in, step_in, decay_in, writes)


def local(
    features,
    gate_pre,
    write_keys,
    read_queries,
    step_sizes,
    log_decay,
    skip_scale,
    norm_gain,
    out_grad,
):
    head_count, length = step_sizes.shape
    head_width = features.shape[1] // head_count
    channels = features.shape[1] * lax.axis_size("head")
    cumul = prefix_sum(log_decay)
    decay_total = jnp.exp(cumul[:, -1])
    scaled = (
        features.reshape(length, head_count, head_width) * jnp.transpose(step_sizes)[:, :, None]
    )
    to_end = jnp.exp(cumul[:, -1:] - cumul)
    weighted_in = scaled * jnp.transpose(to_end)[:, :, None]
    local_state = jnp.einsum("jhp,jn->hpn", weighted_in, write_keys, precision=highest)
    state_in = pair_scan(decay_total, local_state, "seq", False)
    single = length == BLOCK
    if single:
        mixed_w, pull_w = jax.vjp(
            lambda f, s, d, w, r: within_part(f, s, d, w, r, skip_scale),
            features, step_sizes, log_decay, write_keys, read_queries,
        )
        mixed_c, pull_c = jax.vjp(
            lambda d, r: carried_part(d, r, state_in), log_decay, read_queries
        )
        mixed_w = lax.optimization_barrier(mixed_w)
        mixed_out = mixed_w + mixed_c
    else:

        def local_mixer(feat_in, step_in, decay_factors, writes, read_in):
            return run_mixer(
                feat_in, step_in, decay_factors, writes, read_in, state_in, skip_scale, BLOCK
            )

        primal, pullback = jax.vjp(
            local_mixer, features, step_sizes, log_decay, write_keys, read_queries
        )
        mixed_out = primal[1]
    sigmoid_gate = jax.nn.sigmoid(gate_pre)
    active = gate_pre * sigmoid_gate
    gated_out = mixed_out * active
    weighted = out_grad * norm_gain[None, :]
    square_sum, cross_sum = butterfly_psum(
        jnp.stack([jnp.sum(gated_out * gated_out, axis=1), jnp.sum(weighted * gated_out, axis=1)]),
        "head",
    )
    inverse = lax.rsqrt(square_sum / channels + eps)
    grad_gated = (
        inverse[:, None] * weighted
        - (inverse * inverse * inverse * cross_sum / channels)[:, None] * gated_out
    )
    grad_mixed = grad_gated * active
    grad_gate = grad_gated * mixed_out * sigmoid_gate * (1.0 + gate_pre * (1.0 - sigmoid_gate))
    from_start = jnp.transpose(jnp.exp(cumul))
    weighted_grad = grad_mixed.reshape(length, head_count, head_width) * from_start[:, :, None]
    local_grad = jnp.einsum("jhp,jn->hpn", weighted_grad, read_queries, precision=highest)
    if single:
        sg_keep, sg_other, own_start, send_start, first = pair_scan(
            decay_total, local_grad, "seq", True, split=True
        )
        gf_w, gs_w, gd_w, gw_w, gr_w = pull_w(grad_mixed)
        gd_c, gr_c = pull_c(grad_mixed)
        grad_read = butterfly_psum(gr_w + gr_c, "head")
        half = sg_keep.shape[0]

        def end_half(start, grad_half):
            feat_h = lax.dynamic_slice_in_dim(features, start * head_width, half * head_width, 1)
            step_h = lax.dynamic_slice_in_dim(step_sizes, start, half, 0)
            decay_h = lax.dynamic_slice_in_dim(log_decay, start, half, 0)
            state_h = lax.dynamic_slice_in_dim(state_in, start, half, 0)
            _, pull_h = jax.vjp(
                lambda f, s, d, w: end_part(f, s, d, w, state_h),
                feat_h, step_h, decay_h, write_keys,
            )
            return pull_h(grad_half)

        own = end_half(own_start, sg_keep)
        rest = end_half(send_start, sg_other)

        def join(a, b, axis):
            return jnp.where(
                first, jnp.concatenate([b, a], axis), jnp.concatenate([a, b], axis)
            )

        gf_e = join(own[0], rest[0], 1)
        gs_e = join(own[1], rest[1], 0)
        gd_e = join(own[2], rest[2], 0)
        gw_e = own[3] + rest[3]
        grad_features = gf_w + gf_e
        grad_steps = gs_w + gs_e
        grad_decay = gd_w + gd_c + gd_e
        grad_write = butterfly_psum(gw_w + gw_e, "head")
    else:
        state_grad = pair_scan(decay_total, local_grad, "seq", True)
        grad_features, grad_steps, grad_decay, grad_write, grad_read = pullback(
            (state_grad, grad_mixed)
        )
        grad_write, grad_read = butterfly_psum((grad_write, grad_read), "head")
    return (grad_features, grad_gate, grad_write, grad_read, grad_steps, grad_decay)


def solution(mesh):
    placed = (
        P("seq", "head"),
        P("seq", "head"),
        P("seq", None),
        P("seq", None),
        P("head", "seq"),
        P("head", "seq"),
        P("head"),
        P("head"),
        P("seq", "head"),
    )
    return jax.shard_map(
        local,
        mesh=mesh,
        in_specs=placed,
        out_specs=(
            P("seq", "head"),
            P("seq", "head"),
            P("seq", None),
            P("seq", None),
            P("head", "seq"),
            P("head", "seq"),
        ),
        check_vma=False,
    )
```

```python
import jax
import jax.numpy as jnp
from jax import lax
from jax.sharding import PartitionSpec as P

BLOCK = 128


eps = 1e-05
highest = lax.Precision.HIGH


def combine(earlier, later):
    return (earlier[0] * later[0], later[0][:, None, None] * earlier[1] + later[1])


def pair_scan(decay, state, axis, reverse, split=False):
    count = lax.axis_size(axis)
    if count == 1:
        return jnp.zeros_like(state)
    assert count % 2 == 0 and decay.shape[0] % 2 == 0
    place = lax.axis_index(axis)
    virt = count - 1 - place if reverse else place

    def phys(u):
        return count - 1 - u if reverse else u

    half = decay.shape[0] // 2
    groups = count // 2
    side = virt % 2
    group = virt // 2
    first = side == 0
    own_start = (1 - side) * half
    send_start = side * half

    def part(x, start):
        return lax.dynamic_slice_in_dim(x, start, half, 0)

    a_own, s_own = part(decay, own_start), part(state, own_start)
    a_snd, s_snd = part(decay, send_start), part(state, send_start)
    swap = [(phys(u), phys(u ^ 1)) for u in range(count)]
    a_rcv, s_rcv = lax.ppermute((a_snd, s_snd), axis, swap)
    lead = (jnp.where(first, a_own, a_rcv), jnp.where(first, s_own, s_rcv))
    trail = (jnp.where(first, a_rcv, a_own), jnp.where(first, s_rcv, s_own))
    a_tot, s_tot = combine(lead, trail)

    def shift_pairs(k):
        return [
            (phys(2 * g + x), phys(2 * (g + k) + x)) for g in range(groups - k) for x in (0, 1)
        ]

    if groups <= 4:
        a_g = jnp.ones_like(a_tot)
        s_g = jnp.zeros_like(s_tot)
        for r in range(groups - 1):
            out = combine((a_g, s_g), (a_tot, s_tot))
            pairs = [(phys(2 * r + x), phys(2 * (r + 1) + x)) for x in (0, 1)]
            if r == groups - 2:
                s_in = lax.ppermute(out[1], axis, pairs)
                a_in = a_g
            else:
                a_in, s_in = lax.ppermute(out, axis, pairs)
            dst = group == r + 1
            a_g = jnp.where(dst, a_in, a_g)
            s_g = jnp.where(dst, s_in, s_g)
    else:
        a_g, s_g = lax.ppermute((a_tot, s_tot), axis, shift_pairs(1))
        a_g = jnp.where(group == 0, 1.0, a_g)
        s_g = jnp.where(group == 0, 0.0, s_g)
        k = 1
        while k < groups:
            got = lax.ppermute((a_g, s_g), axis, shift_pairs(k))
            a_c, s_c = combine(got, (a_g, s_g))
            a_g = jnp.where(group >= k, a_c, a_g)
            s_g = jnp.where(group >= k, s_c, s_g)
            k *= 2

    with_lead_own = a_own[:, None, None] * s_g + s_own
    with_lead_rcv = a_rcv[:, None, None] * s_g + s_rcv
    send = jnp.where(first, with_lead_own, s_g)
    keep = jnp.where(first, s_g, with_lead_rcv)
    other = lax.ppermute(send, axis, swap)
    if split:
        return keep, other, own_start, send_start, first
    return jnp.where(
        first, jnp.concatenate([other, keep], 0), jnp.concatenate([keep, other], 0)
    )


def butterfly_psum(parts, axis):
    count = lax.axis_size(axis)
    if count & (count - 1):
        return lax.psum(parts, axis)
    k = 1
    while k < count:
        got = lax.ppermute(parts, axis, [(i, i ^ k) for i in range(count)])
        parts = jax.tree.map(jnp.add, parts, got)
        k *= 2
    return parts


def block_step(carry_state, inputs, skip_scale):
    feat_block, step_block, decay_block, write_block, read_block = inputs
    length = decay_block.shape[1]
    cumul = jnp.cumsum(decay_block, axis=1)
    row_index = lax.broadcasted_iota(jnp.int32, (length, length), 0)
    col_index = lax.broadcasted_iota(jnp.int32, (length, length), 1)
    causal = row_index >= col_index
    gaps = jnp.where(causal[None], cumul[:, :, None] - cumul[:, None, :], 0.0)
    weights = jnp.where(causal[None], jnp.exp(gaps), 0.0)
    scores = jnp.dot(read_block, jnp.transpose(write_block), precision=highest)
    scaled = feat_block * jnp.transpose(step_block)[:, :, None]
    masked = weights * scores[None]
    within = jnp.einsum("hij,jhp->ihp", masked, scaled, precision=highest)
    carried = jnp.einsum("in,hpn->ihp", read_block, carry_state, precision=highest)
    carried = carried * jnp.transpose(jnp.exp(cumul))[:, :, None]
    output = within + carried + skip_scale[None, :, None] * feat_block
    to_end = jnp.exp(cumul[:, -1:] - cumul)
    weighted_in = scaled * jnp.transpose(to_end)[:, :, None]
    update = jnp.einsum("jhp,jn->hpn", weighted_in, write_block, precision=highest)
    new_state = jnp.exp(cumul[:, -1])[:, None, None] * carry_state + update
    return (new_state, output)


def run_mixer(
    features, step_sizes, log_decay, write_keys, read_queries, carry_state, skip_scale, block
):
    length = features.shape[0]
    head_count = step_sizes.shape[0]
    head_width = features.shape[1] // head_count
    block_total = length // block
    feat_blocks = features.reshape(block_total, block, head_count, head_width)
    step_blocks = jnp.transpose(step_sizes.reshape(head_count, block_total, block), (1, 0, 2))
    decay_blocks = jnp.transpose(log_decay.reshape(head_count, block_total, block), (1, 0, 2))
    write_blocks = write_keys.reshape(block_total, block, write_keys.shape[1])
    read_blocks = read_queries.reshape(block_total, block, read_queries.shape[1])

    def advance(carried_in, inputs):
        return block_step(carried_in, inputs, skip_scale)

    last_state, outputs = lax.scan(
        advance, carry_state, (feat_blocks, step_blocks, decay_blocks, write_blocks, read_blocks)
    )
    return (last_state, outputs.reshape(length, head_count * head_width))


def prefix_sum(decay_in):
    length = decay_in.shape[1]
    upper = (
        lax.broadcasted_iota(jnp.int32, (length, length), 0)
        <= lax.broadcasted_iota(jnp.int32, (length, length), 1)
    ).astype(decay_in.dtype)
    return jnp.dot(decay_in, upper, precision=lax.Precision.HIGHEST)


def within_part(feat_in, step_in, decay_in, writes, read_in, skip_scale):
    head_count, length = step_in.shape
    head_width = feat_in.shape[1] // head_count
    cumul = prefix_sum(decay_in)
    row_index = lax.broadcasted_iota(jnp.int32, (length, length), 0)
    col_index = lax.broadcasted_iota(jnp.int32, (length, length), 1)
    causal = row_index >= col_index
    gaps = jnp.where(causal[None], cumul[:, :, None] - cumul[:, None, :], 0.0)
    weights = jnp.where(causal[None], jnp.exp(gaps), 0.0)
    scores = jnp.dot(read_in, jnp.transpose(writes), precision=highest)
    feat3 = feat_in.reshape(length, head_count, head_width)
    scaled = feat3 * jnp.transpose(step_in)[:, :, None]
    masked = weights * scores[None]
    within = jnp.einsum("hij,jhp->ihp", masked, scaled, precision=highest)
    return (within + skip_scale[None, :, None] * feat3).reshape(length, -1)


def carried_part(decay_in, read_in, state_in):
    length = decay_in.shape[1]
    cumul = prefix_sum(decay_in)
    carried = jnp.einsum("in,hpn->ihp", read_in, state_in, precision=highest)
    carried = carried * jnp.transpose(jnp.exp(cumul))[:, :, None]
    return carried.reshape(length, -1)


def state_update(feat_in, step_in, decay_in, writes):
    head_count, length = step_in.shape
    head_width = feat_in.shape[1] // head_count
    cumul = prefix_sum(decay_in)
    scaled = feat_in.reshape(length, head_count, head_width) * jnp.transpose(step_in)[:, :, None]
    to_end = jnp.exp(cumul[:, -1:] - cumul)
    weighted_in = scaled * jnp.transpose(to_end)[:, :, None]
    return jnp.einsum("jhp,jn->hpn", weighted_in, writes, precision=highest)


def end_part(feat_in, step_in, decay_in, writes, state_in):
    total = jnp.exp(prefix_sum(decay_in)[:, -1])
    return total[:, None, None] * state_in + state_update(feat_in, step_in, decay_in, writes)


def local(
    features,
    gate_pre,
    write_keys,
    read_queries,
    step_sizes,
    log_decay,
    skip_scale,
    norm_gain,
    out_grad,
):
    head_count, length = step_sizes.shape
    head_width = features.shape[1] // head_count
    channels = features.shape[1] * lax.axis_size("head")
    cumul = prefix_sum(log_decay)
    decay_total = jnp.exp(cumul[:, -1])
    scaled = (
        features.reshape(length, head_count, head_width) * jnp.transpose(step_sizes)[:, :, None]
    )
    to_end = jnp.exp(cumul[:, -1:] - cumul)
    weighted_in = scaled * jnp.transpose(to_end)[:, :, None]
    local_state = jnp.einsum("jhp,jn->hpn", weighted_in, write_keys, precision=highest)
    state_in = pair_scan(decay_total, local_state, "seq", False)
    single = length == BLOCK
    if single:
        mixed_w, pull_w = jax.vjp(
            lambda f, s, d, w, r: within_part(f, s, d, w, r, skip_scale),
            features, step_sizes, log_decay, write_keys, read_queries,
        )
        mixed_c, pull_c = jax.vjp(
            lambda d, r: carried_part(d, r, state_in), log_decay, read_queries
        )
        mixed_w = lax.optimization_barrier(mixed_w)
        mixed_out = mixed_w + mixed_c
    else:

        def local_mixer(feat_in, step_in, decay_factors, writes, read_in):
            return run_mixer(
                feat_in, step_in, decay_factors, writes, read_in, state_in, skip_scale, BLOCK
            )

        primal, pullback = jax.vjp(
            local_mixer, features, step_sizes, log_decay, write_keys, read_queries
        )
        mixed_out = primal[1]
    sigmoid_gate = jax.nn.sigmoid(gate_pre)
    active = gate_pre * sigmoid_gate
    gated_out = mixed_out * active
    weighted = out_grad * norm_gain[None, :]
    square_sum, cross_sum = butterfly_psum(
        jnp.stack([jnp.sum(gated_out * gated_out, axis=1), jnp.sum(weighted * gated_out, axis=1)]),
        "head",
    )
    inverse = lax.rsqrt(square_sum / channels + eps)
    grad_gated = (
        inverse[:, None] * weighted
        - (inverse * inverse * inverse * cross_sum / channels)[:, None] * gated_out
    )
    grad_mixed = grad_gated * active
    grad_gate = grad_gated * mixed_out * sigmoid_gate * (1.0 + gate_pre * (1.0 - sigmoid_gate))
    from_start = jnp.transpose(jnp.exp(cumul))
    weighted_grad = grad_mixed.reshape(length, head_count, head_width) * from_start[:, :, None]
    local_grad = jnp.einsum("jhp,jn->hpn", weighted_grad, read_queries, precision=highest)
    if single:
        sg_keep, sg_other, own_start, send_start, first = pair_scan(
            decay_total, local_grad, "seq", True, split=True
        )
        gf_w, gs_w, gd_w, gw_w, gr_w = pull_w(grad_mixed)
        gd_c, gr_c = pull_c(grad_mixed)
        grad_read = butterfly_psum(gr_w + gr_c, "head")
        half = sg_keep.shape[0]

        def end_half(start, grad_half):
            feat_h = lax.dynamic_slice_in_dim(features, start * head_width, half * head_width, 1)
            step_h = lax.dynamic_slice_in_dim(step_sizes, start, half, 0)
            decay_h = lax.dynamic_slice_in_dim(log_decay, start, half, 0)
            state_h = lax.dynamic_slice_in_dim(state_in, start, half, 0)
            _, pull_h = jax.vjp(
                lambda f, s, d, w: end_part(f, s, d, w, state_h),
                feat_h, step_h, decay_h, write_keys,
            )
            return pull_h(grad_half)

        own = end_half(own_start, sg_keep)
        rest = end_half(send_start, sg_other)

        def add_at(total, piece, start, axis):
            cur = lax.dynamic_slice_in_dim(total, start, piece.shape[axis], axis)
            return lax.dynamic_update_slice_in_dim(total, cur + piece, start, axis)

        gw_e = own[3] + rest[3]
        grad_features = add_at(add_at(gf_w, own[0], own_start * head_width, 1), rest[0],
                               send_start * head_width, 1)
        grad_steps = add_at(add_at(gs_w, own[1], own_start, 0), rest[1], send_start, 0)
        grad_decay = add_at(add_at(gd_w + gd_c, own[2], own_start, 0), rest[2], send_start, 0)
        grad_write = butterfly_psum(gw_w + gw_e, "head")
    else:
        state_grad = pair_scan(decay_total, local_grad, "seq", True)
        grad_features, grad_steps, grad_decay, grad_write, grad_read = pullback(
            (state_grad, grad_mixed)
        )
        grad_write, grad_read = butterfly_psum((grad_write, grad_read), "head")
    return (grad_features, grad_gate, grad_write, grad_read, grad_steps, grad_decay)


def solution(mesh):
    placed = (
        P("seq", "head"),
        P("seq", "head"),
        P("seq", None),
        P("seq", None),
        P("head", "seq"),
        P("head", "seq"),
        P("head"),
        P("head"),
        P("seq", "head"),
    )
    return jax.shard_map(
        local,
        mesh=mesh,
        in_specs=placed,
        out_specs=(
            P("seq", "head"),
            P("seq", "head"),
            P("seq", None),
            P("seq", None),
            P("head", "seq"),
            P("head", "seq"),
        ),
        check_vma=False,
    )
```

```python
import jax
import jax.numpy as jnp
from jax import lax
from jax.sharding import PartitionSpec as P

BLOCK = 128


eps = 1e-05
highest = lax.Precision.HIGH


def combine(earlier, later):
    return (earlier[0] * later[0], later[0][:, None, None] * earlier[1] + later[1])


def pair_scan(decay, state, axis, reverse, split=False):
    count = lax.axis_size(axis)
    if count == 1:
        return jnp.zeros_like(state)
    assert count % 2 == 0 and decay.shape[0] % 2 == 0
    place = lax.axis_index(axis)
    virt = count - 1 - place if reverse else place

    def phys(u):
        return count - 1 - u if reverse else u

    half = decay.shape[0] // 2
    groups = count // 2
    side = virt % 2
    group = virt // 2
    first = side == 0
    own_start = (1 - side) * half
    send_start = side * half

    def part(x, start):
        return lax.dynamic_slice_in_dim(x, start, half, 0)

    a_own, s_own = part(decay, own_start), part(state, own_start)
    a_snd, s_snd = part(decay, send_start), part(state, send_start)
    swap = [(phys(u), phys(u ^ 1)) for u in range(count)]
    a_rcv, s_rcv = lax.ppermute((a_snd, s_snd), axis, swap)
    lead = (jnp.where(first, a_own, a_rcv), jnp.where(first, s_own, s_rcv))
    trail = (jnp.where(first, a_rcv, a_own), jnp.where(first, s_rcv, s_own))
    a_tot, s_tot = combine(lead, trail)

    def shift_pairs(k):
        return [
            (phys(2 * g + x), phys(2 * (g + k) + x)) for g in range(groups - k) for x in (0, 1)
        ]

    if groups <= 4:
        a_g = jnp.ones_like(a_tot)
        s_g = jnp.zeros_like(s_tot)
        for r in range(groups - 1):
            out = combine((a_g, s_g), (a_tot, s_tot))
            pairs = [(phys(2 * r + x), phys(2 * (r + 1) + x)) for x in (0, 1)]
            if r == groups - 2:
                s_in = lax.ppermute(out[1], axis, pairs)
                a_in = a_g
            else:
                a_in, s_in = lax.ppermute(out, axis, pairs)
            dst = group == r + 1
            a_g = jnp.where(dst, a_in, a_g)
            s_g = jnp.where(dst, s_in, s_g)
    else:
        a_g, s_g = lax.ppermute((a_tot, s_tot), axis, shift_pairs(1))
        a_g = jnp.where(group == 0, 1.0, a_g)
        s_g = jnp.where(group == 0, 0.0, s_g)
        k = 1
        while k < groups:
            got = lax.ppermute((a_g, s_g), axis, shift_pairs(k))
            a_c, s_c = combine(got, (a_g, s_g))
            a_g = jnp.where(group >= k, a_c, a_g)
            s_g = jnp.where(group >= k, s_c, s_g)
            k *= 2

    with_lead_own = a_own[:, None, None] * s_g + s_own
    with_lead_rcv = a_rcv[:, None, None] * s_g + s_rcv
    send = jnp.where(first, with_lead_own, s_g)
    keep = jnp.where(first, s_g, with_lead_rcv)
    other = lax.ppermute(send, axis, swap)
    if split:
        return keep, other, own_start, send_start, first
    return jnp.where(
        first, jnp.concatenate([other, keep], 0), jnp.concatenate([keep, other], 0)
    )


def butterfly_psum(parts, axis):
    count = lax.axis_size(axis)
    if count & (count - 1):
        return lax.psum(parts, axis)
    k = count // 2
    while k >= 1:
        got = lax.ppermute(parts, axis, [(i, i ^ k) for i in range(count)])
        parts = jax.tree.map(jnp.add, parts, got)
        k //= 2
    return parts


def block_step(carry_state, inputs, skip_scale):
    feat_block, step_block, decay_block, write_block, read_block = inputs
    length = decay_block.shape[1]
    cumul = jnp.cumsum(decay_block, axis=1)
    row_index = lax.broadcasted_iota(jnp.int32, (length, length), 0)
    col_index = lax.broadcasted_iota(jnp.int32, (length, length), 1)
    causal = row_index >= col_index
    gaps = jnp.where(causal[None], cumul[:, :, None] - cumul[:, None, :], 0.0)
    weights = jnp.where(causal[None], jnp.exp(gaps), 0.0)
    scores = jnp.dot(read_block, jnp.transpose(write_block), precision=highest)
    scaled = feat_block * jnp.transpose(step_block)[:, :, None]
    masked = weights * scores[None]
    within = jnp.einsum("hij,jhp->ihp", masked, scaled, precision=highest)
    carried = jnp.einsum("in,hpn->ihp", read_block, carry_state, precision=highest)
    carried = carried * jnp.transpose(jnp.exp(cumul))[:, :, None]
    output = within + carried + skip_scale[None, :, None] * feat_block
    to_end = jnp.exp(cumul[:, -1:] - cumul)
    weighted_in = scaled * jnp.transpose(to_end)[:, :, None]
    update = jnp.einsum("jhp,jn->hpn", weighted_in, write_block, precision=highest)
    new_state = jnp.exp(cumul[:, -1])[:, None, None] * carry_state + update
    return (new_state, output)


def run_mixer(
    features, step_sizes, log_decay, write_keys, read_queries, carry_state, skip_scale, block
):
    length = features.shape[0]
    head_count = step_sizes.shape[0]
    head_width = features.shape[1] // head_count
    block_total = length // block
    feat_blocks = features.reshape(block_total, block, head_count, head_width)
    step_blocks = jnp.transpose(step_sizes.reshape(head_count, block_total, block), (1, 0, 2))
    decay_blocks = jnp.transpose(log_decay.reshape(head_count, block_total, block), (1, 0, 2))
    write_blocks = write_keys.reshape(block_total, block, write_keys.shape[1])
    read_blocks = read_queries.reshape(block_total, block, read_queries.shape[1])

    def advance(carried_in, inputs):
        return block_step(carried_in, inputs, skip_scale)

    last_state, outputs = lax.scan(
        advance, carry_state, (feat_blocks, step_blocks, decay_blocks, write_blocks, read_blocks)
    )
    return (last_state, outputs.reshape(length, head_count * head_width))


def prefix_sum(decay_in):
    length = decay_in.shape[1]
    upper = (
        lax.broadcasted_iota(jnp.int32, (length, length), 0)
        <= lax.broadcasted_iota(jnp.int32, (length, length), 1)
    ).astype(decay_in.dtype)
    return jnp.dot(decay_in, upper, precision=lax.Precision.HIGHEST)


def within_part(feat_in, step_in, decay_in, writes, read_in, skip_scale):
    head_count, length = step_in.shape
    head_width = feat_in.shape[1] // head_count
    cumul = prefix_sum(decay_in)
    row_index = lax.broadcasted_iota(jnp.int32, (length, length), 0)
    col_index = lax.broadcasted_iota(jnp.int32, (length, length), 1)
    causal = row_index >= col_index
    gaps = jnp.where(causal[None], cumul[:, :, None] - cumul[:, None, :], 0.0)
    weights = jnp.where(causal[None], jnp.exp(gaps), 0.0)
    scores = jnp.dot(read_in, jnp.transpose(writes), precision=highest)
    feat3 = feat_in.reshape(length, head_count, head_width)
    scaled = feat3 * jnp.transpose(step_in)[:, :, None]
    masked = weights * scores[None]
    within = jnp.einsum("hij,jhp->ihp", masked, scaled, precision=highest)
    return (within + skip_scale[None, :, None] * feat3).reshape(length, -1)


def carried_part(decay_in, read_in, state_in):
    length = decay_in.shape[1]
    cumul = prefix_sum(decay_in)
    carried = jnp.einsum("in,hpn->ihp", read_in, state_in, precision=highest)
    carried = carried * jnp.transpose(jnp.exp(cumul))[:, :, None]
    return carried.reshape(length, -1)


def state_update(feat_in, step_in, decay_in, writes):
    head_count, length = step_in.shape
    head_width = feat_in.shape[1] // head_count
    cumul = prefix_sum(decay_in)
    scaled = feat_in.reshape(length, head_count, head_width) * jnp.transpose(step_in)[:, :, None]
    to_end = jnp.exp(cumul[:, -1:] - cumul)
    weighted_in = scaled * jnp.transpose(to_end)[:, :, None]
    return jnp.einsum("jhp,jn->hpn", weighted_in, writes, precision=highest)


def end_part(feat_in, step_in, decay_in, writes, state_in):
    total = jnp.exp(prefix_sum(decay_in)[:, -1])
    return total[:, None, None] * state_in + state_update(feat_in, step_in, decay_in, writes)


def local(
    features,
    gate_pre,
    write_keys,
    read_queries,
    step_sizes,
    log_decay,
    skip_scale,
    norm_gain,
    out_grad,
):
    head_count, length = step_sizes.shape
    head_width = features.shape[1] // head_count
    channels = features.shape[1] * lax.axis_size("head")
    cumul = prefix_sum(log_decay)
    decay_total = jnp.exp(cumul[:, -1])
    scaled = (
        features.reshape(length, head_count, head_width) * jnp.transpose(step_sizes)[:, :, None]
    )
    to_end = jnp.exp(cumul[:, -1:] - cumul)
    weighted_in = scaled * jnp.transpose(to_end)[:, :, None]
    local_state = jnp.einsum("jhp,jn->hpn", weighted_in, write_keys, precision=highest)
    state_in = pair_scan(decay_total, local_state, "seq", False)
    single = length == BLOCK
    if single:
        mixed_w, pull_w = jax.vjp(
            lambda f, s, d, w, r: within_part(f, s, d, w, r, skip_scale),
            features, step_sizes, log_decay, write_keys, read_queries,
        )
        mixed_c, pull_c = jax.vjp(
            lambda d, r: carried_part(d, r, state_in), log_decay, read_queries
        )
        mixed_w = lax.optimization_barrier(mixed_w)
        mixed_out = mixed_w + mixed_c
    else:

        def local_mixer(feat_in, step_in, decay_factors, writes, read_in):
            return run_mixer(
                feat_in, step_in, decay_factors, writes, read_in, state_in, skip_scale, BLOCK
            )

        primal, pullback = jax.vjp(
            local_mixer, features, step_sizes, log_decay, write_keys, read_queries
        )
        mixed_out = primal[1]
    sigmoid_gate = jax.nn.sigmoid(gate_pre)
    active = gate_pre * sigmoid_gate
    gated_out = mixed_out * active
    weighted = out_grad * norm_gain[None, :]
    square_sum, cross_sum = butterfly_psum(
        jnp.stack([jnp.sum(gated_out * gated_out, axis=1), jnp.sum(weighted * gated_out, axis=1)]),
        "head",
    )
    inverse = lax.rsqrt(square_sum / channels + eps)
    grad_gated = (
        inverse[:, None] * weighted
        - (inverse * inverse * inverse * cross_sum / channels)[:, None] * gated_out
    )
    grad_mixed = grad_gated * active
    grad_gate = grad_gated * mixed_out * sigmoid_gate * (1.0 + gate_pre * (1.0 - sigmoid_gate))
    from_start = jnp.transpose(jnp.exp(cumul))
    weighted_grad = grad_mixed.reshape(length, head_count, head_width) * from_start[:, :, None]
    local_grad = jnp.einsum("jhp,jn->hpn", weighted_grad, read_queries, precision=highest)
    if single:
        sg_keep, sg_other, own_start, send_start, first = pair_scan(
            decay_total, local_grad, "seq", True, split=True
        )
        gf_w, gs_w, gd_w, gw_w, gr_w = pull_w(grad_mixed)
        gd_c, gr_c = pull_c(grad_mixed)
        grad_read = butterfly_psum(gr_w + gr_c, "head")
        half = sg_keep.shape[0]

        def end_half(start, grad_half):
            feat_h = lax.dynamic_slice_in_dim(features, start * head_width, half * head_width, 1)
            step_h = lax.dynamic_slice_in_dim(step_sizes, start, half, 0)
            decay_h = lax.dynamic_slice_in_dim(log_decay, start, half, 0)
            state_h = lax.dynamic_slice_in_dim(state_in, start, half, 0)
            _, pull_h = jax.vjp(
                lambda f, s, d, w: end_part(f, s, d, w, state_h),
                feat_h, step_h, decay_h, write_keys,
            )
            return pull_h(grad_half)

        own = end_half(own_start, sg_keep)
        rest = end_half(send_start, sg_other)

        def join(a, b, axis):
            return jnp.where(
                first, jnp.concatenate([b, a], axis), jnp.concatenate([a, b], axis)
            )

        gf_e = join(own[0], rest[0], 1)
        gs_e = join(own[1], rest[1], 0)
        gd_e = join(own[2], rest[2], 0)
        gw_e = own[3] + rest[3]
        grad_features = gf_w + gf_e
        grad_steps = gs_w + gs_e
        grad_decay = gd_w + gd_c + gd_e
        grad_write = butterfly_psum(gw_w + gw_e, "head")
    else:
        state_grad = pair_scan(decay_total, local_grad, "seq", True)
        grad_features, grad_steps, grad_decay, grad_write, grad_read = pullback(
            (state_grad, grad_mixed)
        )
        grad_write, grad_read = butterfly_psum((grad_write, grad_read), "head")
    return (grad_features, grad_gate, grad_write, grad_read, grad_steps, grad_decay)


def solution(mesh):
    placed = (
        P("seq", "head"),
        P("seq", "head"),
        P("seq", None),
        P("seq", None),
        P("head", "seq"),
        P("head", "seq"),
        P("head"),
        P("head"),
        P("seq", "head"),
    )
    return jax.shard_map(
        local,
        mesh=mesh,
        in_specs=placed,
        out_specs=(
            P("seq", "head"),
            P("seq", "head"),
            P("seq", None),
            P("seq", None),
            P("head", "seq"),
            P("head", "seq"),
        ),
        check_vma=False,
    )
```
